32 devices in a mesh: row: 8 (over z, x), col: 4 (over y, core).
Axes of the slice: x: 2, y: 2, z: 4, core: 2. Of those that a mesh axis runs over, the one named last changes fastest.
Arguments:
- low_rhs: bfloat16 [32, 512, 128], P(('row', 'col')), may hold values from -6 to 6
- low_inv: bfloat16 [32, 512, 512], P(('row', 'col'))
- low_tiles: bfloat16 [32, 4, 512, 512], P(('row', 'col')), may hold values from -0.03125 to 0.03125
- tile_rows: int32 [32, 4], P(('row', 'col')), may hold values from -1 to 3, as said below
- tile_cols: int32 [32, 4], P(('row', 'col')), may hold values from 0 to 31, as said below
- top_rhs: bfloat16 [4, 512, 128], P(None, 'row'), may hold values from -6 to 6
- top_inv: bfloat16 [4, 512, 512], P(None, 'row')
- top_tiles: bfloat16 [6, 512, 512], P(None, 'row'), may hold values from -0.125 to 0.125
Outputs:
- low_solution: float32 [32, 512, 128], P(('row', 'col'))
- top_solution: float32 [4, 512, 128], P(None, 'row')
The draws below stay inside these ranges and needn't reach their ends.
Inputs may be any that keep to these rules, and one draw needn't show every extreme that they name: `tile_rows`: in each block's list of 4 slots the used slots come first and name top-level blocks; the remaining slots hold -1. Some list has only its first slot used and some list is full. Slot s of block j names a block of j's aligned group of 4 blocks (j // 4 == tile_cols[j, s] // 4); an empty slot names j itself.
All inputs are finite; a program needn't handle non-finite values.
Results may differ from the reference program's by a relative error of at most 0.022.
Values may be sent and summed in bfloat16 or wider, within the bound.
No kernel may reach another device: no remote copies, remote signals or barrier semaphores. Data moves between devices by JAX's collectives and lax.ppermute only.
A program may use at most 64 MiB of HBM per device.

```python
import jax
import jax.numpy as jnp
from jax import lax

BS = 512
SRC = 128
TOP = 4
SLOTS = 4
PEERS = 4
LOW = 32
NPAIR = 6


def slot_lists(key):
    base = jax.random.fold_in(key, 11)
    first, second, third, fourth = jax.random.split(base, 4)
    live = jnp.minimum(jax.random.randint(first, (LOW,), 1, SLOTS + 1), jax.random.randint(second, (LOW,), 1, SLOTS + 1))
    live = live.at[0].set(1).at[LOW - 1].set(SLOTS)
    slot_index = jnp.arange(SLOTS, dtype=jnp.int32)[None, :]
    alive = slot_index < live[:, None]
    slot_rows = jnp.where(alive, jax.random.randint(third, (LOW, SLOTS), 0, TOP), -1)
    slot_rows = slot_rows.at[0, 0].set(TOP - 1)
    device = jnp.arange(LOW, dtype=jnp.int32)[:, None]
    group = device // PEERS * PEERS
    slot_cols = jnp.where(alive, group + jax.random.randint(fourth, (LOW, SLOTS), 0, PEERS), device)
    slot_cols = slot_cols.at[LOW - 1, 0].set(LOW - 1)
    return (slot_rows.astype(jnp.int32), slot_cols.astype(jnp.int32))


def draw_tile_rows(key, part):
    return slot_lists(key)[0]


def draw_tile_cols(key, part):
    return slot_lists(key)[1]


def draw_low_inv(key, part):
    first, second = jax.random.split(jax.random.fold_in(key, 23))
    noise = jax.random.normal(first, (LOW, BS, BS), jnp.float32)
    diagonal = jax.random.uniform(second, (LOW, BS), jnp.float32, 0.5, 1.5)
    lower = (jnp.arange(BS)[:, None] > jnp.arange(BS)[None, :]).astype(jnp.float32)
    matrix = noise * (0.5 / BS ** 0.5) * lower[None] + diagonal[:, :, None] * jnp.eye(BS, dtype=jnp.float32)[None]
    return matrix.astype(jnp.bfloat16)


def draw_top_inv(key, part):
    first, second = jax.random.split(jax.random.fold_in(key, 37))
    noise = jax.random.normal(first, (TOP, BS, BS), jnp.float32)
    diagonal = jax.random.uniform(second, (TOP, BS), jnp.float32, 0.5, 1.5)
    lower = (jnp.arange(BS)[:, None] > jnp.arange(BS)[None, :]).astype(jnp.float32)
    matrix = noise * (0.5 / BS ** 0.5) * lower[None] + diagonal[:, :, None] * jnp.eye(BS, dtype=jnp.float32)[None]
    return matrix.astype(jnp.bfloat16)


def level_of(own_key, shape, cuts, least, top_value):
    def one(dim, blocks):
        draws = jax.random.uniform(jax.random.fold_in(jax.random.fold_in(own_key, 6), dim), (blocks,), jnp.float32, least / len(cuts), top_value / len(cuts))
        return jnp.repeat(jnp.exp(draws), shape[dim] // blocks).reshape((-1,) + (1,) * (len(shape) - dim - 1))

    factor_of = one(*cuts[0])
    for cut in cuts[1:]:
        factor_of = factor_of * one(*cut)
    return factor_of


def bell_draw(stream_key, shape, deviation, limit, cuts=(), held_as=jnp.bfloat16):
    gain = level_of(stream_key, shape, cuts, -0.22, 0.18) if cuts else 1.0
    array = jax.random.normal(stream_key, shape, jnp.float32) * deviation * gain
    return jnp.minimum(jnp.maximum(array, -limit), limit).astype(held_as)


def setup_inputs(seed: int = 0) -> dict:
    keys = jax.random.split(jax.random.key(seed), 9)
    return {
        "low_rhs": bell_draw(keys[0], (LOW, BS, SRC), 1.0, 6.0, ((0, 32),)),
        "low_inv": draw_low_inv(jax.random.fold_in(keys[8], 71), 0),
        "low_tiles": bell_draw(keys[2], (LOW, SLOTS, BS, BS), (BS * 64) ** -0.5, 0.03125, ((0, 32),)),
        "tile_rows": draw_tile_rows(jax.random.fold_in(keys[8], 71), 0),
        "tile_cols": draw_tile_cols(jax.random.fold_in(keys[8], 71), 0),
        "top_rhs": bell_draw(keys[5], (TOP, BS, SRC), 1.0, 6.0, ((1, 8),)),
        "top_inv": draw_top_inv(jax.random.fold_in(keys[8], 71), 0),
        "top_tiles": bell_draw(keys[7], (NPAIR, BS, BS), (BS * TOP) ** -0.5, 0.125, ((1, 8),)),
    }


def reference(low_rhs, low_inv, low_tiles, tile_rows, tile_cols, top_rhs, top_inv, top_tiles):
    low_forward = jnp.einsum("jab,jbk->jak", low_inv.astype(jnp.float32), low_rhs.astype(jnp.float32)).astype(jnp.bfloat16)
    level_iota = jnp.arange(TOP, dtype=jnp.int32)

    def forward_device(running, item):
        tile_set, slot_rows, slot_cols = item
        picked = low_forward[slot_cols].astype(jnp.float32)
        products = jnp.einsum("sab,sbk->sak", tile_set.astype(jnp.float32), picked)
        pick_level = (slot_rows[:, None] == level_iota[None, :]).astype(jnp.float32)
        return running + jnp.einsum("st,sak->tak", pick_level, products, precision=lax.Precision.HIGHEST), None

    coupling, _ = lax.scan(forward_device, jnp.zeros((TOP, BS, SRC), jnp.float32), (low_tiles, tile_rows, tile_cols))
    top_forward = []
    for t in range(TOP):
        residue = top_rhs[t].astype(jnp.float32) - coupling[t]
        for u in range(t):
            residue = residue - jnp.dot(top_tiles[t * (t - 1) // 2 + u], top_forward[u], preferred_element_type=jnp.float32)
        top_forward.append(jnp.dot(top_inv[t], residue.astype(jnp.bfloat16), preferred_element_type=jnp.float32).astype(jnp.bfloat16))
    top_back = [None] * TOP
    top_out = [None] * TOP
    for t in reversed(range(TOP)):
        update = top_forward[t].astype(jnp.float32)
        for k in range(t + 1, TOP):
            update = update - jnp.dot(top_tiles[k * (k - 1) // 2 + t].T, top_back[k], preferred_element_type=jnp.float32)
        solution = jnp.dot(top_inv[t].T, update.astype(jnp.bfloat16), preferred_element_type=jnp.float32)
        top_out[t] = solution
        top_back[t] = solution.astype(jnp.bfloat16)
    back_stack = jnp.stack(top_back)
    peer_iota = jnp.arange(PEERS, dtype=jnp.int32)

    def backward_device(running, item):
        tile_set, slot_rows, slot_cols, device = item
        alive = slot_rows >= 0
        picked = back_stack[jnp.maximum(slot_rows, 0)].astype(jnp.float32)
        products = jnp.einsum("sab,sak->sbk", tile_set.astype(jnp.float32), picked)
        pick_peer = (((slot_cols % PEERS)[:, None] == peer_iota[None, :]) & alive[:, None]).astype(jnp.float32)
        terms = jnp.einsum("sp,sbk->pbk", pick_peer, products, precision=lax.Precision.HIGHEST)
        rounded = lax.optimization_barrier(terms.astype(jnp.bfloat16)).astype(jnp.float32)
        start = ((device // PEERS) * PEERS).astype(jnp.int32)
        current = lax.dynamic_slice_in_dim(running, start, PEERS, 0)
        return lax.dynamic_update_slice_in_dim(running, current + rounded, start, 0), None

    devices = jnp.arange(LOW, dtype=jnp.int32)
    back_term, _ = lax.scan(backward_device, jnp.zeros((LOW, BS, SRC), jnp.float32), (low_tiles, tile_rows, tile_cols, devices))
    low_update = lax.optimization_barrier((low_forward.astype(jnp.float32) - back_term).astype(jnp.bfloat16)).astype(jnp.float32)
    low_solution = jnp.einsum("jab,jak->jbk", low_inv.astype(jnp.float32), low_update)
    return low_solution, jnp.stack(top_out)
```

```python
import jax
import jax.numpy as jnp
from jax import lax
from jax.sharding import PartitionSpec as P


def shifted(x, axis, size, shift):
    return lax.ppermute(x, axis, [(i, (i + shift) % size) for i in range(size)])


def swapped(x, axis, size, bit):
    return lax.ppermute(x, axis, [(i, i ^ bit) for i in range(size)])


def butterfly_sum(x, axis, size):
    bit = 1
    while bit < size:
        x = x + swapped(x, axis, size, bit)
        bit *= 2
    return x


def local(low_rhs, low_inv, low_tiles, tile_rows, tile_cols, top_rhs, top_inv, top_tiles):
    peers = lax.axis_size("col")
    rows_n = lax.axis_size("row")
    levels = top_rhs.shape[0]
    share = top_rhs.shape[1]
    position = lax.axis_index("row")
    me = lax.axis_index("col")

    stacked = jnp.concatenate([top_inv, top_tiles], axis=0)
    whole = lax.all_gather(stacked, "row", axis=1, tiled=True)
    inv_all = whole[:levels]
    tiles_all = whole[levels:]

    slot_rows = tile_rows[0]
    slot_cols = tile_cols[0] % peers
    alive = slot_rows >= 0
    safe_rows = jnp.maximum(slot_rows, 0)
    own_tiles = low_tiles[0]
    low_forward = jnp.dot(low_inv[0], low_rhs[0], preferred_element_type=jnp.float32).astype(
        jnp.bfloat16
    )
    received = [low_forward] + [shifted(low_forward, "col", peers, s) for s in range(1, peers)]
    order = [(me - s) % peers for s in range(peers)]
    by_source = jnp.stack(received)
    source_of = jnp.stack(order)
    slot_pick = jnp.argmax(source_of[None, :] == slot_cols[:, None], axis=1)
    products = jnp.einsum(
        "sab,sbk->sak", own_tiles, by_source[slot_pick], preferred_element_type=jnp.float32
    )
    pick_level = (slot_rows[:, None] == jnp.arange(levels, dtype=jnp.int32)[None, :]).astype(
        jnp.float32
    )
    coupling = jnp.einsum("st,sak->tak", pick_level, products, precision=lax.Precision.HIGHEST)
    own_rhs = jnp.zeros((levels, share * rows_n, top_rhs.shape[2]), jnp.float32)
    own_rhs = lax.dynamic_update_slice_in_dim(own_rhs, top_rhs.astype(jnp.float32), position * share, 1)
    coupling = coupling - jnp.where(me == 0, own_rhs, 0.0)
    coupling = butterfly_sum(coupling, "col", peers)
    coupling = butterfly_sum(coupling, "row", rows_n)

    top_forward = []
    for level in range(levels):
        residue = -coupling[level]
        for u in range(level):
            residue = residue - jnp.dot(
                tiles_all[level * (level - 1) // 2 + u],
                top_forward[u],
                preferred_element_type=jnp.float32,
            )
        top_forward.append(
            jnp.dot(
                inv_all[level], residue.astype(jnp.bfloat16), preferred_element_type=jnp.float32
            ).astype(jnp.bfloat16)
        )
    top_back = [None] * levels
    top_slices = [None] * levels
    for level in reversed(range(levels)):
        update = top_forward[level].astype(jnp.float32)
        for k in range(level + 1, levels):
            update = update - lax.dot_general(
                tiles_all[k * (k - 1) // 2 + level],
                top_back[k],
                (((0,), (0,)), ((), ())),
                preferred_element_type=jnp.float32,
            )
        solved = lax.dot_general(
            inv_all[level],
            update.astype(jnp.bfloat16),
            (((0,), (0,)), ((), ())),
            preferred_element_type=jnp.float32,
        )
        top_slices[level] = lax.dynamic_slice_in_dim(solved, position * share, share, 0)
        top_back[level] = solved.astype(jnp.bfloat16)
    back_stack = jnp.stack(top_back)
    products_back = jnp.einsum(
        "sab,sak->sbk", own_tiles, back_stack[safe_rows], preferred_element_type=jnp.float32
    )
    pick_peer = (
        (slot_cols[:, None] == source_of[None, :]) & alive[:, None]
    ).astype(jnp.float32)
    terms = jnp.einsum(
        "sp,sbk->pbk", pick_peer, products_back, precision=lax.Precision.HIGHEST
    ).astype(jnp.bfloat16)
    returned = terms[0].astype(jnp.float32)
    for s in range(1, peers):
        returned = returned + shifted(terms[s], "col", peers, peers - s).astype(jnp.float32)
    low_update = (low_forward.astype(jnp.float32) - returned).astype(jnp.bfloat16)
    low_solution = lax.dot_general(
        low_inv[0], low_update, (((0,), (0,)), ((), ())), preferred_element_type=jnp.float32
    )
    return (low_solution[None], jnp.stack(top_slices))


def solution(mesh):
    in_specs = (
        P(("row", "col"), None, None),
        P(("row", "col"), None, None),
        P(("row", "col"), None, None, None),
        P(("row", "col"), None),
        P(("row", "col"), None),
        P(None, "row", None),
        P(None, "row", None),
        P(None, "row", None),
    )
    out_specs = (P(("row", "col"), None, None), P(None, "row", None))
    return jax.shard_map(local, mesh=mesh, in_specs=in_specs, out_specs=out_specs, check_vma=False)
```

```python
import jax
import jax.numpy as jnp
from jax import lax
from jax.sharding import PartitionSpec as P


def shifted(x, axis, size, shift):
    return lax.ppermute(x, axis, [(i, (i + shift) % size) for i in range(size)])


def swapped(x, axis, size, bit):
    return lax.ppermute(x, axis, [(i, i ^ bit) for i in range(size)])


def butterfly_sum(x, axis, size):
    bit = 1
    while bit < size:
        x = x + swapped(x, axis, size, bit)
        bit *= 2
    return x


def summed_everywhere(x, peers, rows_n, me):
    shape = x.shape
    chunks = x.reshape(peers, -1, shape[-1]).astype(jnp.bfloat16)
    bit = peers // 2
    while bit >= 1:
        halves = chunks.reshape(2, -1, *chunks.shape[1:])
        mine = (me // bit) % 2
        keep = lax.dynamic_index_in_dim(halves, mine, 0, keepdims=False)
        give = lax.dynamic_index_in_dim(halves, 1 - mine, 0, keepdims=False)
        got = swapped(give, "col", peers, bit)
        chunks = (keep.astype(jnp.float32) + got.astype(jnp.float32)).astype(jnp.bfloat16)
        bit //= 2
    part = chunks[0]
    bit = 1
    while bit < rows_n:
        got = swapped(part, "row", rows_n, bit)
        part = (part.astype(jnp.float32) + got.astype(jnp.float32)).astype(jnp.bfloat16)
        bit *= 2
    pieces = [part] + [shifted(part, "col", peers, s) for s in range(1, peers)]
    stacked = jnp.stack(pieces)
    index = (me - jnp.arange(peers)) % peers
    ordered = jnp.zeros_like(stacked).at[index].set(stacked)
    return ordered.reshape(shape).astype(jnp.float32)


def local(low_rhs, low_inv, low_tiles, tile_rows, tile_cols, top_rhs, top_inv, top_tiles):
    peers = lax.axis_size("col")
    rows_n = lax.axis_size("row")
    levels = top_rhs.shape[0]
    share = top_rhs.shape[1]
    position = lax.axis_index("row")
    me = lax.axis_index("col")

    stacked = jnp.concatenate([top_inv, top_tiles], axis=0)
    quarter = share // peers
    mine = lax.dynamic_slice_in_dim(stacked, me * quarter, quarter, 1)
    pulled = lax.all_gather(mine, "row", axis=0)
    shared = lax.all_gather(pulled, "col", axis=0)
    whole = jnp.transpose(shared, (2, 1, 0, 3, 4)).reshape(
        stacked.shape[0], rows_n * share, stacked.shape[2]
    )
    inv_all = whole[:levels]
    tiles_all = whole[levels:]

    slot_rows = tile_rows[0]
    slot_cols = tile_cols[0] % peers
    alive = slot_rows >= 0
    safe_rows = jnp.maximum(slot_rows, 0)
    own_tiles = low_tiles[0]
    low_forward = jnp.dot(low_inv[0], low_rhs[0], preferred_element_type=jnp.float32).astype(
        jnp.bfloat16
    )
    received = [low_forward] + [shifted(low_forward, "col", peers, s) for s in range(1, peers)]
    order = [(me - s) % peers for s in range(peers)]
    by_source = jnp.stack(received)
    source_of = jnp.stack(order)
    slot_pick = jnp.argmax(source_of[None, :] == slot_cols[:, None], axis=1)
    products = jnp.einsum(
        "sab,sbk->sak", own_tiles, by_source[slot_pick], preferred_element_type=jnp.float32
    )
    pick_level = (slot_rows[:, None] == jnp.arange(levels, dtype=jnp.int32)[None, :]).astype(
        jnp.float32
    )
    coupling = jnp.einsum("st,sak->tak", pick_level, products, precision=lax.Precision.HIGHEST)
    own_rhs = jnp.zeros((levels, share * rows_n, top_rhs.shape[2]), jnp.float32)
    own_rhs = lax.dynamic_update_slice_in_dim(own_rhs, top_rhs.astype(jnp.float32), position * share, 1)
    coupling = coupling - jnp.where(me == 0, own_rhs, 0.0)
    coupling = summed_everywhere(coupling, peers, rows_n, me)

    top_forward = []
    for level in range(levels):
        residue = -coupling[level]
        for u in range(level):
            residue = residue - jnp.dot(
                tiles_all[level * (level - 1) // 2 + u],
                top_forward[u],
                preferred_element_type=jnp.float32,
            )
        top_forward.append(
            jnp.dot(
                inv_all[level], residue.astype(jnp.bfloat16), preferred_element_type=jnp.float32
            ).astype(jnp.bfloat16)
        )
    top_back = [None] * levels
    top_slices = [None] * levels
    for level in reversed(range(levels)):
        update = top_forward[level].astype(jnp.float32)
        for k in range(level + 1, levels):
            update = update - lax.dot_general(
                tiles_all[k * (k - 1) // 2 + level],
                top_back[k],
                (((0,), (0,)), ((), ())),
                preferred_element_type=jnp.float32,
            )
        solved = lax.dot_general(
            inv_all[level],
            update.astype(jnp.bfloat16),
            (((0,), (0,)), ((), ())),
            preferred_element_type=jnp.float32,
        )
        top_slices[level] = lax.dynamic_slice_in_dim(solved, position * share, share, 0)
        top_back[level] = solved.astype(jnp.bfloat16)
    back_stack = jnp.stack(top_back)
    products_back = jnp.einsum(
        "sab,sak->sbk", own_tiles, back_stack[safe_rows], preferred_element_type=jnp.float32
    )
    pick_peer = (
        (slot_cols[:, None] == source_of[None, :]) & alive[:, None]
    ).astype(jnp.float32)
    terms = jnp.einsum(
        "sp,sbk->pbk", pick_peer, products_back, precision=lax.Precision.HIGHEST
    ).astype(jnp.bfloat16)
    returned = terms[0].astype(jnp.float32)
    for s in range(1, peers):
        returned = returned + shifted(terms[s], "col", peers, peers - s).astype(jnp.float32)
    low_update = (low_forward.astype(jnp.float32) - returned).astype(jnp.bfloat16)
    low_solution = lax.dot_general(
        low_inv[0], low_update, (((0,), (0,)), ((), ())), preferred_element_type=jnp.float32
    )
    return (low_solution[None], jnp.stack(top_slices))


def solution(mesh):
    in_specs = (
        P(("row", "col"), None, None),
        P(("row", "col"), None, None),
        P(("row", "col"), None, None, None),
        P(("row", "col"), None),
        P(("row", "col"), None),
        P(None, "row", None),
        P(None, "row", None),
        P(None, "row", None),
    )
    out_specs = (P(("row", "col"), None, None), P(None, "row", None))
    return jax.shard_map(local, mesh=mesh, in_specs=in_specs, out_specs=out_specs, check_vma=False)
```

```python
import jax
import jax.numpy as jnp
import numpy as np
from jax import lax
from jax.sharding import PartitionSpec as P


def shifted(x, axis, size, shift):
    return lax.ppermute(x, axis, [(i, (i + shift) % size) for i in range(size)])


def swapped(x, axis, size, bit):
    return lax.ppermute(x, axis, [(i, i ^ bit) for i in range(size)])


def broadcast_from(x, owner, me, axis, size):
    got = None
    for s in range(1, size):
        part = lax.ppermute(x, axis, [(owner, (owner + s) % size)])
        got = part if got is None else got + part
    return jnp.where(me == owner, x, got)


def pair_index(t, u):
    return t * (t - 1) // 2 + u


def tile_table(levels):
    table = np.zeros((levels, levels - 1), np.int32)
    for c in range(levels):
        for j in range(levels - 1):
            table[c, j] = pair_index(c, j) if j < c else pair_index(j + 1, c)
    return table


def summed_chunks(x, peers, rows_n, me):
    chunks = x.reshape(peers, -1, x.shape[-1]).astype(jnp.bfloat16)
    bit = peers // 2
    while bit >= 1:
        halves = chunks.reshape(2, -1, *chunks.shape[1:])
        mine = (me // bit) % 2
        keep = lax.dynamic_index_in_dim(halves, mine, 0, keepdims=False)
        give = lax.dynamic_index_in_dim(halves, 1 - mine, 0, keepdims=False)
        got = swapped(give, "col", peers, bit)
        chunks = (keep.astype(jnp.float32) + got.astype(jnp.float32)).astype(jnp.bfloat16)
        bit //= 2
    part = chunks[0]
    bit = 1
    while bit < rows_n:
        got = swapped(part, "row", rows_n, bit)
        part = (part.astype(jnp.float32) + got.astype(jnp.float32)).astype(jnp.bfloat16)
        bit *= 2
    return part


def gathered_chunks(part, peers, me):
    pieces = [part] + [shifted(part, "col", peers, s) for s in range(1, peers)]
    stacked = jnp.stack(pieces)
    source = (me - jnp.arange(peers)) % peers
    return jnp.zeros_like(stacked).at[source].set(stacked)


def local(low_rhs, low_inv, low_tiles, tile_rows, tile_cols, top_rhs, top_inv, top_tiles):
    peers = lax.axis_size("col")
    rows_n = lax.axis_size("row")
    levels = top_rhs.shape[0]
    share = top_rhs.shape[1]
    width = top_rhs.shape[2]
    position = lax.axis_index("row")
    me = lax.axis_index("col")
    owned = jnp.minimum(me, levels - 1)

    picks = jnp.asarray(tile_table(levels))[owned]
    mine = jnp.concatenate(
        [lax.dynamic_index_in_dim(top_inv, owned, 0), jnp.take(top_tiles, picks, axis=0)], axis=0
    )
    mats = lax.all_gather(mine, "row", axis=1, tiled=True)
    inv = mats[0]

    slot_rows = tile_rows[0]
    slot_cols = tile_cols[0] % peers
    alive = slot_rows >= 0
    safe_rows = jnp.maximum(slot_rows, 0)
    own_tiles = low_tiles[0]
    low_forward = jnp.dot(low_inv[0], low_rhs[0], preferred_element_type=jnp.float32).astype(
        jnp.bfloat16
    )
    received = [low_forward] + [shifted(low_forward, "col", peers, s) for s in range(1, peers)]
    source_of = (me - jnp.arange(peers)) % peers
    by_source = jnp.stack(received)
    slot_pick = jnp.argmax(source_of[None, :] == slot_cols[:, None], axis=1)
    products = jnp.einsum(
        "sab,sbk->sak", own_tiles, by_source[slot_pick], preferred_element_type=jnp.float32
    )
    pick_level = (slot_rows[:, None] == jnp.arange(levels, dtype=jnp.int32)[None, :]).astype(
        jnp.float32
    )
    coupling = jnp.einsum("st,sak->tak", pick_level, products, precision=lax.Precision.HIGHEST)
    own_rhs = jnp.zeros((levels, share * rows_n, width), jnp.float32)
    own_rhs = lax.dynamic_update_slice_in_dim(own_rhs, top_rhs.astype(jnp.float32), position * share, 1)
    coupling = coupling - jnp.where(me == 0, own_rhs, 0.0)
    part = summed_chunks(coupling, peers, rows_n, me)
    if peers == levels:
        level_sum = part
    else:
        level_sum = gathered_chunks(part, peers, me).reshape(levels, -1, width)[owned]
    rhs_level = -level_sum.astype(jnp.float32)

    top_forward = [None] * levels
    for level in range(levels):
        residue = rhs_level
        for u in range(level):
            residue = residue - jnp.dot(mats[1 + u], top_forward[u], preferred_element_type=jnp.float32)
        solved = jnp.dot(inv, residue.astype(jnp.bfloat16), preferred_element_type=jnp.float32)
        solved = solved.astype(jnp.bfloat16)
        if level < levels - 1:
            solved = broadcast_from(solved, level, me, "col", peers)
        top_forward[level] = solved
    top_back = [None] * levels
    top_slices = [None] * levels
    for level in reversed(range(levels)):
        update = top_forward[level].astype(jnp.float32)
        for k in range(level + 1, levels):
            update = update - lax.dot_general(
                mats[k], top_back[k], (((0,), (0,)), ((), ())), preferred_element_type=jnp.float32
            )
        solved = lax.dot_general(
            inv, update.astype(jnp.bfloat16), (((0,), (0,)), ((), ())), preferred_element_type=jnp.float32
        )
        solved = broadcast_from(solved, level, me, "col", peers)
        top_slices[level] = lax.dynamic_slice_in_dim(solved, position * share, share, 0)
        top_back[level] = solved.astype(jnp.bfloat16)

    back_stack = jnp.stack(top_back)
    products_back = jnp.einsum(
        "sab,sak->sbk", own_tiles, back_stack[safe_rows], preferred_element_type=jnp.float32
    )
    pick_peer = ((slot_cols[:, None] == source_of[None, :]) & alive[:, None]).astype(jnp.float32)
    terms = jnp.einsum(
        "sp,sbk->pbk", pick_peer, products_back, precision=lax.Precision.HIGHEST
    ).astype(jnp.bfloat16)
    returned = terms[0].astype(jnp.float32)
    for s in range(1, peers):
        returned = returned + shifted(terms[s], "col", peers, peers - s).astype(jnp.float32)
    low_update = (low_forward.astype(jnp.float32) - returned).astype(jnp.bfloat16)
    low_solution = lax.dot_general(
        low_inv[0], low_update, (((0,), (0,)), ((), ())), preferred_element_type=jnp.float32
    )
    return (low_solution[None], jnp.stack(top_slices))


def solution(mesh):
    in_specs = (
        P(("row", "col"), None, None),
        P(("row", "col"), None, None),
        P(("row", "col"), None, None, None),
        P(("row", "col"), None),
        P(("row", "col"), None),
        P(None, "row", None),
        P(None, "row", None),
        P(None, "row", None),
    )
    out_specs = (P(("row", "col"), None, None), P(None, "row", None))
    return jax.shard_map(local, mesh=mesh, in_specs=in_specs, out_specs=out_specs, check_vma=False)
```

```python
import jax
import jax.numpy as jnp
import numpy as np
from jax import lax
from jax.sharding import PartitionSpec as P


def shifted(x, axis, size, shift):
    return lax.ppermute(x, axis, [(i, (i + shift) % size) for i in range(size)])


def swapped(x, axis, size, bit):
    return lax.ppermute(x, axis, [(i, i ^ bit) for i in range(size)])


def broadcast_from(x, owner, me, axis, size):
    got = None
    for s in range(1, size):
        part = lax.ppermute(x, axis, [(owner, (owner + s) % size)])
        got = part if got is None else got + part
    return jnp.where(me == owner, x, got)


def pair_index(t, u):
    return t * (t - 1) // 2 + u


def tile_table(levels):
    table = np.zeros((levels, levels - 1), np.int32)
    for c in range(levels):
        for j in range(levels - 1):
            table[c, j] = pair_index(c, j) if j < c else pair_index(j + 1, c)
    return table


def summed_chunks(x, peers, rows_n, me):
    chunks = x.reshape(peers, -1, x.shape[-1]).astype(jnp.bfloat16)
    bit = peers // 2
    while bit >= 1:
        halves = chunks.reshape(2, -1, *chunks.shape[1:])
        mine = (me // bit) % 2
        keep = lax.dynamic_index_in_dim(halves, mine, 0, keepdims=False)
        give = lax.dynamic_index_in_dim(halves, 1 - mine, 0, keepdims=False)
        got = swapped(give, "col", peers, bit)
        chunks = (keep.astype(jnp.float32) + got.astype(jnp.float32)).astype(jnp.bfloat16)
        bit //= 2
    part = chunks[0]
    bit = 1
    while bit < rows_n:
        got = swapped(part, "row", rows_n, bit)
        part = (part.astype(jnp.float32) + got.astype(jnp.float32)).astype(jnp.bfloat16)
        bit *= 2
    return part


def gathered_chunks(part, peers, me):
    pieces = [part] + [shifted(part, "col", peers, s) for s in range(1, peers)]
    stacked = jnp.stack(pieces)
    source = (me - jnp.arange(peers)) % peers
    return jnp.zeros_like(stacked).at[source].set(stacked)


def local(low_rhs, low_inv, low_tiles, tile_rows, tile_cols, top_rhs, top_inv, top_tiles):
    peers = lax.axis_size("col")
    rows_n = lax.axis_size("row")
    levels = top_rhs.shape[0]
    share = top_rhs.shape[1]
    width = top_rhs.shape[2]
    position = lax.axis_index("row")
    me = lax.axis_index("col")
    owned = jnp.minimum(me, levels - 1)

    picks = jnp.asarray(tile_table(levels))[owned]
    mine = jnp.concatenate(
        [lax.dynamic_index_in_dim(top_inv, owned, 0), jnp.take(top_tiles, picks, axis=0)], axis=0
    )
    mats = lax.all_gather(mine, "row", axis=1, tiled=True)
    inv = mats[0]

    slot_rows = tile_rows[0]
    slot_cols = tile_cols[0] % peers
    alive = slot_rows >= 0
    safe_rows = jnp.maximum(slot_rows, 0)
    own_tiles = low_tiles[0]
    low_forward = jnp.dot(low_inv[0], low_rhs[0], preferred_element_type=jnp.float32).astype(
        jnp.bfloat16
    )
    received = [low_forward] + [shifted(low_forward, "col", peers, s) for s in range(1, peers)]
    source_of = (me - jnp.arange(peers)) % peers
    by_source = jnp.stack(received)
    slot_pick = jnp.argmax(source_of[None, :] == slot_cols[:, None], axis=1)
    products = jnp.einsum(
        "sab,sbk->sak", own_tiles, by_source[slot_pick], preferred_element_type=jnp.float32
    )
    pick_level = (slot_rows[:, None] == jnp.arange(levels, dtype=jnp.int32)[None, :]).astype(
        jnp.float32
    )
    coupling = jnp.einsum("st,sak->tak", pick_level, products, precision=lax.Precision.HIGHEST)
    own_rhs = jnp.zeros((levels, share * rows_n, width), jnp.float32)
    own_rhs = lax.dynamic_update_slice_in_dim(own_rhs, top_rhs.astype(jnp.float32), position * share, 1)
    coupling = coupling - jnp.where(me == 0, own_rhs, 0.0)
    part = summed_chunks(coupling, peers, rows_n, me)
    if peers == levels:
        level_sum = part
    else:
        level_sum = gathered_chunks(part, peers, me).reshape(levels, -1, width)[owned]
    rhs_level = -level_sum.astype(jnp.float32)

    top_forward = [None] * levels
    pushed = None
    for level in range(levels):
        residue = rhs_level
        if level > 0:
            pushed = lax.ppermute(pushed, "col", [(level - 1, level)])
            residue = residue - pushed[0]
        solved = jnp.dot(inv, residue.astype(jnp.bfloat16), preferred_element_type=jnp.float32)
        top_forward[level] = solved.astype(jnp.bfloat16)
        if level < levels - 1:
            later = jnp.einsum(
                "kab,bc->kac", mats[level + 1 : levels], top_forward[level], preferred_element_type=jnp.float32
            )
            pushed = later if level == 0 else pushed[1:] + later
    own_solution = None
    for level in reversed(range(levels)):
        update = top_forward[level].astype(jnp.float32)
        if level < levels - 1:
            pushed = lax.ppermute(pushed, "col", [(level + 1, level)])
            update = update - pushed[level]
        solved = lax.dot_general(
            inv, update.astype(jnp.bfloat16), (((0,), (0,)), ((), ())), preferred_element_type=jnp.float32
        )
        own_solution = solved if own_solution is None else jnp.where(me == level, solved, own_solution)
        if level > 0:
            earlier = jnp.einsum(
                "uab,ac->ubc", mats[1 : level + 1], solved.astype(jnp.bfloat16), preferred_element_type=jnp.float32
            )
            pushed = earlier if level == levels - 1 else pushed[:level] + earlier
    solutions = gathered_chunks(own_solution, peers, me)[:levels]
    top_slices = [lax.dynamic_slice_in_dim(solutions[t], position * share, share, 0) for t in range(levels)]
    top_back = [solutions[t].astype(jnp.bfloat16) for t in range(levels)]

    back_stack = jnp.stack(top_back)
    products_back = jnp.einsum(
        "sab,sak->sbk", own_tiles, back_stack[safe_rows], preferred_element_type=jnp.float32
    )
    pick_peer = ((slot_cols[:, None] == source_of[None, :]) & alive[:, None]).astype(jnp.float32)
    terms = jnp.einsum(
        "sp,sbk->pbk", pick_peer, products_back, precision=lax.Precision.HIGHEST
    ).astype(jnp.bfloat16)
    returned = terms[0].astype(jnp.float32)
    for s in range(1, peers):
        returned = returned + shifted(terms[s], "col", peers, peers - s).astype(jnp.float32)
    low_update = (low_forward.astype(jnp.float32) - returned).astype(jnp.bfloat16)
    low_solution = lax.dot_general(
        low_inv[0], low_update, (((0,), (0,)), ((), ())), preferred_element_type=jnp.float32
    )
    return (low_solution[None], jnp.stack(top_slices))


def solution(mesh):
    in_specs = (
        P(("row", "col"), None, None),
        P(("row", "col"), None, None),
        P(("row", "col"), None, None, None),
        P(("row", "col"), None),
        P(("row", "col"), None),
        P(None, "row", None),
        P(None, "row", None),
        P(None, "row", None),
    )
    out_specs = (P(("row", "col"), None, None), P(None, "row", None))
    return jax.shard_map(local, mesh=mesh, in_specs=in_specs, out_specs=out_specs, check_vma=False)
```

```python
import jax
import jax.numpy as jnp
import numpy as np
from jax import lax
from jax.experimental import pallas as pl
from jax.experimental.pallas import tpu as pltpu
from jax.sharding import PartitionSpec as P

SMEM = pl.BlockSpec(memory_space=pltpu.SMEM)
VMEM = pl.BlockSpec(memory_space=pltpu.VMEM)


def coupling_kernel(rows_ref, picks_ref, fold_ref, tiles_ref, panels_ref, rhs_ref, out_ref):
    out_ref[...] = jnp.zeros_like(out_ref)
    share = rhs_ref.shape[1]

    @pl.when(fold_ref[1] == 0)
    def _():
        start = pl.multiple_of(fold_ref[0], 8)
        out_ref[:, pl.ds(start, share), :] = -rhs_ref[...].astype(jnp.float32)

    for s in range(tiles_ref.shape[0]):
        level = rows_ref[s]

        @pl.when(level >= 0)
        def _():
            prod = jnp.dot(tiles_ref[s], panels_ref[picks_ref[s]], preferred_element_type=jnp.float32)
            out_ref[level] += prod


def coupling_terms(slot_rows, picks, fold, tiles, panels, rhs, levels):
    return pl.pallas_call(
        coupling_kernel,
        out_shape=jax.ShapeDtypeStruct((levels, panels.shape[1], panels.shape[2]), jnp.float32),
        in_specs=[SMEM, SMEM, SMEM, VMEM, VMEM, VMEM],
        out_specs=VMEM,
    )(slot_rows, picks, fold, tiles, panels, rhs)


def back_kernel(rows_ref, dests_ref, tiles_ref, back_ref, out_ref, acc_ref):
    acc_ref[...] = jnp.zeros_like(acc_ref)
    for s in range(tiles_ref.shape[0]):
        level = rows_ref[s]

        @pl.when(level >= 0)
        def _():
            prod = lax.dot_general(
                tiles_ref[s], back_ref[level], (((0,), (0,)), ((), ())), preferred_element_type=jnp.float32
            )
            acc_ref[dests_ref[s]] += prod

    out_ref[...] = acc_ref[...].astype(out_ref.dtype)


def back_terms(slot_rows, dests, tiles, back, peers):
    shape = (peers, tiles.shape[2], back.shape[2])
    return pl.pallas_call(
        back_kernel,
        out_shape=jax.ShapeDtypeStruct(shape, jnp.bfloat16),
        in_specs=[SMEM, SMEM, VMEM, VMEM],
        out_specs=VMEM,
        scratch_shapes=[pltpu.VMEM(shape, jnp.float32)],
    )(slot_rows, dests, tiles, back)


def shifted(x, axis, size, shift):
    return lax.ppermute(x, axis, [(i, (i + shift) % size) for i in range(size)])


def swapped(x, axis, size, bit):
    return lax.ppermute(x, axis, [(i, i ^ bit) for i in range(size)])


def broadcast_from(x, owner, me, axis, size):
    got = None
    for s in range(1, size):
        part = lax.ppermute(x, axis, [(owner, (owner + s) % size)])
        got = part if got is None else got + part
    return jnp.where(me == owner, x, got)


def pair_index(t, u):
    return t * (t - 1) // 2 + u


def tile_table(levels):
    table = np.zeros((levels, levels - 1), np.int32)
    for c in range(levels):
        for j in range(levels - 1):
            table[c, j] = pair_index(c, j) if j < c else pair_index(j + 1, c)
    return table


def summed_chunks(x, peers, rows_n, me):
    chunks = x.reshape(peers, -1, x.shape[-1]).astype(jnp.bfloat16)
    bit = peers // 2
    while bit >= 1:
        halves = chunks.reshape(2, -1, *chunks.shape[1:])
        mine = (me // bit) % 2
        keep = lax.dynamic_index_in_dim(halves, mine, 0, keepdims=False)
        give = lax.dynamic_index_in_dim(halves, 1 - mine, 0, keepdims=False)
        got = swapped(give, "col", peers, bit)
        chunks = (keep.astype(jnp.float32) + got.astype(jnp.float32)).astype(jnp.bfloat16)
        bit //= 2
    part = chunks[0]
    bit = 1
    while bit < rows_n:
        got = swapped(part, "row", rows_n, bit)
        part = (part.astype(jnp.float32) + got.astype(jnp.float32)).astype(jnp.bfloat16)
        bit *= 2
    return part


def gathered_chunks(part, peers, me):
    pieces = [part] + [shifted(part, "col", peers, s) for s in range(1, peers)]
    stacked = jnp.stack(pieces)
    source = (me - jnp.arange(peers)) % peers
    return jnp.zeros_like(stacked).at[source].set(stacked)


def local(low_rhs, low_inv, low_tiles, tile_rows, tile_cols, top_rhs, top_inv, top_tiles):
    peers = lax.axis_size("col")
    rows_n = lax.axis_size("row")
    levels = top_rhs.shape[0]
    share = top_rhs.shape[1]
    width = top_rhs.shape[2]
    position = lax.axis_index("row")
    me = lax.axis_index("col")
    owned = jnp.minimum(me, levels - 1)

    picks = jnp.asarray(tile_table(levels))[owned]
    mine = jnp.concatenate(
        [lax.dynamic_index_in_dim(top_inv, owned, 0), jnp.take(top_tiles, picks, axis=0)], axis=0
    )
    mats = lax.all_gather(mine, "row", axis=1, tiled=True)
    inv = mats[0]

    slot_rows = tile_rows[0]
    slot_cols = tile_cols[0] % peers
    own_tiles = low_tiles[0]
    low_forward = jnp.dot(low_inv[0], low_rhs[0], preferred_element_type=jnp.float32).astype(
        jnp.bfloat16
    )
    received = [low_forward] + [shifted(low_forward, "col", peers, s) for s in range(1, peers)]
    source_of = (me - jnp.arange(peers)) % peers
    by_source = jnp.stack(received)
    slot_pick = jnp.argmax(source_of[None, :] == slot_cols[:, None], axis=1).astype(jnp.int32)
    fold = jnp.stack([position * share, me]).astype(jnp.int32)
    coupling = coupling_terms(slot_rows, slot_pick, fold, own_tiles, by_source, top_rhs, levels)
    part = summed_chunks(coupling, peers, rows_n, me)
    if peers == levels:
        level_sum = part
    else:
        level_sum = gathered_chunks(part, peers, me).reshape(levels, -1, width)[owned]
    rhs_level = -level_sum.astype(jnp.float32)

    top_forward = [None] * levels
    pushed = None
    for level in range(levels):
        residue = rhs_level
        if level > 0:
            pushed = lax.ppermute(pushed, "col", [(level - 1, level)])
            residue = residue - pushed[0]
        solved = jnp.dot(inv, residue.astype(jnp.bfloat16), preferred_element_type=jnp.float32)
        top_forward[level] = solved.astype(jnp.bfloat16)
        if level < levels - 1:
            later = jnp.einsum(
                "kab,bc->kac", mats[level + 1 : levels], top_forward[level], preferred_element_type=jnp.float32
            )
            pushed = later if level == 0 else pushed[1:] + later
    own_solution = None
    for level in reversed(range(levels)):
        update = top_forward[level].astype(jnp.float32)
        if level < levels - 1:
            pushed = lax.ppermute(pushed, "col", [(level + 1, level)])
            update = update - pushed[level]
        solved = lax.dot_general(
            inv, update.astype(jnp.bfloat16), (((0,), (0,)), ((), ())), preferred_element_type=jnp.float32
        )
        own_solution = solved if own_solution is None else jnp.where(me == level, solved, own_solution)
        if level > 0:
            earlier = jnp.einsum(
                "uab,ac->ubc", mats[1 : level + 1], solved.astype(jnp.bfloat16), preferred_element_type=jnp.float32
            )
            pushed = earlier if level == levels - 1 else pushed[:level] + earlier
    solutions = gathered_chunks(own_solution, peers, me)[:levels]
    top_slices = [lax.dynamic_slice_in_dim(solutions[t], position * share, share, 0) for t in range(levels)]
    top_back = [solutions[t].astype(jnp.bfloat16) for t in range(levels)]

    back_stack = jnp.stack(top_back)
    dests = ((me - slot_cols) % peers).astype(jnp.int32)
    terms = back_terms(slot_rows, dests, own_tiles, back_stack, peers)
    returned = terms[0].astype(jnp.float32)
    for s in range(1, peers):
        returned = returned + shifted(terms[s], "col", peers, peers - s).astype(jnp.float32)
    low_update = (low_forward.astype(jnp.float32) - returned).astype(jnp.bfloat16)
    low_solution = lax.dot_general(
        low_inv[0], low_update, (((0,), (0,)), ((), ())), preferred_element_type=jnp.float32
    )
    return (low_solution[None], jnp.stack(top_slices))


def solution(mesh):
    in_specs = (
        P(("row", "col"), None, None),
        P(("row", "col"), None, None),
        P(("row", "col"), None, None, None),
        P(("row", "col"), None),
        P(("row", "col"), None),
        P(None, "row", None),
        P(None, "row", None),
        P(None, "row", None),
    )
    out_specs = (P(("row", "col"), None, None), P(None, "row", None))
    return jax.shard_map(local, mesh=mesh, in_specs=in_specs, out_specs=out_specs, check_vma=False)
```

```python
import jax
import jax.numpy as jnp
import numpy as np
from jax import lax
from jax.experimental import pallas as pl
from jax.experimental.pallas import tpu as pltpu
from jax.sharding import PartitionSpec as P

SMEM = pl.BlockSpec(memory_space=pltpu.SMEM)
VMEM = pl.BlockSpec(memory_space=pltpu.VMEM)


def coupling_kernel(rows_ref, picks_ref, fold_ref, tiles_ref, panels_ref, rhs_ref, out_ref):
    out_ref[...] = jnp.zeros_like(out_ref)
    share = rhs_ref.shape[1]

    @pl.when(fold_ref[1] == 0)
    def _():
        start = pl.multiple_of(fold_ref[0], 8)
        out_ref[:, pl.ds(start, share), :] = -rhs_ref[...].astype(jnp.float32)

    for s in range(tiles_ref.shape[0]):
        level = rows_ref[s]

        @pl.when(level >= 0)
        def _():
            prod = jnp.dot(tiles_ref[s], panels_ref[picks_ref[s]], preferred_element_type=jnp.float32)
            out_ref[level] += prod


def coupling_terms(slot_rows, picks, fold, tiles, panels, rhs, levels):
    return pl.pallas_call(
        coupling_kernel,
        out_shape=jax.ShapeDtypeStruct((levels, panels.shape[1], panels.shape[2]), jnp.float32),
        in_specs=[SMEM, SMEM, SMEM, VMEM, VMEM, VMEM],
        out_specs=VMEM,
    )(slot_rows, picks, fold, tiles, panels, rhs)


def back_upper_kernel(rows_ref, dests_ref, tiles_ref, back_ref, out_ref):
    out_ref[...] = jnp.zeros_like(out_ref)
    for s in range(tiles_ref.shape[0]):
        level = rows_ref[s]

        @pl.when(level >= 1)
        def _():
            prod = lax.dot_general(
                tiles_ref[s], back_ref[level - 1], (((0,), (0,)), ((), ())), preferred_element_type=jnp.float32
            )
            out_ref[dests_ref[s]] += prod


def back_first_kernel(rows_ref, dests_ref, tiles_ref, back_ref, upper_ref, out_ref, acc_ref):
    acc_ref[...] = upper_ref[...]
    for s in range(tiles_ref.shape[0]):
        level = rows_ref[s]

        @pl.when(level == 0)
        def _():
            prod = lax.dot_general(
                tiles_ref[s], back_ref[...], (((0,), (0,)), ((), ())), preferred_element_type=jnp.float32
            )
            acc_ref[dests_ref[s]] += prod

    out_ref[...] = acc_ref[...].astype(out_ref.dtype)


def back_upper(slot_rows, dests, tiles, back, peers):
    shape = (peers, tiles.shape[2], back.shape[2])
    return pl.pallas_call(
        back_upper_kernel,
        out_shape=jax.ShapeDtypeStruct(shape, jnp.float32),
        in_specs=[SMEM, SMEM, VMEM, VMEM],
        out_specs=VMEM,
    )(slot_rows, dests, tiles, back)


def back_first(slot_rows, dests, tiles, back, upper):
    return pl.pallas_call(
        back_first_kernel,
        out_shape=jax.ShapeDtypeStruct(upper.shape, jnp.bfloat16),
        in_specs=[SMEM, SMEM, VMEM, VMEM, VMEM],
        out_specs=VMEM,
        scratch_shapes=[pltpu.VMEM(upper.shape, jnp.float32)],
    )(slot_rows, dests, tiles, back, upper)


def shifted(x, axis, size, shift):
    return lax.ppermute(x, axis, [(i, (i + shift) % size) for i in range(size)])


def swapped(x, axis, size, bit):
    return lax.ppermute(x, axis, [(i, i ^ bit) for i in range(size)])


def broadcast_from(x, owner, me, axis, size):
    got = None
    for s in range(1, size):
        part = lax.ppermute(x, axis, [(owner, (owner + s) % size)])
        got = part if got is None else got + part
    return jnp.where(me == owner, x, got)


def pair_index(t, u):
    return t * (t - 1) // 2 + u


def tile_table(levels):
    table = np.zeros((levels, levels - 1), np.int32)
    for c in range(levels):
        for j in range(levels - 1):
            table[c, j] = pair_index(c, j) if j < c else pair_index(j + 1, c)
    return table


def summed_chunks(x, peers, rows_n, me):
    chunks = x.reshape(peers, -1, x.shape[-1]).astype(jnp.bfloat16)
    bit = peers // 2
    while bit >= 1:
        halves = chunks.reshape(2, -1, *chunks.shape[1:])
        mine = (me // bit) % 2
        keep = lax.dynamic_index_in_dim(halves, mine, 0, keepdims=False)
        give = lax.dynamic_index_in_dim(halves, 1 - mine, 0, keepdims=False)
        got = swapped(give, "col", peers, bit)
        chunks = (keep.astype(jnp.float32) + got.astype(jnp.float32)).astype(jnp.bfloat16)
        bit //= 2
    part = chunks[0]
    bit = 1
    while bit < rows_n:
        got = swapped(part, "row", rows_n, bit)
        part = (part.astype(jnp.float32) + got.astype(jnp.float32)).astype(jnp.bfloat16)
        bit *= 2
    return part


def gathered_chunks(part, peers, me):
    pieces = [part] + [shifted(part, "col", peers, s) for s in range(1, peers)]
    stacked = jnp.stack(pieces)
    source = (me - jnp.arange(peers)) % peers
    return jnp.zeros_like(stacked).at[source].set(stacked)


def local(low_rhs, low_inv, low_tiles, tile_rows, tile_cols, top_rhs, top_inv, top_tiles):
    peers = lax.axis_size("col")
    rows_n = lax.axis_size("row")
    levels = top_rhs.shape[0]
    share = top_rhs.shape[1]
    width = top_rhs.shape[2]
    position = lax.axis_index("row")
    me = lax.axis_index("col")
    owned = jnp.minimum(me, levels - 1)

    picks = jnp.asarray(tile_table(levels))[owned]
    mine = jnp.concatenate(
        [lax.dynamic_index_in_dim(top_inv, owned, 0), jnp.take(top_tiles, picks, axis=0)], axis=0
    )
    mats = lax.all_gather(mine, "row", axis=1, tiled=True)
    inv = mats[0]

    slot_rows = tile_rows[0]
    slot_cols = tile_cols[0] % peers
    own_tiles = low_tiles[0]
    low_forward = jnp.dot(low_inv[0], low_rhs[0], preferred_element_type=jnp.float32).astype(
        jnp.bfloat16
    )
    received = [low_forward] + [shifted(low_forward, "col", peers, s) for s in range(1, peers)]
    source_of = (me - jnp.arange(peers)) % peers
    by_source = jnp.stack(received)
    slot_pick = jnp.argmax(source_of[None, :] == slot_cols[:, None], axis=1).astype(jnp.int32)
    fold = jnp.stack([position * share, me]).astype(jnp.int32)
    coupling = coupling_terms(slot_rows, slot_pick, fold, own_tiles, by_source, top_rhs, levels)
    part = summed_chunks(coupling, peers, rows_n, me)
    if peers == levels:
        level_sum = part
    else:
        level_sum = gathered_chunks(part, peers, me).reshape(levels, -1, width)[owned]
    rhs_level = -level_sum.astype(jnp.float32)

    top_forward = [None] * levels
    pushed = None
    for level in range(levels):
        residue = rhs_level
        if level > 0:
            pushed = lax.ppermute(pushed, "col", [(level - 1, level)])
            residue = residue - pushed[0]
        solved = jnp.dot(inv, residue.astype(jnp.bfloat16), preferred_element_type=jnp.float32)
        top_forward[level] = solved.astype(jnp.bfloat16)
        if level < levels - 1:
            later = jnp.einsum(
                "kab,bc->kac", mats[level + 1 : levels], top_forward[level], preferred_element_type=jnp.float32
            )
            pushed = later if level == 0 else pushed[1:] + later
    solutions = [None] * levels
    for level in reversed(range(levels)):
        update = top_forward[level].astype(jnp.float32)
        if level < levels - 1:
            pushed = lax.ppermute(pushed, "col", [(level + 1, level)])
            update = update - pushed[level]
        solved = lax.dot_general(
            inv, update.astype(jnp.bfloat16), (((0,), (0,)), ((), ())), preferred_element_type=jnp.float32
        )
        if level > 0:
            earlier = jnp.einsum(
                "uab,ac->ubc", mats[1 : level + 1], solved.astype(jnp.bfloat16), preferred_element_type=jnp.float32
            )
            pushed = earlier if level == levels - 1 else pushed[:level] + earlier
        solutions[level] = broadcast_from(solved, level, me, "col", peers)
    top_slices = [lax.dynamic_slice_in_dim(solutions[t], position * share, share, 0) for t in range(levels)]
    top_back = [solutions[t].astype(jnp.bfloat16) for t in range(levels)]

    dests = ((me - slot_cols) % peers).astype(jnp.int32)
    upper = back_upper(slot_rows, dests, own_tiles, jnp.stack(top_back[1:]), peers)
    terms = back_first(slot_rows, dests, own_tiles, top_back[0], upper)
    returned = terms[0].astype(jnp.float32)
    for s in range(1, peers):
        returned = returned + shifted(terms[s], "col", peers, peers - s).astype(jnp.float32)
    low_update = (low_forward.astype(jnp.float32) - returned).astype(jnp.bfloat16)
    low_solution = lax.dot_general(
        low_inv[0], low_update, (((0,), (0,)), ((), ())), preferred_element_type=jnp.float32
    )
    return (low_solution[None], jnp.stack(top_slices))


def solution(mesh):
    in_specs = (
        P(("row", "col"), None, None),
        P(("row", "col"), None, None),
        P(("row", "col"), None, None, None),
        P(("row", "col"), None),
        P(("row", "col"), None),
        P(None, "row", None),
        P(None, "row", None),
        P(None, "row", None),
    )
    out_specs = (P(("row", "col"), None, None), P(None, "row", None))
    return jax.shard_map(local, mesh=mesh, in_specs=in_specs, out_specs=out_specs, check_vma=False)
```

```python
import jax
import jax.numpy as jnp
import numpy as np
from jax import lax
from jax.experimental import pallas as pl
from jax.experimental.pallas import tpu as pltpu
from jax.sharding import PartitionSpec as P

SMEM = pl.BlockSpec(memory_space=pltpu.SMEM)
VMEM = pl.BlockSpec(memory_space=pltpu.VMEM)


def coupling_kernel(rows_ref, picks_ref, fold_ref, tiles_ref, panels_ref, rhs_ref, out_ref):
    out_ref[...] = jnp.zeros_like(out_ref)
    share = rhs_ref.shape[1]

    @pl.when(fold_ref[1] == 0)
    def _():
        start = pl.multiple_of(fold_ref[0], 8)
        out_ref[:, pl.ds(start, share), :] = -rhs_ref[...].astype(jnp.float32)

    for s in range(tiles_ref.shape[0]):
        level = rows_ref[s]

        @pl.when(level >= 0)
        def _():
            prod = jnp.dot(tiles_ref[s], panels_ref[picks_ref[s]], preferred_element_type=jnp.float32)
            out_ref[level] += prod


def coupling_terms(slot_rows, picks, fold, tiles, panels, rhs, levels):
    return pl.pallas_call(
        coupling_kernel,
        out_shape=jax.ShapeDtypeStruct((levels, panels.shape[1], panels.shape[2]), jnp.float32),
        in_specs=[SMEM, SMEM, SMEM, VMEM, VMEM, VMEM],
        out_specs=VMEM,
    )(slot_rows, picks, fold, tiles, panels, rhs)


def back_kernel(rows_ref, dests_ref, tiles_ref, back_ref, out_ref, acc_ref):
    acc_ref[...] = jnp.zeros_like(acc_ref)
    for s in range(tiles_ref.shape[0]):
        level = rows_ref[s]

        @pl.when(level >= 0)
        def _():
            prod = lax.dot_general(
                tiles_ref[s], back_ref[level], (((0,), (0,)), ((), ())), preferred_element_type=jnp.float32
            )
            acc_ref[dests_ref[s]] += prod

    out_ref[...] = acc_ref[...].astype(out_ref.dtype)


def back_terms(slot_rows, dests, tiles, back, peers):
    shape = (peers, tiles.shape[2], back.shape[2])
    return pl.pallas_call(
        back_kernel,
        out_shape=jax.ShapeDtypeStruct(shape, jnp.bfloat16),
        in_specs=[SMEM, SMEM, VMEM, VMEM],
        out_specs=VMEM,
        scratch_shapes=[pltpu.VMEM(shape, jnp.float32)],
    )(slot_rows, dests, tiles, back)


def shifted(x, axis, size, shift):
    return lax.ppermute(x, axis, [(i, (i + shift) % size) for i in range(size)])


def swapped(x, axis, size, bit):
    return lax.ppermute(x, axis, [(i, i ^ bit) for i in range(size)])


def broadcast_from(x, owner, me, axis, size):
    got = None
    for s in range(1, size):
        part = lax.ppermute(x, axis, [(owner, (owner + s) % size)])
        got = part if got is None else got + part
    return jnp.where(me == owner, x, got)


def pair_index(t, u):
    return t * (t - 1) // 2 + u


def holdings(levels):
    hold = [[] for _ in range(levels)]
    for t in range(1, levels):
        for u in range(t):
            keeper = t if (levels > 2 and t == levels - 1 and u == 0) else u
            hold[keeper].append((t, u))
    return hold


def tile_table(levels):
    hold = holdings(levels)
    width = max(len(h) for h in hold)
    table = np.zeros((levels, width), np.int32)
    for c in range(levels):
        for j, (t, u) in enumerate(hold[c]):
            table[c, j] = pair_index(t, u)
    return table


def plus(a, b):
    return b if a is None else a + b


def held_slice(mats, positions):
    if positions == list(range(positions[0], positions[0] + len(positions))):
        return mats[1 + positions[0] : 1 + positions[0] + len(positions)]
    return jnp.stack([mats[1 + p] for p in positions])


def summed_chunks(x, peers, rows_n, me):
    chunks = x.reshape(peers, -1, x.shape[-1]).astype(jnp.bfloat16)
    bit = peers // 2
    while bit >= 1:
        halves = chunks.reshape(2, -1, *chunks.shape[1:])
        mine = (me // bit) % 2
        keep = lax.dynamic_index_in_dim(halves, mine, 0, keepdims=False)
        give = lax.dynamic_index_in_dim(halves, 1 - mine, 0, keepdims=False)
        got = swapped(give, "col", peers, bit)
        chunks = (keep.astype(jnp.float32) + got.astype(jnp.float32)).astype(jnp.bfloat16)
        bit //= 2
    part = chunks[0]
    bit = 1
    while bit < rows_n:
        got = swapped(part, "row", rows_n, bit)
        part = (part.astype(jnp.float32) + got.astype(jnp.float32)).astype(jnp.bfloat16)
        bit *= 2
    return part


def gathered_chunks(part, peers, me):
    pieces = [part] + [shifted(part, "col", peers, s) for s in range(1, peers)]
    stacked = jnp.stack(pieces)
    source = (me - jnp.arange(peers)) % peers
    return jnp.zeros_like(stacked).at[source].set(stacked)


def local(low_rhs, low_inv, low_tiles, tile_rows, tile_cols, top_rhs, top_inv, top_tiles):
    peers = lax.axis_size("col")
    rows_n = lax.axis_size("row")
    levels = top_rhs.shape[0]
    share = top_rhs.shape[1]
    width = top_rhs.shape[2]
    position = lax.axis_index("row")
    me = lax.axis_index("col")
    owned = jnp.minimum(me, levels - 1)

    picks = jnp.asarray(tile_table(levels))[owned]
    mine = jnp.concatenate(
        [lax.dynamic_index_in_dim(top_inv, owned, 0), jnp.take(top_tiles, picks, axis=0)], axis=0
    )
    mats = lax.all_gather(mine, "row", axis=1, tiled=True)
    inv = mats[0]

    slot_rows = tile_rows[0]
    slot_cols = tile_cols[0] % peers
    own_tiles = low_tiles[0]
    low_forward = jnp.dot(low_inv[0], low_rhs[0], preferred_element_type=jnp.float32).astype(
        jnp.bfloat16
    )
    received = [low_forward] + [shifted(low_forward, "col", peers, s) for s in range(1, peers)]
    source_of = (me - jnp.arange(peers)) % peers
    by_source = jnp.stack(received)
    slot_pick = jnp.argmax(source_of[None, :] == slot_cols[:, None], axis=1).astype(jnp.int32)
    fold = jnp.stack([position * share, me]).astype(jnp.int32)
    coupling = coupling_terms(slot_rows, slot_pick, fold, own_tiles, by_source, top_rhs, levels)
    part = summed_chunks(coupling, peers, rows_n, me)
    if peers == levels:
        level_sum = part
    else:
        level_sum = gathered_chunks(part, peers, me).reshape(levels, -1, width)[owned]
    rhs_level = -level_sum.astype(jnp.float32)

    hold = holdings(levels)
    top_forward = [None] * levels
    pushed = {}
    direct = {}
    for level in range(levels):
        residue = rhs_level
        if level > 0:
            keys = [k for k in range(level, levels) if pushed.get(k) is not None]
            message = lax.ppermute(jnp.stack([pushed[k] for k in keys]), "col", [(level - 1, level)])
            pushed = {k: message[i] for i, k in enumerate(keys)}
            if pushed.get(level) is not None:
                residue = residue - pushed[level]
        for j, (t, u) in enumerate(hold[level]):
            if t == level:
                residue = residue - jnp.dot(mats[1 + j], direct[(t, u)], preferred_element_type=jnp.float32)
        solved = jnp.dot(inv, residue.astype(jnp.bfloat16), preferred_element_type=jnp.float32)
        top_forward[level] = solved.astype(jnp.bfloat16)
        for k in range(level + 1, levels):
            if (k, level) in hold[k]:
                direct[(k, level)] = lax.ppermute(top_forward[level], "col", [(level, k)])
        positions = [j for j, (t, u) in enumerate(hold[level]) if u == level]
        if positions and level < levels - 1:
            later = jnp.einsum(
                "kab,bc->kac", held_slice(mats, positions), top_forward[level], preferred_element_type=jnp.float32
            )
            for i, j in enumerate(positions):
                k = hold[level][j][0]
                pushed[k] = plus(pushed.get(k), later[i])
    own_solution = None
    carried = {}
    for level in reversed(range(levels)):
        update = top_forward[level].astype(jnp.float32)
        if level < levels - 1:
            keys = sorted(carried)
            message = lax.ppermute(jnp.stack([carried[k] for k in keys]), "col", [(level + 1, level)])
            carried = {k: message[i] for i, k in enumerate(keys)}
            if carried.get(("q", level)) is not None:
                update = update - carried.pop(("q", level))
        for j, (t, u) in enumerate(hold[level]):
            if u == level:
                update = update - lax.dot_general(
                    mats[1 + j],
                    carried[("x", t)].astype(jnp.bfloat16),
                    (((0,), (0,)), ((), ())),
                    preferred_element_type=jnp.float32,
                )
        solved = lax.dot_general(
            inv, update.astype(jnp.bfloat16), (((0,), (0,)), ((), ())), preferred_element_type=jnp.float32
        )
        own_solution = solved if own_solution is None else jnp.where(me == level, solved, own_solution)
        if level == 0:
            break
        for j, (t, u) in enumerate(hold[level]):
            if t == level:
                term = lax.dot_general(
                    mats[1 + j],
                    solved.astype(jnp.bfloat16),
                    (((0,), (0,)), ((), ())),
                    preferred_element_type=jnp.float32,
                )
                carried[("q", u)] = plus(carried.get(("q", u)), term)
        carried[("x", level)] = solved
        below = {t for c in range(level) for (t, u) in hold[c] if u == c}
        carried = {k: v for k, v in carried.items() if k[0] == "q" or k[1] in below}
    solutions = gathered_chunks(own_solution, peers, me)[:levels]
    top_slices = [lax.dynamic_slice_in_dim(solutions[t], position * share, share, 0) for t in range(levels)]
    top_back = [solutions[t].astype(jnp.bfloat16) for t in range(levels)]

    back_stack = jnp.stack(top_back)
    dests = ((me - slot_cols) % peers).astype(jnp.int32)
    terms = back_terms(slot_rows, dests, own_tiles, back_stack, peers)
    returned = terms[0].astype(jnp.float32)
    for s in range(1, peers):
        returned = returned + shifted(terms[s], "col", peers, peers - s).astype(jnp.float32)
    low_update = (low_forward.astype(jnp.float32) - returned).astype(jnp.bfloat16)
    low_solution = lax.dot_general(
        low_inv[0], low_update, (((0,), (0,)), ((), ())), preferred_element_type=jnp.float32
    )
    return (low_solution[None], jnp.stack(top_slices))


def solution(mesh):
    in_specs = (
        P(("row", "col"), None, None),
        P(("row", "col"), None, None),
        P(("row", "col"), None, None, None),
        P(("row", "col"), None),
        P(("row", "col"), None),
        P(None, "row", None),
        P(None, "row", None),
        P(None, "row", None),
    )
    out_specs = (P(("row", "col"), None, None), P(None, "row", None))
    return jax.shard_map(local, mesh=mesh, in_specs=in_specs, out_specs=out_specs, check_vma=False)
```

```python
import jax
import jax.numpy as jnp
import numpy as np
from jax import lax
from jax.experimental import pallas as pl
from jax.experimental.pallas import tpu as pltpu
from jax.sharding import PartitionSpec as P

SMEM = pl.BlockSpec(memory_space=pltpu.SMEM)
VMEM = pl.BlockSpec(memory_space=pltpu.VMEM)


def coupling_kernel(rows_ref, picks_ref, fold_ref, tiles_ref, panels_ref, rhs_ref, out_ref):
    out_ref[...] = jnp.zeros_like(out_ref)
    share = rhs_ref.shape[1]

    @pl.when(fold_ref[1] == 0)
    def _():
        start = pl.multiple_of(fold_ref[0], 8)
        out_ref[:, pl.ds(start, share), :] = -rhs_ref[...].astype(jnp.float32)

    for s in range(tiles_ref.shape[0]):
        level = rows_ref[s]

        @pl.when(level >= 0)
        def _():
            prod = jnp.dot(tiles_ref[s], panels_ref[picks_ref[s]], preferred_element_type=jnp.float32)
            out_ref[level] += prod


def coupling_terms(slot_rows, picks, fold, tiles, panels, rhs, levels):
    return pl.pallas_call(
        coupling_kernel,
        out_shape=jax.ShapeDtypeStruct((levels, panels.shape[1], panels.shape[2]), jnp.float32),
        in_specs=[SMEM, SMEM, SMEM, VMEM, VMEM, VMEM],
        out_specs=VMEM,
    )(slot_rows, picks, fold, tiles, panels, rhs)


def back_kernel(rows_ref, dests_ref, tiles_ref, back_ref, out_ref, acc_ref):
    acc_ref[...] = jnp.zeros_like(acc_ref)
    for s in range(tiles_ref.shape[0]):
        level = rows_ref[s]

        @pl.when(level >= 0)
        def _():
            prod = lax.dot_general(
                tiles_ref[s], back_ref[level], (((0,), (0,)), ((), ())), preferred_element_type=jnp.float32
            )
            acc_ref[dests_ref[s]] += prod

    out_ref[...] = acc_ref[...].astype(out_ref.dtype)


def back_terms(slot_rows, dests, tiles, back, peers):
    shape = (peers, tiles.shape[2], back.shape[2])
    return pl.pallas_call(
        back_kernel,
        out_shape=jax.ShapeDtypeStruct(shape, jnp.bfloat16),
        in_specs=[SMEM, SMEM, VMEM, VMEM],
        out_specs=VMEM,
        scratch_shapes=[pltpu.VMEM(shape, jnp.float32)],
    )(slot_rows, dests, tiles, back)


def shifted(x, axis, size, shift):
    return lax.ppermute(x, axis, [(i, (i + shift) % size) for i in range(size)])


def swapped(x, axis, size, bit):
    return lax.ppermute(x, axis, [(i, i ^ bit) for i in range(size)])


def broadcast_from(x, owner, me, axis, size):
    got = None
    for s in range(1, size):
        part = lax.ppermute(x, axis, [(owner, (owner + s) % size)])
        got = part if got is None else got + part
    return jnp.where(me == owner, x, got)


def forward_hop(level, rhs, pushed_in, in_keys, direct, row_pos, mats, pushes, out_keys):
    def kernel(*refs):
        refs = list(refs)
        rhs_ref = refs.pop(0)
        pin_ref = refs.pop(0) if in_keys else None
        direct_ref = refs.pop(0) if row_pos else None
        mats_ref = refs.pop(0)
        f_ref = refs.pop(0)
        out_ref = refs.pop(0) if out_keys else None
        residue = rhs_ref[...]
        if level in in_keys:
            residue = residue - pin_ref[in_keys.index(level)]
        for pos in row_pos:
            residue = residue - jnp.dot(mats_ref[pos], direct_ref[...], preferred_element_type=jnp.float32)
        f = jnp.dot(mats_ref[0], residue.astype(jnp.bfloat16), preferred_element_type=jnp.float32)
        f = f.astype(jnp.bfloat16)
        f_ref[...] = f
        for i, k in enumerate(out_keys):
            value = pin_ref[in_keys.index(k)] if k in in_keys else None
            if k in pushes:
                value = plus(value, jnp.dot(mats_ref[pushes[k]], f, preferred_element_type=jnp.float32))
            out_ref[i] = value

    args = [rhs] + ([pushed_in] if in_keys else []) + ([direct] if row_pos else []) + [mats]
    shape = rhs.shape
    outs = [jax.ShapeDtypeStruct(shape, jnp.bfloat16)]
    if out_keys:
        outs.append(jax.ShapeDtypeStruct((len(out_keys),) + shape, jnp.float32))
    result = pl.pallas_call(
        kernel, out_shape=outs, in_specs=[VMEM] * len(args), out_specs=[VMEM] * len(outs)
    )(*args)
    return result[0], (result[1] if out_keys else None)


def backward_hop(level, forward, carried_in, in_keys, mats, pulls, pushes, out_keys):
    def kernel(*refs):
        refs = list(refs)
        f_ref = refs.pop(0)
        cin_ref = refs.pop(0) if in_keys else None
        mats_ref = refs.pop(0)
        x_ref = refs.pop(0)
        out_ref = refs.pop(0) if out_keys else None
        update = f_ref[...].astype(jnp.float32)
        if ("q", level) in in_keys:
            update = update - cin_ref[in_keys.index(("q", level))]
        for pos, k in pulls:
            update = update - lax.dot_general(
                mats_ref[pos],
                cin_ref[in_keys.index(("x", k))].astype(jnp.bfloat16),
                (((0,), (0,)), ((), ())),
                preferred_element_type=jnp.float32,
            )
        x = lax.dot_general(
            mats_ref[0], update.astype(jnp.bfloat16), (((0,), (0,)), ((), ())), preferred_element_type=jnp.float32
        )
        x_ref[...] = x
        xb = x.astype(jnp.bfloat16)
        for i, key in enumerate(out_keys):
            if key == ("x", level):
                out_ref[i] = x
                continue
            value = cin_ref[in_keys.index(key)] if key in in_keys else None
            if key[0] == "q" and key[1] in pushes:
                term = lax.dot_general(
                    mats_ref[pushes[key[1]]], xb, (((0,), (0,)), ((), ())), preferred_element_type=jnp.float32
                )
                value = plus(value, term)
            out_ref[i] = value

    args = [forward] + ([carried_in] if in_keys else []) + [mats]
    shape = forward.shape
    outs = [jax.ShapeDtypeStruct(shape, jnp.float32)]
    if out_keys:
        outs.append(jax.ShapeDtypeStruct((len(out_keys),) + shape, jnp.float32))
    result = pl.pallas_call(
        kernel, out_shape=outs, in_specs=[VMEM] * len(args), out_specs=[VMEM] * len(outs)
    )(*args)
    return result[0], (result[1] if out_keys else None)


def pair_index(t, u):
    return t * (t - 1) // 2 + u


def holdings(levels):
    hold = [[] for _ in range(levels)]
    for t in range(1, levels):
        for u in range(t):
            keeper = t if (levels > 2 and t == levels - 1 and u == 0) else u
            hold[keeper].append((t, u))
    return hold


def tile_table(levels):
    hold = holdings(levels)
    width = max(len(h) for h in hold)
    table = np.zeros((levels, width), np.int32)
    for c in range(levels):
        for j, (t, u) in enumerate(hold[c]):
            table[c, j] = pair_index(t, u)
    return table


def plus(a, b):
    return b if a is None else a + b


def held_slice(mats, positions):
    if positions == list(range(positions[0], positions[0] + len(positions))):
        return mats[1 + positions[0] : 1 + positions[0] + len(positions)]
    return jnp.stack([mats[1 + p] for p in positions])


def summed_chunks(x, peers, rows_n, me):
    chunks = x.reshape(peers, -1, x.shape[-1]).astype(jnp.bfloat16)
    bit = peers // 2
    while bit >= 1:
        halves = chunks.reshape(2, -1, *chunks.shape[1:])
        mine = (me // bit) % 2
        keep = lax.dynamic_index_in_dim(halves, mine, 0, keepdims=False)
        give = lax.dynamic_index_in_dim(halves, 1 - mine, 0, keepdims=False)
        got = swapped(give, "col", peers, bit)
        chunks = (keep.astype(jnp.float32) + got.astype(jnp.float32)).astype(jnp.bfloat16)
        bit //= 2
    part = chunks[0]
    bit = 1
    while bit < rows_n:
        got = swapped(part, "row", rows_n, bit)
        part = (part.astype(jnp.float32) + got.astype(jnp.float32)).astype(jnp.bfloat16)
        bit *= 2
    return part


def gathered_chunks(part, peers, me):
    pieces = [part] + [shifted(part, "col", peers, s) for s in range(1, peers)]
    stacked = jnp.stack(pieces)
    source = (me - jnp.arange(peers)) % peers
    return jnp.zeros_like(stacked).at[source].set(stacked)


def local(low_rhs, low_inv, low_tiles, tile_rows, tile_cols, top_rhs, top_inv, top_tiles):
    peers = lax.axis_size("col")
    rows_n = lax.axis_size("row")
    levels = top_rhs.shape[0]
    share = top_rhs.shape[1]
    width = top_rhs.shape[2]
    position = lax.axis_index("row")
    me = lax.axis_index("col")
    owned = jnp.minimum(me, levels - 1)

    picks = jnp.asarray(tile_table(levels))[owned]
    mine = jnp.concatenate(
        [lax.dynamic_index_in_dim(top_inv, owned, 0), jnp.take(top_tiles, picks, axis=0)], axis=0
    )
    mats = lax.all_gather(mine, "row", axis=1, tiled=True)
    inv = mats[0]

    slot_rows = tile_rows[0]
    slot_cols = tile_cols[0] % peers
    own_tiles = low_tiles[0]
    low_forward = jnp.dot(low_inv[0], low_rhs[0], preferred_element_type=jnp.float32).astype(
        jnp.bfloat16
    )
    received = [low_forward] + [shifted(low_forward, "col", peers, s) for s in range(1, peers)]
    source_of = (me - jnp.arange(peers)) % peers
    by_source = jnp.stack(received)
    slot_pick = jnp.argmax(source_of[None, :] == slot_cols[:, None], axis=1).astype(jnp.int32)
    fold = jnp.stack([position * share, me]).astype(jnp.int32)
    coupling = coupling_terms(slot_rows, slot_pick, fold, own_tiles, by_source, top_rhs, levels)
    part = summed_chunks(coupling, peers, rows_n, me)
    if peers == levels:
        level_sum = part
    else:
        level_sum = gathered_chunks(part, peers, me).reshape(levels, -1, width)[owned]
    rhs_level = -level_sum.astype(jnp.float32)

    hold = holdings(levels)
    top_forward = [None] * levels
    message, in_keys = None, []
    pending = set()
    direct = {}
    for level in range(levels):
        if level > 0:
            message = lax.ppermute(message, "col", [(level - 1, level)])
        row_pos = [1 + j for j, (t, u) in enumerate(hold[level]) if t == level]
        pushes = {t: 1 + j for j, (t, u) in enumerate(hold[level]) if u == level}
        pending = (pending | set(pushes)) - {level}
        out_keys = sorted(k for k in pending if k > level) if level < levels - 1 else []
        sources = [u for (t, u) in hold[level] if t == level]
        solved, sent = forward_hop(
            level,
            rhs_level,
            message,
            in_keys,
            direct[(level, sources[0])] if sources else None,
            row_pos,
            mats,
            pushes,
            out_keys,
        )
        top_forward[level] = solved
        for k in range(level + 1, levels):
            if (k, level) in hold[k]:
                direct[(k, level)] = lax.ppermute(solved, "col", [(level, k)])
        message, in_keys = sent, out_keys
    own_solution = None
    message, in_keys = None, []
    for level in reversed(range(levels)):
        if level < levels - 1:
            message = lax.ppermute(message, "col", [(level + 1, level)])
        pulls = [(1 + j, t) for j, (t, u) in enumerate(hold[level]) if u == level]
        pushes = {u: 1 + j for j, (t, u) in enumerate(hold[level]) if t == level}
        below = {t for c in range(level) for (t, u) in hold[c] if u == c}
        out_keys = []
        if level > 0:
            qs = {k[1] for k in in_keys if k[0] == "q"} | set(pushes)
            out_keys = [("q", u) for u in sorted(qs) if u < level]
            xs = {k[1] for k in in_keys if k[0] == "x"} | {level}
            out_keys += [("x", k) for k in sorted(xs) if k in below]
        solved, sent = backward_hop(
            level, top_forward[level], message, in_keys, mats, pulls, pushes, out_keys
        )
        own_solution = solved if own_solution is None else jnp.where(me == level, solved, own_solution)
        message, in_keys = sent, out_keys
    solutions = gathered_chunks(own_solution, peers, me)[:levels]
    top_slices = [lax.dynamic_slice_in_dim(solutions[t], position * share, share, 0) for t in range(levels)]
    top_back = [solutions[t].astype(jnp.bfloat16) for t in range(levels)]

    back_stack = jnp.stack(top_back)
    dests = ((me - slot_cols) % peers).astype(jnp.int32)
    terms = back_terms(slot_rows, dests, own_tiles, back_stack, peers)
    returned = terms[0].astype(jnp.float32)
    for s in range(1, peers):
        returned = returned + shifted(terms[s], "col", peers, peers - s).astype(jnp.float32)
    low_update = (low_forward.astype(jnp.float32) - returned).astype(jnp.bfloat16)
    low_solution = lax.dot_general(
        low_inv[0], low_update, (((0,), (0,)), ((), ())), preferred_element_type=jnp.float32
    )
    return (low_solution[None], jnp.stack(top_slices))


def solution(mesh):
    in_specs = (
        P(("row", "col"), None, None),
        P(("row", "col"), None, None),
        P(("row", "col"), None, None, None),
        P(("row", "col"), None),
        P(("row", "col"), None),
        P(None, "row", None),
        P(None, "row", None),
        P(None, "row", None),
    )
    out_specs = (P(("row", "col"), None, None), P(None, "row", None))
    return jax.shard_map(local, mesh=mesh, in_specs=in_specs, out_specs=out_specs, check_vma=False)
```

```python
import jax
import jax.numpy as jnp
import numpy as np
from jax import lax
from jax.experimental import pallas as pl
from jax.experimental.pallas import tpu as pltpu
from jax.sharding import PartitionSpec as P

SMEM = pl.BlockSpec(memory_space=pltpu.SMEM)
VMEM = pl.BlockSpec(memory_space=pltpu.VMEM)


def coupling_kernel(rows_ref, picks_ref, fold_ref, tiles_ref, panels_ref, rhs_ref, out_ref, acc_ref):
    acc_ref[...] = jnp.zeros_like(acc_ref)
    share = rhs_ref.shape[1]

    @pl.when(fold_ref[1] == 0)
    def _():
        start = pl.multiple_of(fold_ref[0], 8)
        acc_ref[:, pl.ds(start, share), :] = -rhs_ref[...].astype(jnp.float32)

    for s in range(tiles_ref.shape[0]):
        level = rows_ref[s]

        @pl.when(level >= 0)
        def _():
            prod = jnp.dot(tiles_ref[s], panels_ref[picks_ref[s]], preferred_element_type=jnp.float32)
            acc_ref[level] += prod

    out_ref[...] = acc_ref[...].astype(out_ref.dtype)


def coupling_terms(slot_rows, picks, fold, tiles, panels, rhs, levels):
    shape = (levels, panels.shape[1], panels.shape[2])
    return pl.pallas_call(
        coupling_kernel,
        out_shape=jax.ShapeDtypeStruct(shape, jnp.bfloat16),
        in_specs=[SMEM, SMEM, SMEM, VMEM, VMEM, VMEM],
        out_specs=VMEM,
        scratch_shapes=[pltpu.VMEM(shape, jnp.float32)],
    )(slot_rows, picks, fold, tiles, panels, rhs)


def back_kernel(rows_ref, dests_ref, tiles_ref, back_ref, out_ref, acc_ref):
    acc_ref[...] = jnp.zeros_like(acc_ref)
    for s in range(tiles_ref.shape[0]):
        level = rows_ref[s]

        @pl.when(level >= 0)
        def _():
            prod = lax.dot_general(
                tiles_ref[s], back_ref[level], (((0,), (0,)), ((), ())), preferred_element_type=jnp.float32
            )
            acc_ref[dests_ref[s]] += prod

    out_ref[...] = acc_ref[...].astype(out_ref.dtype)


def back_terms(slot_rows, dests, tiles, back, peers):
    shape = (peers, tiles.shape[2], back.shape[2])
    return pl.pallas_call(
        back_kernel,
        out_shape=jax.ShapeDtypeStruct(shape, jnp.bfloat16),
        in_specs=[SMEM, SMEM, VMEM, VMEM],
        out_specs=VMEM,
        scratch_shapes=[pltpu.VMEM(shape, jnp.float32)],
    )(slot_rows, dests, tiles, back)


def shifted(x, axis, size, shift):
    return lax.ppermute(x, axis, [(i, (i + shift) % size) for i in range(size)])


def swapped(x, axis, size, bit):
    return lax.ppermute(x, axis, [(i, i ^ bit) for i in range(size)])


def broadcast_from(x, owner, me, axis, size):
    got = None
    for s in range(1, size):
        part = lax.ppermute(x, axis, [(owner, (owner + s) % size)])
        got = part if got is None else got + part
    return jnp.where(me == owner, x, got)


def pair_index(t, u):
    return t * (t - 1) // 2 + u


def tile_table(levels):
    table = np.zeros((levels, levels - 1), np.int32)
    for c in range(levels):
        for j in range(levels - 1):
            table[c, j] = pair_index(c, j) if j < c else pair_index(j + 1, c)
    return table


def summed_chunks(x, peers, rows_n, me):
    chunks = x.reshape(peers, -1, x.shape[-1]).astype(jnp.bfloat16)
    bit = 1
    while bit < peers:
        pairs = chunks.reshape(-1, 2, *chunks.shape[1:])
        mine = (me // bit) % 2
        keep = lax.dynamic_index_in_dim(pairs, mine, 1, keepdims=False)
        give = lax.dynamic_index_in_dim(pairs, 1 - mine, 1, keepdims=False)
        got = swapped(give, "col", peers, bit)
        chunks = (keep.astype(jnp.float32) + got.astype(jnp.float32)).astype(jnp.bfloat16)
        bit *= 2
    part = chunks[0]
    bit = 1
    while bit < rows_n:
        got = swapped(part, "row", rows_n, bit)
        part = (part.astype(jnp.float32) + got.astype(jnp.float32)).astype(jnp.bfloat16)
        bit *= 2
    return part


def gathered_chunks(part, peers, me):
    pieces = [part] + [shifted(part, "col", peers, s) for s in range(1, peers)]
    stacked = jnp.stack(pieces)
    source = (me - jnp.arange(peers)) % peers
    return jnp.zeros_like(stacked).at[source].set(stacked)


def local(low_rhs, low_inv, low_tiles, tile_rows, tile_cols, top_rhs, top_inv, top_tiles):
    peers = lax.axis_size("col")
    rows_n = lax.axis_size("row")
    levels = top_rhs.shape[0]
    share = top_rhs.shape[1]
    width = top_rhs.shape[2]
    position = lax.axis_index("row")
    me = lax.axis_index("col")
    owned = jnp.minimum(me, levels - 1)

    picks = jnp.asarray(tile_table(levels))[owned]
    mine = jnp.concatenate(
        [lax.dynamic_index_in_dim(top_inv, owned, 0), jnp.take(top_tiles, picks, axis=0)], axis=0
    )
    mats = lax.all_gather(mine, "row", axis=1, tiled=True)
    inv = mats[0]

    slot_rows = tile_rows[0]
    slot_cols = tile_cols[0] % peers
    own_tiles = low_tiles[0]
    low_forward = jnp.dot(low_inv[0], low_rhs[0], preferred_element_type=jnp.float32).astype(
        jnp.bfloat16
    )
    received = [low_forward] + [shifted(low_forward, "col", peers, s) for s in range(1, peers)]
    source_of = (me - jnp.arange(peers)) % peers
    by_source = jnp.stack(received)
    slot_pick = jnp.argmax(source_of[None, :] == slot_cols[:, None], axis=1).astype(jnp.int32)
    fold = jnp.stack([position * share, me]).astype(jnp.int32)
    coupling = coupling_terms(slot_rows, slot_pick, fold, own_tiles, by_source, top_rhs, levels)
    part = summed_chunks(coupling, peers, rows_n, me)
    if peers == levels:
        level_sum = part
    else:
        level_sum = gathered_chunks(part, peers, me).reshape(levels, -1, width)[owned]
    rhs_level = -level_sum.astype(jnp.float32)

    top_forward = [None] * levels
    pushed = None
    for level in range(levels):
        residue = rhs_level
        if level > 0:
            pushed = lax.ppermute(pushed, "col", [(level - 1, level)])
            residue = residue - pushed[0]
        solved = jnp.dot(inv, residue.astype(jnp.bfloat16), preferred_element_type=jnp.float32)
        top_forward[level] = solved.astype(jnp.bfloat16)
        if level < levels - 1:
            later = jnp.einsum(
                "kab,bc->kac", mats[level + 1 : levels], top_forward[level], preferred_element_type=jnp.float32
            )
            pushed = later if level == 0 else pushed[1:] + later
    own_solution = None
    for level in reversed(range(levels)):
        update = top_forward[level].astype(jnp.float32)
        if level < levels - 1:
            pushed = lax.ppermute(pushed, "col", [(level + 1, level)])
            update = update - pushed[level]
        solved = lax.dot_general(
            inv, update.astype(jnp.bfloat16), (((0,), (0,)), ((), ())), preferred_element_type=jnp.float32
        )
        own_solution = solved if own_solution is None else jnp.where(me == level, solved, own_solution)
        if level > 0:
            earlier = jnp.einsum(
                "uab,ac->ubc", mats[1 : level + 1], solved.astype(jnp.bfloat16), preferred_element_type=jnp.float32
            )
            pushed = earlier if level == levels - 1 else pushed[:level] + earlier
    solutions = gathered_chunks(own_solution, peers, me)[:levels]
    top_slices = [lax.dynamic_slice_in_dim(solutions[t], position * share, share, 0) for t in range(levels)]
    top_back = [solutions[t].astype(jnp.bfloat16) for t in range(levels)]

    back_stack = jnp.stack(top_back)
    dests = ((me - slot_cols) % peers).astype(jnp.int32)
    terms = back_terms(slot_rows, dests, own_tiles, back_stack, peers)
    returned = terms[0].astype(jnp.float32)
    for s in range(1, peers):
        returned = returned + shifted(terms[s], "col", peers, peers - s).astype(jnp.float32)
    low_update = (low_forward.astype(jnp.float32) - returned).astype(jnp.bfloat16)
    low_solution = lax.dot_general(
        low_inv[0], low_update, (((0,), (0,)), ((), ())), preferred_element_type=jnp.float32
    )
    return (low_solution[None], jnp.stack(top_slices))


def solution(mesh):
    in_specs = (
        P(("row", "col"), None, None),
        P(("row", "col"), None, None),
        P(("row", "col"), None, None, None),
        P(("row", "col"), None),
        P(("row", "col"), None),
        P(None, "row", None),
        P(None, "row", None),
        P(None, "row", None),
    )
    out_specs = (P(("row", "col"), None, None), P(None, "row", None))
    return jax.shard_map(local, mesh=mesh, in_specs=in_specs, out_specs=out_specs, check_vma=False)
```

```python
import functools

import jax
import jax.numpy as jnp
import numpy as np
from jax import lax
from jax.experimental import pallas as pl
from jax.experimental.pallas import tpu as pltpu
from jax.sharding import PartitionSpec as P

SMEM = pl.BlockSpec(memory_space=pltpu.SMEM)
VMEM = pl.BlockSpec(memory_space=pltpu.VMEM)


def coupling_kernel(rows_ref, picks_ref, fold_ref, tiles_ref, panels_ref, rhs_ref, out_ref, acc_ref):
    acc_ref[...] = jnp.zeros_like(acc_ref)
    share = rhs_ref.shape[1]

    @pl.when(fold_ref[1] == 0)
    def _():
        start = pl.multiple_of(fold_ref[0], 8)
        acc_ref[:, pl.ds(start, share), :] = -rhs_ref[...].astype(jnp.float32)

    for s in range(tiles_ref.shape[0]):
        level = rows_ref[s]

        @pl.when(level >= 0)
        def _():
            prod = jnp.dot(tiles_ref[s], panels_ref[picks_ref[s]], preferred_element_type=jnp.float32)
            acc_ref[level] += prod

    out_ref[...] = acc_ref[...].astype(out_ref.dtype)


def coupling_terms(slot_rows, picks, fold, tiles, panels, rhs, levels):
    shape = (levels, panels.shape[1], panels.shape[2])
    return pl.pallas_call(
        coupling_kernel,
        out_shape=jax.ShapeDtypeStruct(shape, jnp.bfloat16),
        in_specs=[SMEM, SMEM, SMEM, VMEM, VMEM, VMEM],
        out_specs=VMEM,
        scratch_shapes=[pltpu.VMEM(shape, jnp.float32)],
    )(slot_rows, picks, fold, tiles, panels, rhs)


def back_kernel(rows_ref, dests_ref, tiles_ref, back_ref, out_ref, acc_ref):
    acc_ref[...] = jnp.zeros_like(acc_ref)
    for s in range(tiles_ref.shape[0]):
        level = rows_ref[s]

        @pl.when(level >= 0)
        def _():
            prod = lax.dot_general(
                tiles_ref[s], back_ref[level], (((0,), (0,)), ((), ())), preferred_element_type=jnp.float32
            )
            acc_ref[dests_ref[s]] += prod

    out_ref[...] = acc_ref[...].astype(out_ref.dtype)


def back_terms(slot_rows, dests, tiles, back, peers):
    shape = (peers, tiles.shape[2], back.shape[2])
    return pl.pallas_call(
        back_kernel,
        out_shape=jax.ShapeDtypeStruct(shape, jnp.bfloat16),
        in_specs=[SMEM, SMEM, VMEM, VMEM],
        out_specs=VMEM,
        scratch_shapes=[pltpu.VMEM(shape, jnp.float32)],
    )(slot_rows, dests, tiles, back)


def shifted(x, axis, size, shift):
    return lax.ppermute(x, axis, [(i, (i + shift) % size) for i in range(size)])


def swapped(x, axis, size, bit):
    return lax.ppermute(x, axis, [(i, i ^ bit) for i in range(size)])


def broadcast_from(x, owner, me, axis, size):
    got = None
    for s in range(1, size):
        part = lax.ppermute(x, axis, [(owner, (owner + s) % size)])
        got = part if got is None else got + part
    return jnp.where(me == owner, x, got)


def tail_kernel(levels, peers, rows_ref, dests_ref, table_ref, start_ref, tiles_ref, *refs):
    x_refs = refs[:peers]
    term_refs = refs[peers : 2 * peers]
    slices_ref = refs[2 * peers]
    acc_ref = refs[2 * peers + 1]
    share = slices_ref.shape[1]
    start = pl.multiple_of(start_ref[0], 8)
    for t in range(levels):
        for p in range(peers):

            @pl.when(table_ref[t] == p)
            def _():
                slices_ref[t] = x_refs[p][pl.ds(start, share), :]

    acc_ref[...] = jnp.zeros_like(acc_ref)
    for s in range(tiles_ref.shape[0]):
        level = rows_ref[s]
        piece = table_ref[jnp.maximum(level, 0)]
        for p in range(peers):

            @pl.when((level >= 0) & (piece == p))
            def _():
                prod = lax.dot_general(
                    tiles_ref[s],
                    x_refs[p][...].astype(jnp.bfloat16),
                    (((0,), (0,)), ((), ())),
                    preferred_element_type=jnp.float32,
                )
                acc_ref[dests_ref[s]] += prod

    for p in range(peers):
        term_refs[p][...] = acc_ref[p].astype(jnp.bfloat16)


def tail_terms(slot_rows, dests, table, start, tiles, pieces, levels, share):
    peers = len(pieces)
    shape = pieces[0].shape
    outs = [jax.ShapeDtypeStruct(shape, jnp.bfloat16) for _ in range(peers)]
    outs.append(jax.ShapeDtypeStruct((levels, share, shape[1]), jnp.float32))
    result = pl.pallas_call(
        functools.partial(tail_kernel, levels, peers),
        out_shape=outs,
        in_specs=[SMEM] * 4 + [VMEM] * (1 + peers),
        out_specs=[VMEM] * (peers + 1),
        scratch_shapes=[pltpu.VMEM((peers,) + shape, jnp.float32)],
    )(slot_rows, dests, table, start, tiles, *pieces)
    return result[:peers], result[peers]


def last_kernel(forward_ref, inv_ref, *refs):
    term_refs = refs[:-1]
    out_ref = refs[-1]
    returned = term_refs[0][...].astype(jnp.float32)
    for ref in term_refs[1:]:
        returned = returned + ref[...].astype(jnp.float32)
    update = (forward_ref[...].astype(jnp.float32) - returned).astype(jnp.bfloat16)
    out_ref[0] = lax.dot_general(
        inv_ref[0], update, (((0,), (0,)), ((), ())), preferred_element_type=jnp.float32
    )


def last_solve(forward, inv, terms):
    return pl.pallas_call(
        last_kernel,
        out_shape=jax.ShapeDtypeStruct((1,) + forward.shape, jnp.float32),
        in_specs=[VMEM] * (2 + len(terms)),
        out_specs=VMEM,
    )(forward, inv, *terms)


def pair_index(t, u):
    return t * (t - 1) // 2 + u


def tile_table(levels):
    table = np.zeros((levels, levels - 1), np.int32)
    for c in range(levels):
        for j in range(levels - 1):
            table[c, j] = pair_index(c, j) if j < c else pair_index(j + 1, c)
    return table


def summed_chunks(x, peers, rows_n, me):
    chunks = x.reshape(peers, -1, x.shape[-1]).astype(jnp.bfloat16)
    bit = 1
    while bit < peers:
        pairs = chunks.reshape(-1, 2, *chunks.shape[1:])
        mine = (me // bit) % 2
        keep = lax.dynamic_index_in_dim(pairs, mine, 1, keepdims=False)
        give = lax.dynamic_index_in_dim(pairs, 1 - mine, 1, keepdims=False)
        got = swapped(give, "col", peers, bit)
        chunks = (keep.astype(jnp.float32) + got.astype(jnp.float32)).astype(jnp.bfloat16)
        bit *= 2
    part = chunks[0]
    bit = 1
    while bit < rows_n:
        got = swapped(part, "row", rows_n, bit)
        part = (part.astype(jnp.float32) + got.astype(jnp.float32)).astype(jnp.bfloat16)
        bit *= 2
    return part


def gathered_chunks(part, peers, me):
    pieces = [part] + [shifted(part, "col", peers, s) for s in range(1, peers)]
    stacked = jnp.stack(pieces)
    source = (me - jnp.arange(peers)) % peers
    return jnp.zeros_like(stacked).at[source].set(stacked)


def local(low_rhs, low_inv, low_tiles, tile_rows, tile_cols, top_rhs, top_inv, top_tiles):
    peers = lax.axis_size("col")
    rows_n = lax.axis_size("row")
    levels = top_rhs.shape[0]
    share = top_rhs.shape[1]
    width = top_rhs.shape[2]
    position = lax.axis_index("row")
    me = lax.axis_index("col")
    owned = jnp.minimum(me, levels - 1)

    picks = jnp.asarray(tile_table(levels))[owned]
    mine = jnp.concatenate(
        [lax.dynamic_index_in_dim(top_inv, owned, 0), jnp.take(top_tiles, picks, axis=0)], axis=0
    )
    mats = lax.all_gather(mine, "row", axis=1, tiled=True)
    inv = mats[0]

    slot_rows = tile_rows[0]
    slot_cols = tile_cols[0] % peers
    own_tiles = low_tiles[0]
    low_forward = jnp.dot(low_inv[0], low_rhs[0], preferred_element_type=jnp.float32).astype(
        jnp.bfloat16
    )
    received = [low_forward] + [shifted(low_forward, "col", peers, s) for s in range(1, peers)]
    source_of = (me - jnp.arange(peers)) % peers
    by_source = jnp.stack(received)
    slot_pick = jnp.argmax(source_of[None, :] == slot_cols[:, None], axis=1).astype(jnp.int32)
    fold = jnp.stack([position * share, me]).astype(jnp.int32)
    coupling = coupling_terms(slot_rows, slot_pick, fold, own_tiles, by_source, top_rhs, levels)
    part = summed_chunks(coupling, peers, rows_n, me)
    if peers == levels:
        level_sum = part
    else:
        level_sum = gathered_chunks(part, peers, me).reshape(levels, -1, width)[owned]
    rhs_level = -level_sum.astype(jnp.float32)

    top_forward = [None] * levels
    pushed = None
    for level in range(levels):
        residue = rhs_level
        if level > 0:
            pushed = lax.ppermute(pushed, "col", [(level - 1, level)])
            residue = residue - pushed[0]
        solved = jnp.dot(inv, residue.astype(jnp.bfloat16), preferred_element_type=jnp.float32)
        top_forward[level] = solved.astype(jnp.bfloat16)
        if level < levels - 1:
            later = jnp.einsum(
                "kab,bc->kac", mats[level + 1 : levels], top_forward[level], preferred_element_type=jnp.float32
            )
            pushed = later if level == 0 else pushed[1:] + later
    own_solution = None
    for level in reversed(range(levels)):
        update = top_forward[level].astype(jnp.float32)
        if level < levels - 1:
            pushed = lax.ppermute(pushed, "col", [(level + 1, level)])
            update = update - pushed[level]
        solved = lax.dot_general(
            inv, update.astype(jnp.bfloat16), (((0,), (0,)), ((), ())), preferred_element_type=jnp.float32
        )
        own_solution = solved if own_solution is None else jnp.where(me == level, solved, own_solution)
        if level > 0:
            earlier = jnp.einsum(
                "uab,ac->ubc", mats[1 : level + 1], solved.astype(jnp.bfloat16), preferred_element_type=jnp.float32
            )
            pushed = earlier if level == levels - 1 else pushed[:level] + earlier
    pieces = [own_solution] + [shifted(own_solution, "col", peers, s) for s in range(1, peers)]
    table = ((me - jnp.arange(levels)) % peers).astype(jnp.int32)
    dests = ((me - slot_cols) % peers).astype(jnp.int32)
    start = (position * share)[None].astype(jnp.int32)
    terms, top_rows = tail_terms(slot_rows, dests, table, start, own_tiles, pieces, levels, share)
    returned = [terms[0]] + [shifted(terms[s], "col", peers, peers - s) for s in range(1, peers)]
    low_solution = last_solve(low_forward, low_inv, returned)
    return (low_solution, top_rows)


def solution(mesh):
    in_specs = (
        P(("row", "col"), None, None),
        P(("row", "col"), None, None),
        P(("row", "col"), None, None, None),
        P(("row", "col"), None),
        P(("row", "col"), None),
        P(None, "row", None),
        P(None, "row", None),
        P(None, "row", None),
    )
    out_specs = (P(("row", "col"), None, None), P(None, "row", None))
    return jax.shard_map(local, mesh=mesh, in_specs=in_specs, out_specs=out_specs, check_vma=False)
```

```python
import functools

import jax
import jax.numpy as jnp
import numpy as np
from jax import lax
from jax.experimental import pallas as pl
from jax.experimental.pallas import tpu as pltpu
from jax.sharding import PartitionSpec as P

SMEM = pl.BlockSpec(memory_space=pltpu.SMEM)
VMEM = pl.BlockSpec(memory_space=pltpu.VMEM)


def coupling_kernel(rows_ref, picks_ref, fold_ref, tiles_ref, panels_ref, rhs_ref, out_ref, acc_ref):
    acc_ref[...] = jnp.zeros_like(acc_ref)
    share = rhs_ref.shape[1]

    @pl.when(fold_ref[1] == 0)
    def _():
        start = pl.multiple_of(fold_ref[0], 8)
        acc_ref[:, pl.ds(start, share), :] = -rhs_ref[...].astype(jnp.float32)

    for s in range(tiles_ref.shape[0]):
        level = rows_ref[s]

        @pl.when(level >= 0)
        def _():
            prod = jnp.dot(tiles_ref[s], panels_ref[picks_ref[s]], preferred_element_type=jnp.float32)
            acc_ref[level] += prod

    out_ref[...] = acc_ref[...].astype(out_ref.dtype)


def coupling_terms(slot_rows, picks, fold, tiles, panels, rhs, levels):
    shape = (levels, panels.shape[1], panels.shape[2])
    return pl.pallas_call(
        coupling_kernel,
        out_shape=jax.ShapeDtypeStruct(shape, jnp.bfloat16),
        in_specs=[SMEM, SMEM, SMEM, VMEM, VMEM, VMEM],
        out_specs=VMEM,
        scratch_shapes=[pltpu.VMEM(shape, jnp.float32)],
    )(slot_rows, picks, fold, tiles, panels, rhs)


def back_kernel(rows_ref, dests_ref, tiles_ref, back_ref, out_ref, acc_ref):
    acc_ref[...] = jnp.zeros_like(acc_ref)
    for s in range(tiles_ref.shape[0]):
        level = rows_ref[s]

        @pl.when(level >= 0)
        def _():
            prod = lax.dot_general(
                tiles_ref[s], back_ref[level], (((0,), (0,)), ((), ())), preferred_element_type=jnp.float32
            )
            acc_ref[dests_ref[s]] += prod

    out_ref[...] = acc_ref[...].astype(out_ref.dtype)


def back_terms(slot_rows, dests, tiles, back, peers):
    shape = (peers, tiles.shape[2], back.shape[2])
    return pl.pallas_call(
        back_kernel,
        out_shape=jax.ShapeDtypeStruct(shape, jnp.bfloat16),
        in_specs=[SMEM, SMEM, VMEM, VMEM],
        out_specs=VMEM,
        scratch_shapes=[pltpu.VMEM(shape, jnp.float32)],
    )(slot_rows, dests, tiles, back)


def shifted(x, axis, size, shift):
    return lax.ppermute(x, axis, [(i, (i + shift) % size) for i in range(size)])


def swapped(x, axis, size, bit):
    return lax.ppermute(x, axis, [(i, i ^ bit) for i in range(size)])


def broadcast_from(x, owner, me, axis, size):
    got = None
    for s in range(1, size):
        part = lax.ppermute(x, axis, [(owner, (owner + s) % size)])
        got = part if got is None else got + part
    return jnp.where(me == owner, x, got)


def tail_kernel(levels, peers, rows_ref, dests_ref, table_ref, start_ref, tiles_ref, *refs):
    x_refs = refs[:peers]
    term_refs = refs[peers : 2 * peers]
    slices_ref = refs[2 * peers]
    acc_ref = refs[2 * peers + 1]
    share = slices_ref.shape[1]
    start = pl.multiple_of(start_ref[0], 8)
    for t in range(levels):
        for p in range(peers):

            @pl.when(table_ref[t] == p)
            def _():
                slices_ref[t] = x_refs[p][pl.ds(start, share), :]

    acc_ref[...] = jnp.zeros_like(acc_ref)
    for s in range(tiles_ref.shape[0]):
        level = rows_ref[s]
        piece = table_ref[jnp.maximum(level, 0)]
        for p in range(peers):

            @pl.when((level >= 0) & (piece == p))
            def _():
                prod = lax.dot_general(
                    tiles_ref[s],
                    x_refs[p][...].astype(jnp.bfloat16),
                    (((0,), (0,)), ((), ())),
                    preferred_element_type=jnp.float32,
                )
                acc_ref[dests_ref[s]] += prod

    for p in range(peers):
        term_refs[p][...] = acc_ref[p].astype(jnp.bfloat16)


def tail_terms(slot_rows, dests, table, start, tiles, pieces, levels, share):
    peers = len(pieces)
    shape = pieces[0].shape
    outs = [jax.ShapeDtypeStruct(shape, jnp.bfloat16) for _ in range(peers)]
    outs.append(jax.ShapeDtypeStruct((levels, share, shape[1]), jnp.float32))
    result = pl.pallas_call(
        functools.partial(tail_kernel, levels, peers),
        out_shape=outs,
        in_specs=[SMEM] * 4 + [VMEM] * (1 + peers),
        out_specs=[VMEM] * (peers + 1),
        scratch_shapes=[pltpu.VMEM((peers,) + shape, jnp.float32)],
    )(slot_rows, dests, table, start, tiles, *pieces)
    return result[:peers], result[peers]


def last_kernel(forward_ref, inv_ref, *refs):
    term_refs = refs[:-1]
    out_ref = refs[-1]
    returned = term_refs[0][...].astype(jnp.float32)
    for ref in term_refs[1:]:
        returned = returned + ref[...].astype(jnp.float32)
    update = (forward_ref[...].astype(jnp.float32) - returned).astype(jnp.bfloat16)
    out_ref[0] = lax.dot_general(
        inv_ref[0], update, (((0,), (0,)), ((), ())), preferred_element_type=jnp.float32
    )


def last_solve(forward, inv, terms):
    return pl.pallas_call(
        last_kernel,
        out_shape=jax.ShapeDtypeStruct((1,) + forward.shape, jnp.float32),
        in_specs=[VMEM] * (2 + len(terms)),
        out_specs=VMEM,
    )(forward, inv, *terms)


def pair_index(t, u):
    return t * (t - 1) // 2 + u


def tile_table(levels):
    table = np.zeros((levels, levels - 1), np.int32)
    for c in range(levels):
        for j in range(levels - 1):
            table[c, j] = pair_index(c, j) if j < c else pair_index(j + 1, c)
    return table


def summed_chunks(x, peers, rows_n, me):
    chunks = x.reshape(peers, -1, x.shape[-1]).astype(jnp.bfloat16)
    bit = 1
    while bit < peers:
        pairs = chunks.reshape(-1, 2, *chunks.shape[1:])
        mine = (me // bit) % 2
        keep = lax.dynamic_index_in_dim(pairs, mine, 1, keepdims=False)
        give = lax.dynamic_index_in_dim(pairs, 1 - mine, 1, keepdims=False)
        got = swapped(give, "col", peers, bit)
        chunks = (keep.astype(jnp.float32) + got.astype(jnp.float32)).astype(jnp.bfloat16)
        bit *= 2
    part = chunks[0]
    bit = 1
    while bit < rows_n:
        got = swapped(part, "row", rows_n, bit)
        part = (part.astype(jnp.float32) + got.astype(jnp.float32)).astype(jnp.bfloat16)
        bit *= 2
    return part


def gathered_chunks(part, peers, me):
    pieces = [part] + [shifted(part, "col", peers, s) for s in range(1, peers)]
    stacked = jnp.stack(pieces)
    source = (me - jnp.arange(peers)) % peers
    return jnp.zeros_like(stacked).at[source].set(stacked)


def local(low_rhs, low_inv, low_tiles, tile_rows, tile_cols, top_rhs, top_inv, top_tiles):
    peers = lax.axis_size("col")
    rows_n = lax.axis_size("row")
    levels = top_rhs.shape[0]
    share = top_rhs.shape[1]
    width = top_rhs.shape[2]
    position = lax.axis_index("row")
    me = lax.axis_index("col")
    owned = jnp.minimum(me, levels - 1)

    picks = jnp.asarray(tile_table(levels))[owned]
    mine = jnp.concatenate(
        [lax.dynamic_index_in_dim(top_inv, owned, 0), jnp.take(top_tiles, picks, axis=0)], axis=0
    )
    mats = jnp.zeros((mine.shape[0], share * rows_n, mine.shape[2]), mine.dtype)
    for s in range(rows_n):
        piece = mine if s == 0 else shifted(mine, "row", rows_n, s)
        mats = lax.dynamic_update_slice_in_dim(mats, piece, ((position - s) % rows_n) * share, 1)
    inv = mats[0]

    slot_rows = tile_rows[0]
    slot_cols = tile_cols[0] % peers
    own_tiles = low_tiles[0]
    low_forward = jnp.dot(low_inv[0], low_rhs[0], preferred_element_type=jnp.float32).astype(
        jnp.bfloat16
    )
    received = [low_forward] + [shifted(low_forward, "col", peers, s) for s in range(1, peers)]
    source_of = (me - jnp.arange(peers)) % peers
    by_source = jnp.stack(received)
    slot_pick = jnp.argmax(source_of[None, :] == slot_cols[:, None], axis=1).astype(jnp.int32)
    fold = jnp.stack([position * share, me]).astype(jnp.int32)
    coupling = coupling_terms(slot_rows, slot_pick, fold, own_tiles, by_source, top_rhs, levels)
    part = summed_chunks(coupling, peers, rows_n, me)
    if peers == levels:
        level_sum = part
    else:
        level_sum = gathered_chunks(part, peers, me).reshape(levels, -1, width)[owned]
    rhs_level = -level_sum.astype(jnp.float32)

    top_forward = [None] * levels
    pushed = None
    for level in range(levels):
        residue = rhs_level
        if level > 0:
            pushed = lax.ppermute(pushed, "col", [(level - 1, level)])
            residue = residue - pushed[0]
        solved = jnp.dot(inv, residue.astype(jnp.bfloat16), preferred_element_type=jnp.float32)
        top_forward[level] = solved.astype(jnp.bfloat16)
        if level < levels - 1:
            later = jnp.einsum(
                "kab,bc->kac", mats[level + 1 : levels], top_forward[level], preferred_element_type=jnp.float32
            )
            pushed = later if level == 0 else pushed[1:] + later
    own_solution = None
    for level in reversed(range(levels)):
        update = top_forward[level].astype(jnp.float32)
        if level < levels - 1:
            pushed = lax.ppermute(pushed, "col", [(level + 1, level)])
            update = update - pushed[level]
        solved = lax.dot_general(
            inv, update.astype(jnp.bfloat16), (((0,), (0,)), ((), ())), preferred_element_type=jnp.float32
        )
        own_solution = solved if own_solution is None else jnp.where(me == level, solved, own_solution)
        if level > 0:
            earlier = jnp.einsum(
                "uab,ac->ubc", mats[1 : level + 1], solved.astype(jnp.bfloat16), preferred_element_type=jnp.float32
            )
            pushed = earlier if level == levels - 1 else pushed[:level] + earlier
    pieces = [own_solution] + [shifted(own_solution, "col", peers, s) for s in range(1, peers)]
    table = ((me - jnp.arange(levels)) % peers).astype(jnp.int32)
    dests = ((me - slot_cols) % peers).astype(jnp.int32)
    start = (position * share)[None].astype(jnp.int32)
    terms, top_rows = tail_terms(slot_rows, dests, table, start, own_tiles, pieces, levels, share)
    returned = [terms[0]] + [shifted(terms[s], "col", peers, peers - s) for s in range(1, peers)]
    low_solution = last_solve(low_forward, low_inv, returned)
    return (low_solution, top_rows)


def solution(mesh):
    in_specs = (
        P(("row", "col"), None, None),
        P(("row", "col"), None, None),
        P(("row", "col"), None, None, None),
        P(("row", "col"), None),
        P(("row", "col"), None),
        P(None, "row", None),
        P(None, "row", None),
        P(None, "row", None),
    )
    out_specs = (P(("row", "col"), None, None), P(None, "row", None))
    return jax.shard_map(local, mesh=mesh, in_specs=in_specs, out_specs=out_specs, check_vma=False)
```

```python
import functools

import jax
import jax.numpy as jnp
import numpy as np
from jax import lax
from jax.experimental import pallas as pl
from jax.experimental.pallas import tpu as pltpu
from jax.sharding import PartitionSpec as P

SMEM = pl.BlockSpec(memory_space=pltpu.SMEM)
VMEM = pl.BlockSpec(memory_space=pltpu.VMEM)


def coupling_kernel(rows_ref, picks_ref, fold_ref, tiles_ref, panels_ref, rhs_ref, out_ref, acc_ref):
    acc_ref[...] = jnp.zeros_like(acc_ref)
    share = rhs_ref.shape[1]

    @pl.when(fold_ref[1] == 0)
    def _():
        start = pl.multiple_of(fold_ref[0], 8)
        acc_ref[:, pl.ds(start, share), :] = -rhs_ref[...].astype(jnp.float32)

    for s in range(tiles_ref.shape[0]):
        level = rows_ref[s]

        @pl.when(level >= 0)
        def _():
            prod = jnp.dot(tiles_ref[s], panels_ref[picks_ref[s]], preferred_element_type=jnp.float32)
            acc_ref[level] += prod

    out_ref[...] = acc_ref[...].astype(out_ref.dtype)


def coupling_terms(slot_rows, picks, fold, tiles, panels, rhs, levels):
    shape = (levels, panels.shape[1], panels.shape[2])
    return pl.pallas_call(
        coupling_kernel,
        out_shape=jax.ShapeDtypeStruct(shape, jnp.bfloat16),
        in_specs=[SMEM, SMEM, SMEM, VMEM, VMEM, VMEM],
        out_specs=VMEM,
        scratch_shapes=[pltpu.VMEM(shape, jnp.float32)],
    )(slot_rows, picks, fold, tiles, panels, rhs)


def back_kernel(rows_ref, dests_ref, tiles_ref, back_ref, out_ref, acc_ref):
    acc_ref[...] = jnp.zeros_like(acc_ref)
    for s in range(tiles_ref.shape[0]):
        level = rows_ref[s]

        @pl.when(level >= 0)
        def _():
            prod = lax.dot_general(
                tiles_ref[s], back_ref[level], (((0,), (0,)), ((), ())), preferred_element_type=jnp.float32
            )
            acc_ref[dests_ref[s]] += prod

    out_ref[...] = acc_ref[...].astype(out_ref.dtype)


def back_terms(slot_rows, dests, tiles, back, peers):
    shape = (peers, tiles.shape[2], back.shape[2])
    return pl.pallas_call(
        back_kernel,
        out_shape=jax.ShapeDtypeStruct(shape, jnp.bfloat16),
        in_specs=[SMEM, SMEM, VMEM, VMEM],
        out_specs=VMEM,
        scratch_shapes=[pltpu.VMEM(shape, jnp.float32)],
    )(slot_rows, dests, tiles, back)


def shifted(x, axis, size, shift):
    return lax.ppermute(x, axis, [(i, (i + shift) % size) for i in range(size)])


def swapped(x, axis, size, bit):
    return lax.ppermute(x, axis, [(i, i ^ bit) for i in range(size)])


def broadcast_from(x, owner, me, axis, size):
    got = None
    for s in range(1, size):
        part = lax.ppermute(x, axis, [(owner, (owner + s) % size)])
        got = part if got is None else got + part
    return jnp.where(me == owner, x, got)


def tail_kernel(levels, peers, rows_ref, dests_ref, table_ref, start_ref, tiles_ref, *refs):
    x_refs = refs[:peers]
    term_refs = refs[peers : 2 * peers]
    slices_ref = refs[2 * peers]
    acc_ref = refs[2 * peers + 1]
    share = slices_ref.shape[1]
    start = pl.multiple_of(start_ref[0], 8)
    for t in range(levels):
        for p in range(peers):

            @pl.when(table_ref[t] == p)
            def _():
                slices_ref[t] = x_refs[p][pl.ds(start, share), :]

    acc_ref[...] = jnp.zeros_like(acc_ref)
    for s in range(tiles_ref.shape[0]):
        level = rows_ref[s]
        piece = table_ref[jnp.maximum(level, 0)]
        for p in range(peers):

            @pl.when((level >= 0) & (piece == p))
            def _():
                prod = lax.dot_general(
                    tiles_ref[s],
                    x_refs[p][...].astype(jnp.bfloat16),
                    (((0,), (0,)), ((), ())),
                    preferred_element_type=jnp.float32,
                )
                acc_ref[dests_ref[s]] += prod

    for p in range(peers):
        term_refs[p][...] = acc_ref[p].astype(jnp.bfloat16)


def tail_terms(slot_rows, dests, table, start, tiles, pieces, levels, share):
    peers = len(pieces)
    shape = pieces[0].shape
    outs = [jax.ShapeDtypeStruct(shape, jnp.bfloat16) for _ in range(peers)]
    outs.append(jax.ShapeDtypeStruct((levels, share, shape[1]), jnp.float32))
    result = pl.pallas_call(
        functools.partial(tail_kernel, levels, peers),
        out_shape=outs,
        in_specs=[SMEM] * 4 + [VMEM] * (1 + peers),
        out_specs=[VMEM] * (peers + 1),
        scratch_shapes=[pltpu.VMEM((peers,) + shape, jnp.float32)],
    )(slot_rows, dests, table, start, tiles, *pieces)
    return result[:peers], result[peers]


def last_kernel(forward_ref, inv_ref, *refs):
    term_refs = refs[:-1]
    out_ref = refs[-1]
    returned = term_refs[0][...].astype(jnp.float32)
    for ref in term_refs[1:]:
        returned = returned + ref[...].astype(jnp.float32)
    update = (forward_ref[...].astype(jnp.float32) - returned).astype(jnp.bfloat16)
    out_ref[0] = lax.dot_general(
        inv_ref[0], update, (((0,), (0,)), ((), ())), preferred_element_type=jnp.float32
    )


def last_solve(forward, inv, terms):
    return pl.pallas_call(
        last_kernel,
        out_shape=jax.ShapeDtypeStruct((1,) + forward.shape, jnp.float32),
        in_specs=[VMEM] * (2 + len(terms)),
        out_specs=VMEM,
    )(forward, inv, *terms)


def upper_kernel(levels, peers, rows_ref, dests_ref, table_ref, start_ref, tiles_ref, *refs):
    x_refs = refs[:peers]
    acc_ref = refs[peers]
    slices_ref = refs[peers + 1]
    share = slices_ref.shape[1]
    start = pl.multiple_of(start_ref[0], 8)
    for t in range(1, levels):
        for p in range(peers):

            @pl.when(table_ref[t] == p)
            def _():
                slices_ref[t] = x_refs[p][pl.ds(start, share), :]

    acc_ref[...] = jnp.zeros_like(acc_ref)
    for s in range(tiles_ref.shape[0]):
        level = rows_ref[s]
        piece = table_ref[jnp.maximum(level, 0)]
        for p in range(peers):

            @pl.when((level >= 1) & (piece == p))
            def _():
                prod = lax.dot_general(
                    tiles_ref[s],
                    x_refs[p][...].astype(jnp.bfloat16),
                    (((0,), (0,)), ((), ())),
                    preferred_element_type=jnp.float32,
                )
                acc_ref[dests_ref[s]] += prod


def upper_terms(slot_rows, dests, table, start, tiles, pieces, levels, share):
    peers = len(pieces)
    shape = pieces[0].shape
    outs = [
        jax.ShapeDtypeStruct((peers,) + shape, jnp.float32),
        jax.ShapeDtypeStruct((levels, share, shape[1]), jnp.float32),
    ]
    return pl.pallas_call(
        functools.partial(upper_kernel, levels, peers),
        out_shape=outs,
        in_specs=[SMEM] * 4 + [VMEM] * (1 + peers),
        out_specs=[VMEM, VMEM],
    )(slot_rows, dests, table, start, tiles, *pieces)


def first_kernel(peers, rows_ref, dests_ref, start_ref, tiles_ref, x_ref, upper_ref, rows_in_ref, *refs):
    term_refs = refs[:peers]
    slices_ref = refs[peers]
    acc_ref = refs[peers + 1]
    share = slices_ref.shape[1]
    start = pl.multiple_of(start_ref[0], 8)
    slices_ref[...] = rows_in_ref[...]
    slices_ref[0] = x_ref[pl.ds(start, share), :]
    acc_ref[...] = upper_ref[...]
    first = x_ref[...].astype(jnp.bfloat16)
    for s in range(tiles_ref.shape[0]):

        @pl.when(rows_ref[s] == 0)
        def _():
            prod = lax.dot_general(
                tiles_ref[s], first, (((0,), (0,)), ((), ())), preferred_element_type=jnp.float32
            )
            acc_ref[dests_ref[s]] += prod

    for p in range(peers):
        term_refs[p][...] = acc_ref[p].astype(jnp.bfloat16)


def first_terms(slot_rows, dests, start, tiles, first, upper, upper_rows):
    peers = upper.shape[0]
    outs = [jax.ShapeDtypeStruct(first.shape, jnp.bfloat16) for _ in range(peers)]
    outs.append(jax.ShapeDtypeStruct(upper_rows.shape, jnp.float32))
    result = pl.pallas_call(
        functools.partial(first_kernel, peers),
        out_shape=outs,
        in_specs=[SMEM] * 3 + [VMEM] * 4,
        out_specs=[VMEM] * (peers + 1),
        scratch_shapes=[pltpu.VMEM(upper.shape, jnp.float32)],
    )(slot_rows, dests, start, tiles, first, upper, upper_rows)
    return result[:peers], result[peers]


def pair_index(t, u):
    return t * (t - 1) // 2 + u


def tile_table(levels):
    table = np.zeros((levels, levels - 1), np.int32)
    for c in range(levels):
        for j in range(levels - 1):
            table[c, j] = pair_index(c, j) if j < c else pair_index(j + 1, c)
    return table


def summed_chunks(x, peers, rows_n, me):
    chunks = x.reshape(peers, -1, x.shape[-1]).astype(jnp.bfloat16)
    bit = 1
    while bit < peers:
        pairs = chunks.reshape(-1, 2, *chunks.shape[1:])
        mine = (me // bit) % 2
        keep = lax.dynamic_index_in_dim(pairs, mine, 1, keepdims=False)
        give = lax.dynamic_index_in_dim(pairs, 1 - mine, 1, keepdims=False)
        got = swapped(give, "col", peers, bit)
        chunks = (keep.astype(jnp.float32) + got.astype(jnp.float32)).astype(jnp.bfloat16)
        bit *= 2
    part = chunks[0]
    bit = 1
    while bit < rows_n:
        got = swapped(part, "row", rows_n, bit)
        part = (part.astype(jnp.float32) + got.astype(jnp.float32)).astype(jnp.bfloat16)
        bit *= 2
    return part


def gathered_chunks(part, peers, me):
    pieces = [part] + [shifted(part, "col", peers, s) for s in range(1, peers)]
    stacked = jnp.stack(pieces)
    source = (me - jnp.arange(peers)) % peers
    return jnp.zeros_like(stacked).at[source].set(stacked)


def local(low_rhs, low_inv, low_tiles, tile_rows, tile_cols, top_rhs, top_inv, top_tiles):
    peers = lax.axis_size("col")
    rows_n = lax.axis_size("row")
    levels = top_rhs.shape[0]
    share = top_rhs.shape[1]
    width = top_rhs.shape[2]
    position = lax.axis_index("row")
    me = lax.axis_index("col")
    owned = jnp.minimum(me, levels - 1)

    picks = jnp.asarray(tile_table(levels))[owned]
    mine = jnp.concatenate(
        [lax.dynamic_index_in_dim(top_inv, owned, 0), jnp.take(top_tiles, picks, axis=0)], axis=0
    )
    mats = lax.all_gather(mine, "row", axis=1, tiled=True)
    inv = mats[0]

    slot_rows = tile_rows[0]
    slot_cols = tile_cols[0] % peers
    own_tiles = low_tiles[0]
    low_forward = jnp.dot(low_inv[0], low_rhs[0], preferred_element_type=jnp.float32).astype(
        jnp.bfloat16
    )
    received = [low_forward] + [shifted(low_forward, "col", peers, s) for s in range(1, peers)]
    source_of = (me - jnp.arange(peers)) % peers
    by_source = jnp.stack(received)
    slot_pick = jnp.argmax(source_of[None, :] == slot_cols[:, None], axis=1).astype(jnp.int32)
    fold = jnp.stack([position * share, me]).astype(jnp.int32)
    coupling = coupling_terms(slot_rows, slot_pick, fold, own_tiles, by_source, top_rhs, levels)
    part = summed_chunks(coupling, peers, rows_n, me)
    if peers == levels:
        level_sum = part
    else:
        level_sum = gathered_chunks(part, peers, me).reshape(levels, -1, width)[owned]
    rhs_level = -level_sum.astype(jnp.float32)

    top_forward = [None] * levels
    pushed = None
    for level in range(levels):
        residue = rhs_level
        if level > 0:
            pushed = lax.ppermute(pushed, "col", [(level - 1, level)])
            residue = residue - pushed[0]
        solved = jnp.dot(inv, residue.astype(jnp.bfloat16), preferred_element_type=jnp.float32)
        top_forward[level] = solved.astype(jnp.bfloat16)
        if level < levels - 1:
            later = jnp.einsum(
                "kab,bc->kac", mats[level + 1 : levels], top_forward[level], preferred_element_type=jnp.float32
            )
            pushed = later if level == 0 else pushed[1:] + later
    own_solution = None
    table = ((me - jnp.arange(levels)) % peers).astype(jnp.int32)
    dests = ((me - slot_cols) % peers).astype(jnp.int32)
    start = (position * share)[None].astype(jnp.int32)
    for level in reversed(range(levels)):
        update = top_forward[level].astype(jnp.float32)
        if level < levels - 1:
            pushed = lax.ppermute(pushed, "col", [(level + 1, level)])
            update = update - pushed[level]
        solved = lax.dot_general(
            inv, update.astype(jnp.bfloat16), (((0,), (0,)), ((), ())), preferred_element_type=jnp.float32
        )
        own_solution = solved if own_solution is None else jnp.where(me == level, solved, own_solution)
        if level > 0:
            earlier = jnp.einsum(
                "uab,ac->ubc", mats[1 : level + 1], solved.astype(jnp.bfloat16), preferred_element_type=jnp.float32
            )
            pushed = earlier if level == levels - 1 else pushed[:level] + earlier
        if level == 1:
            pieces = [own_solution] + [shifted(own_solution, "col", peers, s) for s in range(1, peers)]
            upper, upper_rows = upper_terms(slot_rows, dests, table, start, own_tiles, pieces, levels, share)
    first = broadcast_from(solved, 0, me, "col", peers)
    terms, top_rows = first_terms(slot_rows, dests, start, own_tiles, first, upper, upper_rows)
    returned = [terms[0]] + [shifted(terms[s], "col", peers, peers - s) for s in range(1, peers)]
    low_solution = last_solve(low_forward, low_inv, returned)
    return (low_solution, top_rows)


def solution(mesh):
    in_specs = (
        P(("row", "col"), None, None),
        P(("row", "col"), None, None),
        P(("row", "col"), None, None, None),
        P(("row", "col"), None),
        P(("row", "col"), None),
        P(None, "row", None),
        P(None, "row", None),
        P(None, "row", None),
    )
    out_specs = (P(("row", "col"), None, None), P(None, "row", None))
    return jax.shard_map(local, mesh=mesh, in_specs=in_specs, out_specs=out_specs, check_vma=False)
```

```python
import functools

import jax
import jax.numpy as jnp
import numpy as np
from jax import lax
from jax.experimental import pallas as pl
from jax.experimental.pallas import tpu as pltpu
from jax.sharding import PartitionSpec as P

SMEM = pl.BlockSpec(memory_space=pltpu.SMEM)
VMEM = pl.BlockSpec(memory_space=pltpu.VMEM)


def coupling_kernel(rows_ref, picks_ref, fold_ref, tiles_ref, panels_ref, rhs_ref, out_ref, acc_ref):
    acc_ref[...] = jnp.zeros_like(acc_ref)
    share = rhs_ref.shape[1]

    @pl.when(fold_ref[1] == 0)
    def _():
        start = pl.multiple_of(fold_ref[0], 8)
        acc_ref[:, pl.ds(start, share), :] = -rhs_ref[...].astype(jnp.float32)

    for s in range(tiles_ref.shape[0]):
        level = rows_ref[s]

        @pl.when(level >= 0)
        def _():
            prod = jnp.dot(tiles_ref[s], panels_ref[picks_ref[s]], preferred_element_type=jnp.float32)
            acc_ref[level] += prod

    out_ref[...] = acc_ref[...].astype(out_ref.dtype)


def coupling_terms(slot_rows, picks, fold, tiles, panels, rhs, levels):
    shape = (levels, panels.shape[1], panels.shape[2])
    return pl.pallas_call(
        coupling_kernel,
        out_shape=jax.ShapeDtypeStruct(shape, jnp.bfloat16),
        in_specs=[SMEM, SMEM, SMEM, VMEM, VMEM, VMEM],
        out_specs=VMEM,
        scratch_shapes=[pltpu.VMEM(shape, jnp.float32)],
    )(slot_rows, picks, fold, tiles, panels, rhs)


def back_kernel(rows_ref, dests_ref, tiles_ref, back_ref, out_ref, acc_ref):
    acc_ref[...] = jnp.zeros_like(acc_ref)
    for s in range(tiles_ref.shape[0]):
        level = rows_ref[s]

        @pl.when(level >= 0)
        def _():
            prod = lax.dot_general(
                tiles_ref[s], back_ref[level], (((0,), (0,)), ((), ())), preferred_element_type=jnp.float32
            )
            acc_ref[dests_ref[s]] += prod

    out_ref[...] = acc_ref[...].astype(out_ref.dtype)


def back_terms(slot_rows, dests, tiles, back, peers):
    shape = (peers, tiles.shape[2], back.shape[2])
    return pl.pallas_call(
        back_kernel,
        out_shape=jax.ShapeDtypeStruct(shape, jnp.bfloat16),
        in_specs=[SMEM, SMEM, VMEM, VMEM],
        out_specs=VMEM,
        scratch_shapes=[pltpu.VMEM(shape, jnp.float32)],
    )(slot_rows, dests, tiles, back)


def shifted(x, axis, size, shift):
    return lax.ppermute(x, axis, [(i, (i + shift) % size) for i in range(size)])


def swapped(x, axis, size, bit):
    return lax.ppermute(x, axis, [(i, i ^ bit) for i in range(size)])


def broadcast_from(x, owner, me, axis, size):
    got = None
    for s in range(1, size):
        part = lax.ppermute(x, axis, [(owner, (owner + s) % size)])
        got = part if got is None else got + part
    return jnp.where(me == owner, x, got)


def tail_kernel(levels, peers, rows_ref, dests_ref, table_ref, start_ref, tiles_ref, *refs):
    x_refs = refs[:peers]
    term_refs = refs[peers : 2 * peers]
    slices_ref = refs[2 * peers]
    acc_ref = refs[2 * peers + 1]
    share = slices_ref.shape[1]
    start = pl.multiple_of(start_ref[0], 8)
    for t in range(levels):
        for p in range(peers):

            @pl.when(table_ref[t] == p)
            def _():
                slices_ref[t] = x_refs[p][pl.ds(start, share), :]

    acc_ref[...] = jnp.zeros_like(acc_ref)
    for s in range(tiles_ref.shape[0]):
        level = rows_ref[s]
        piece = table_ref[jnp.maximum(level, 0)]
        for p in range(peers):

            @pl.when((level >= 0) & (piece == p))
            def _():
                prod = lax.dot_general(
                    tiles_ref[s],
                    x_refs[p][...].astype(jnp.bfloat16),
                    (((0,), (0,)), ((), ())),
                    preferred_element_type=jnp.float32,
                )
                acc_ref[dests_ref[s]] += prod

    for p in range(peers):
        term_refs[p][...] = acc_ref[p].astype(jnp.bfloat16)


def tail_terms(slot_rows, dests, table, start, tiles, pieces, levels, share):
    peers = len(pieces)
    shape = pieces[0].shape
    outs = [jax.ShapeDtypeStruct(shape, jnp.bfloat16) for _ in range(peers)]
    outs.append(jax.ShapeDtypeStruct((levels, share, shape[1]), jnp.float32))
    result = pl.pallas_call(
        functools.partial(tail_kernel, levels, peers),
        out_shape=outs,
        in_specs=[SMEM] * 4 + [VMEM] * (1 + peers),
        out_specs=[VMEM] * (peers + 1),
        scratch_shapes=[pltpu.VMEM((peers,) + shape, jnp.float32)],
    )(slot_rows, dests, table, start, tiles, *pieces)
    return result[:peers], result[peers]


def last_kernel(forward_ref, inv_ref, *refs):
    term_refs = refs[:-1]
    out_ref = refs[-1]
    returned = term_refs[0][...].astype(jnp.float32)
    for ref in term_refs[1:]:
        returned = returned + ref[...].astype(jnp.float32)
    update = (forward_ref[...].astype(jnp.float32) - returned).astype(jnp.bfloat16)
    out_ref[0] = lax.dot_general(
        inv_ref[0], update, (((0,), (0,)), ((), ())), preferred_element_type=jnp.float32
    )


def last_solve(forward, inv, terms):
    return pl.pallas_call(
        last_kernel,
        out_shape=jax.ShapeDtypeStruct((1,) + forward.shape, jnp.float32),
        in_specs=[VMEM] * (2 + len(terms)),
        out_specs=VMEM,
    )(forward, inv, *terms)


def pair_index(t, u):
    return t * (t - 1) // 2 + u


def tile_table(levels):
    table = np.zeros((levels, levels - 1), np.int32)
    for c in range(levels):
        for j in range(levels - 1):
            table[c, j] = pair_index(c, j) if j < c else pair_index(j + 1, c)
    return table


def summed_chunks(x, peers, rows_n, me):
    chunks = x.reshape(peers, -1, x.shape[-1]).astype(jnp.bfloat16)
    bit = 1
    while bit < peers:
        pairs = chunks.reshape(-1, 2, *chunks.shape[1:])
        mine = (me // bit) % 2
        keep = lax.dynamic_index_in_dim(pairs, mine, 1, keepdims=False)
        give = lax.dynamic_index_in_dim(pairs, 1 - mine, 1, keepdims=False)
        got = swapped(give, "col", peers, bit)
        chunks = (keep.astype(jnp.float32) + got.astype(jnp.float32)).astype(jnp.bfloat16)
        bit *= 2
    part = chunks[0]
    bit = 1
    while bit < rows_n:
        got = swapped(part, "row", rows_n, bit)
        part = (part.astype(jnp.float32) + got.astype(jnp.float32)).astype(jnp.bfloat16)
        bit *= 2
    return part


def gathered_chunks(part, peers, me):
    pieces = [part] + [shifted(part, "col", peers, s) for s in range(1, peers)]
    stacked = jnp.stack(pieces)
    source = (me - jnp.arange(peers)) % peers
    return jnp.zeros_like(stacked).at[source].set(stacked)


def local(low_rhs, low_inv, low_tiles, tile_rows, tile_cols, top_rhs, top_inv, top_tiles):
    peers = lax.axis_size("col")
    rows_n = lax.axis_size("row")
    levels = top_rhs.shape[0]
    share = top_rhs.shape[1]
    width = top_rhs.shape[2]
    position = lax.axis_index("row")
    me = lax.axis_index("col")
    owned = jnp.minimum(me, levels - 1)

    pieces = [lax.dynamic_slice_in_dim(top_inv, owned, 1, 0)]
    for j in range(levels - 1):
        index = jnp.where(j < owned, owned * (owned - 1) // 2 + j, (j + 1) * j // 2 + owned)
        pieces.append(lax.dynamic_slice_in_dim(top_tiles, index, 1, 0))
    mine = jnp.concatenate(pieces, axis=0)
    mats = lax.all_gather(mine, "row", axis=1, tiled=True)
    inv = mats[0]

    slot_rows = tile_rows[0]
    slot_cols = tile_cols[0] % peers
    own_tiles = low_tiles[0]
    low_forward = jnp.dot(low_inv[0], low_rhs[0], preferred_element_type=jnp.float32).astype(
        jnp.bfloat16
    )
    received = [low_forward] + [shifted(low_forward, "col", peers, s) for s in range(1, peers)]
    source_of = (me - jnp.arange(peers)) % peers
    by_source = jnp.stack(received)
    slot_pick = jnp.argmax(source_of[None, :] == slot_cols[:, None], axis=1).astype(jnp.int32)
    fold = jnp.stack([position * share, me]).astype(jnp.int32)
    coupling = coupling_terms(slot_rows, slot_pick, fold, own_tiles, by_source, top_rhs, levels)
    part = summed_chunks(coupling, peers, rows_n, me)
    if peers == levels:
        level_sum = part
    else:
        level_sum = gathered_chunks(part, peers, me).reshape(levels, -1, width)[owned]
    rhs_level = -level_sum.astype(jnp.float32)

    top_forward = [None] * levels
    pushed = None
    for level in range(levels):
        residue = rhs_level
        if level > 0:
            pushed = lax.ppermute(pushed, "col", [(level - 1, level)])
            residue = residue - pushed[0]
        solved = jnp.dot(inv, residue.astype(jnp.bfloat16), preferred_element_type=jnp.float32)
        top_forward[level] = solved.astype(jnp.bfloat16)
        if level < levels - 1:
            later = jnp.einsum(
                "kab,bc->kac", mats[level + 1 : levels], top_forward[level], preferred_element_type=jnp.float32
            )
            pushed = later if level == 0 else pushed[1:] + later
    own_solution = None
    for level in reversed(range(levels)):
        update = top_forward[level].astype(jnp.float32)
        if level < levels - 1:
            pushed = lax.ppermute(pushed, "col", [(level + 1, level)])
            update = update - pushed[level]
        solved = lax.dot_general(
            inv, update.astype(jnp.bfloat16), (((0,), (0,)), ((), ())), preferred_element_type=jnp.float32
        )
        own_solution = solved if own_solution is None else jnp.where(me == level, solved, own_solution)
        if level > 0:
            earlier = jnp.einsum(
                "uab,ac->ubc", mats[1 : level + 1], solved.astype(jnp.bfloat16), preferred_element_type=jnp.float32
            )
            pushed = earlier if level == levels - 1 else pushed[:level] + earlier
    pieces = [own_solution] + [shifted(own_solution, "col", peers, s) for s in range(1, peers)]
    table = ((me - jnp.arange(levels)) % peers).astype(jnp.int32)
    dests = ((me - slot_cols) % peers).astype(jnp.int32)
    start = (position * share)[None].astype(jnp.int32)
    terms, top_rows = tail_terms(slot_rows, dests, table, start, own_tiles, pieces, levels, share)
    returned = [terms[0]] + [shifted(terms[s], "col", peers, peers - s) for s in range(1, peers)]
    low_solution = last_solve(low_forward, low_inv, returned)
    return (low_solution, top_rows)


def solution(mesh):
    in_specs = (
        P(("row", "col"), None, None),
        P(("row", "col"), None, None),
        P(("row", "col"), None, None, None),
        P(("row", "col"), None),
        P(("row", "col"), None),
        P(None, "row", None),
        P(None, "row", None),
        P(None, "row", None),
    )
    out_specs = (P(("row", "col"), None, None), P(None, "row", None))
    return jax.shard_map(local, mesh=mesh, in_specs=in_specs, out_specs=out_specs, check_vma=False)
```

```python
import functools

import jax
import jax.numpy as jnp
import numpy as np
from jax import lax
from jax.experimental import pallas as pl
from jax.experimental.pallas import tpu as pltpu
from jax.sharding import PartitionSpec as P

SMEM = pl.BlockSpec(memory_space=pltpu.SMEM)
VMEM = pl.BlockSpec(memory_space=pltpu.VMEM)


def coupling_kernel(rows_ref, picks_ref, fold_ref, tiles_ref, panels_ref, rhs_ref, out_ref, acc_ref):
    acc_ref[...] = jnp.zeros_like(acc_ref)
    share = rhs_ref.shape[1]

    @pl.when(fold_ref[1] == 0)
    def _():
        start = pl.multiple_of(fold_ref[0], 8)
        acc_ref[:, pl.ds(start, share), :] = -rhs_ref[...].astype(jnp.float32)

    for s in range(tiles_ref.shape[0]):
        level = rows_ref[s]

        @pl.when(level >= 0)
        def _():
            prod = jnp.dot(tiles_ref[s], panels_ref[picks_ref[s]], preferred_element_type=jnp.float32)
            acc_ref[level] += prod

    out_ref[...] = acc_ref[...].astype(out_ref.dtype)


def coupling_terms(slot_rows, picks, fold, tiles, panels, rhs, levels):
    shape = (levels, panels.shape[1], panels.shape[2])
    return pl.pallas_call(
        coupling_kernel,
        out_shape=jax.ShapeDtypeStruct(shape, jnp.bfloat16),
        in_specs=[SMEM, SMEM, SMEM, VMEM, VMEM, VMEM],
        out_specs=VMEM,
        scratch_shapes=[pltpu.VMEM(shape, jnp.float32)],
    )(slot_rows, picks, fold, tiles, panels, rhs)


def back_kernel(rows_ref, dests_ref, tiles_ref, back_ref, out_ref, acc_ref):
    acc_ref[...] = jnp.zeros_like(acc_ref)
    for s in range(tiles_ref.shape[0]):
        level = rows_ref[s]

        @pl.when(level >= 0)
        def _():
            prod = lax.dot_general(
                tiles_ref[s], back_ref[level], (((0,), (0,)), ((), ())), preferred_element_type=jnp.float32
            )
            acc_ref[dests_ref[s]] += prod

    out_ref[...] = acc_ref[...].astype(out_ref.dtype)


def back_terms(slot_rows, dests, tiles, back, peers):
    shape = (peers, tiles.shape[2], back.shape[2])
    return pl.pallas_call(
        back_kernel,
        out_shape=jax.ShapeDtypeStruct(shape, jnp.bfloat16),
        in_specs=[SMEM, SMEM, VMEM, VMEM],
        out_specs=VMEM,
        scratch_shapes=[pltpu.VMEM(shape, jnp.float32)],
    )(slot_rows, dests, tiles, back)


def shifted(x, axis, size, shift):
    return lax.ppermute(x, axis, [(i, (i + shift) % size) for i in range(size)])


def swapped(x, axis, size, bit):
    return lax.ppermute(x, axis, [(i, i ^ bit) for i in range(size)])


def broadcast_from(x, owner, me, axis, size):
    got = None
    for s in range(1, size):
        part = lax.ppermute(x, axis, [(owner, (owner + s) % size)])
        got = part if got is None else got + part
    return jnp.where(me == owner, x, got)


def tail_kernel(levels, peers, rows_ref, dests_ref, table_ref, start_ref, tiles_ref, *refs):
    x_refs = refs[:peers]
    term_refs = refs[peers : 2 * peers]
    slices_ref = refs[2 * peers]
    acc_ref = refs[2 * peers + 1]
    share = slices_ref.shape[1]
    start = pl.multiple_of(start_ref[0], 8)
    for t in range(levels):
        for p in range(peers):

            @pl.when(table_ref[t] == p)
            def _():
                slices_ref[t] = x_refs[p][pl.ds(start, share), :]

    acc_ref[...] = jnp.zeros_like(acc_ref)
    for s in range(tiles_ref.shape[0]):
        level = rows_ref[s]
        piece = table_ref[jnp.maximum(level, 0)]
        for p in range(peers):

            @pl.when((level >= 0) & (piece == p))
            def _():
                prod = lax.dot_general(
                    tiles_ref[s],
                    x_refs[p][...].astype(jnp.bfloat16),
                    (((0,), (0,)), ((), ())),
                    preferred_element_type=jnp.float32,
                )
                acc_ref[dests_ref[s]] += prod

    for p in range(peers):
        term_refs[p][...] = acc_ref[p].astype(jnp.bfloat16)


def tail_terms(slot_rows, dests, table, start, tiles, pieces, levels, share):
    peers = len(pieces)
    shape = pieces[0].shape
    outs = [jax.ShapeDtypeStruct(shape, jnp.bfloat16) for _ in range(peers)]
    outs.append(jax.ShapeDtypeStruct((levels, share, shape[1]), jnp.float32))
    result = pl.pallas_call(
        functools.partial(tail_kernel, levels, peers),
        out_shape=outs,
        in_specs=[SMEM] * 4 + [VMEM] * (1 + peers),
        out_specs=[VMEM] * (peers + 1),
        scratch_shapes=[pltpu.VMEM((peers,) + shape, jnp.float32)],
    )(slot_rows, dests, table, start, tiles, *pieces)
    return result[:peers], result[peers]


def last_kernel(forward_ref, inv_ref, *refs):
    term_refs = refs[:-1]
    out_ref = refs[-1]
    returned = term_refs[0][...].astype(jnp.float32)
    for ref in term_refs[1:]:
        returned = returned + ref[...].astype(jnp.float32)
    update = (forward_ref[...].astype(jnp.float32) - returned).astype(jnp.bfloat16)
    out_ref[0] = lax.dot_general(
        inv_ref[0], update, (((0,), (0,)), ((), ())), preferred_element_type=jnp.float32
    )


def last_solve(forward, inv, terms):
    return pl.pallas_call(
        last_kernel,
        out_shape=jax.ShapeDtypeStruct((1,) + forward.shape, jnp.float32),
        in_specs=[VMEM] * (2 + len(terms)),
        out_specs=VMEM,
    )(forward, inv, *terms)


def hop(x, source, target):
    if source // 2 == target // 2:
        return lax.ppermute(x, "col", [(source, target)])
    sent = lax.ppermute(x.astype(jnp.bfloat16), "col", [(source, target)])
    return sent.astype(jnp.float32)


def pair_index(t, u):
    return t * (t - 1) // 2 + u


def tile_table(levels):
    table = np.zeros((levels, levels - 1), np.int32)
    for c in range(levels):
        for j in range(levels - 1):
            table[c, j] = pair_index(c, j) if j < c else pair_index(j + 1, c)
    return table


def summed_chunks(x, peers, rows_n, me):
    chunks = x.reshape(peers, -1, x.shape[-1]).astype(jnp.bfloat16)
    bit = 1
    while bit < peers:
        pairs = chunks.reshape(-1, 2, *chunks.shape[1:])
        mine = (me // bit) % 2
        keep = lax.dynamic_index_in_dim(pairs, mine, 1, keepdims=False)
        give = lax.dynamic_index_in_dim(pairs, 1 - mine, 1, keepdims=False)
        got = swapped(give, "col", peers, bit)
        chunks = (keep.astype(jnp.float32) + got.astype(jnp.float32)).astype(jnp.bfloat16)
        bit *= 2
    part = chunks[0]
    bit = 1
    while bit < rows_n:
        got = swapped(part, "row", rows_n, bit)
        part = (part.astype(jnp.float32) + got.astype(jnp.float32)).astype(jnp.bfloat16)
        bit *= 2
    return part


def gathered_chunks(part, peers, me):
    pieces = [part] + [shifted(part, "col", peers, s) for s in range(1, peers)]
    stacked = jnp.stack(pieces)
    source = (me - jnp.arange(peers)) % peers
    return jnp.zeros_like(stacked).at[source].set(stacked)


def local(low_rhs, low_inv, low_tiles, tile_rows, tile_cols, top_rhs, top_inv, top_tiles):
    peers = lax.axis_size("col")
    rows_n = lax.axis_size("row")
    levels = top_rhs.shape[0]
    share = top_rhs.shape[1]
    width = top_rhs.shape[2]
    position = lax.axis_index("row")
    me = lax.axis_index("col")
    owned = jnp.minimum(me, levels - 1)

    pieces = [lax.dynamic_slice_in_dim(top_inv, owned, 1, 0)]
    for j in range(levels - 1):
        index = jnp.where(j < owned, owned * (owned - 1) // 2 + j, (j + 1) * j // 2 + owned)
        pieces.append(lax.dynamic_slice_in_dim(top_tiles, index, 1, 0))
    mine = jnp.concatenate(pieces, axis=0)
    mats = lax.all_gather(mine, "row", axis=1, tiled=True)
    inv = mats[0]

    slot_rows = tile_rows[0]
    slot_cols = tile_cols[0] % peers
    own_tiles = low_tiles[0]
    low_forward = jnp.dot(low_inv[0], low_rhs[0], preferred_element_type=jnp.float32).astype(
        jnp.bfloat16
    )
    received = [low_forward] + [shifted(low_forward, "col", peers, s) for s in range(1, peers)]
    source_of = (me - jnp.arange(peers)) % peers
    by_source = jnp.stack(received)
    slot_pick = jnp.argmax(source_of[None, :] == slot_cols[:, None], axis=1).astype(jnp.int32)
    fold = jnp.stack([position * share, me]).astype(jnp.int32)
    coupling = coupling_terms(slot_rows, slot_pick, fold, own_tiles, by_source, top_rhs, levels)
    part = summed_chunks(coupling, peers, rows_n, me)
    if peers == levels:
        level_sum = part
    else:
        level_sum = gathered_chunks(part, peers, me).reshape(levels, -1, width)[owned]
    rhs_level = -level_sum.astype(jnp.float32)

    top_forward = [None] * levels
    pushed = None
    for level in range(levels):
        residue = rhs_level
        if level > 0:
            pushed = hop(pushed, level - 1, level)
            residue = residue - pushed[0]
        solved = jnp.dot(inv, residue.astype(jnp.bfloat16), preferred_element_type=jnp.float32)
        top_forward[level] = solved.astype(jnp.bfloat16)
        if level < levels - 1:
            later = jnp.einsum(
                "kab,bc->kac", mats[level + 1 : levels], top_forward[level], preferred_element_type=jnp.float32
            )
            pushed = later if level == 0 else pushed[1:] + later
    own_solution = None
    for level in reversed(range(levels)):
        update = top_forward[level].astype(jnp.float32)
        if level < levels - 1:
            pushed = hop(pushed, level + 1, level)
            update = update - pushed[level]
        solved = lax.dot_general(
            inv, update.astype(jnp.bfloat16), (((0,), (0,)), ((), ())), preferred_element_type=jnp.float32
        )
        own_solution = solved if own_solution is None else jnp.where(me == level, solved, own_solution)
        if level > 0:
            earlier = jnp.einsum(
                "uab,ac->ubc", mats[1 : level + 1], solved.astype(jnp.bfloat16), preferred_element_type=jnp.float32
            )
            pushed = earlier if level == levels - 1 else pushed[:level] + earlier
    pieces = [own_solution] + [shifted(own_solution, "col", peers, s) for s in range(1, peers)]
    table = ((me - jnp.arange(levels)) % peers).astype(jnp.int32)
    dests = ((me - slot_cols) % peers).astype(jnp.int32)
    start = (position * share)[None].astype(jnp.int32)
    terms, top_rows = tail_terms(slot_rows, dests, table, start, own_tiles, pieces, levels, share)
    returned = [terms[0]] + [shifted(terms[s], "col", peers, peers - s) for s in range(1, peers)]
    low_solution = last_solve(low_forward, low_inv, returned)
    return (low_solution, top_rows)


def solution(mesh):
    in_specs = (
        P(("row", "col"), None, None),
        P(("row", "col"), None, None),
        P(("row", "col"), None, None, None),
        P(("row", "col"), None),
        P(("row", "col"), None),
        P(None, "row", None),
        P(None, "row", None),
        P(None, "row", None),
    )
    out_specs = (P(("row", "col"), None, None), P(None, "row", None))
    return jax.shard_map(local, mesh=mesh, in_specs=in_specs, out_specs=out_specs, check_vma=False)
```

```python
import functools

import jax
import jax.numpy as jnp
import numpy as np
from jax import lax
from jax.experimental import pallas as pl
from jax.experimental.pallas import tpu as pltpu
from jax.sharding import PartitionSpec as P

SMEM = pl.BlockSpec(memory_space=pltpu.SMEM)
VMEM = pl.BlockSpec(memory_space=pltpu.VMEM)


def coupling_kernel(rows_ref, picks_ref, fold_ref, tiles_ref, panels_ref, rhs_ref, out_ref, acc_ref):
    acc_ref[...] = jnp.zeros_like(acc_ref)
    share = rhs_ref.shape[1]

    @pl.when(fold_ref[1] == 0)
    def _():
        start = pl.multiple_of(fold_ref[0], 8)
        acc_ref[:, pl.ds(start, share), :] = -rhs_ref[...].astype(jnp.float32)

    for s in range(tiles_ref.shape[0]):
        level = rows_ref[s]

        @pl.when(level >= 0)
        def _():
            prod = jnp.dot(tiles_ref[s], panels_ref[picks_ref[s]], preferred_element_type=jnp.float32)
            acc_ref[level] += prod

    out_ref[...] = acc_ref[...].astype(out_ref.dtype)


def coupling_terms(slot_rows, picks, fold, tiles, panels, rhs, levels):
    shape = (levels, panels.shape[1], panels.shape[2])
    return pl.pallas_call(
        coupling_kernel,
        out_shape=jax.ShapeDtypeStruct(shape, jnp.bfloat16),
        in_specs=[SMEM, SMEM, SMEM, VMEM, VMEM, VMEM],
        out_specs=VMEM,
        scratch_shapes=[pltpu.VMEM(shape, jnp.float32)],
    )(slot_rows, picks, fold, tiles, panels, rhs)


def back_kernel(rows_ref, dests_ref, tiles_ref, back_ref, out_ref, acc_ref):
    acc_ref[...] = jnp.zeros_like(acc_ref)
    for s in range(tiles_ref.shape[0]):
        level = rows_ref[s]

        @pl.when(level >= 0)
        def _():
            prod = lax.dot_general(
                tiles_ref[s], back_ref[level], (((0,), (0,)), ((), ())), preferred_element_type=jnp.float32
            )
            acc_ref[dests_ref[s]] += prod

    out_ref[...] = acc_ref[...].astype(out_ref.dtype)


def back_terms(slot_rows, dests, tiles, back, peers):
    shape = (peers, tiles.shape[2], back.shape[2])
    return pl.pallas_call(
        back_kernel,
        out_shape=jax.ShapeDtypeStruct(shape, jnp.bfloat16),
        in_specs=[SMEM, SMEM, VMEM, VMEM],
        out_specs=VMEM,
        scratch_shapes=[pltpu.VMEM(shape, jnp.float32)],
    )(slot_rows, dests, tiles, back)


def shifted(x, axis, size, shift):
    return lax.ppermute(x, axis, [(i, (i + shift) % size) for i in range(size)])


def swapped(x, axis, size, bit):
    return lax.ppermute(x, axis, [(i, i ^ bit) for i in range(size)])


def broadcast_from(x, owner, me, axis, size):
    got = None
    for s in range(1, size):
        part = lax.ppermute(x, axis, [(owner, (owner + s) % size)])
        got = part if got is None else got + part
    return jnp.where(me == owner, x, got)


def tail_kernel(levels, peers, rows_ref, dests_ref, table_ref, start_ref, tiles_ref, *refs):
    x_refs = refs[:peers]
    term_refs = refs[peers : 2 * peers]
    slices_ref = refs[2 * peers]
    acc_ref = refs[2 * peers + 1]
    share = slices_ref.shape[1]
    start = pl.multiple_of(start_ref[0], 8)
    for t in range(levels):
        for p in range(peers):

            @pl.when(table_ref[t] == p)
            def _():
                bulk = x_refs[p].shape[0] - share
                high = x_refs[p][pl.ds(start, share), :].astype(jnp.float32)
                slices_ref[t] = high + x_refs[p][pl.ds(bulk, share), :].astype(jnp.float32)

    acc_ref[...] = jnp.zeros_like(acc_ref)
    for s in range(tiles_ref.shape[0]):
        level = rows_ref[s]
        piece = table_ref[jnp.maximum(level, 0)]
        for p in range(peers):

            @pl.when((level >= 0) & (piece == p))
            def _():
                prod = lax.dot_general(
                    tiles_ref[s],
                    x_refs[p][pl.ds(0, tiles_ref.shape[2]), :],
                    (((0,), (0,)), ((), ())),
                    preferred_element_type=jnp.float32,
                )
                acc_ref[dests_ref[s]] += prod

    for p in range(peers):
        term_refs[p][...] = acc_ref[p].astype(jnp.bfloat16)


def tail_terms(slot_rows, dests, table, start, tiles, pieces, levels, share):
    peers = len(pieces)
    shape = (tiles.shape[2], pieces[0].shape[1])
    outs = [jax.ShapeDtypeStruct(shape, jnp.bfloat16) for _ in range(peers)]
    outs.append(jax.ShapeDtypeStruct((levels, share, shape[1]), jnp.float32))
    result = pl.pallas_call(
        functools.partial(tail_kernel, levels, peers),
        out_shape=outs,
        in_specs=[SMEM] * 4 + [VMEM] * (1 + peers),
        out_specs=[VMEM] * (peers + 1),
        scratch_shapes=[pltpu.VMEM((peers,) + shape, jnp.float32)],
    )(slot_rows, dests, table, start, tiles, *pieces)
    return result[:peers], result[peers]


def last_kernel(forward_ref, inv_ref, *refs):
    term_refs = refs[:-1]
    out_ref = refs[-1]
    returned = term_refs[0][...].astype(jnp.float32)
    for ref in term_refs[1:]:
        returned = returned + ref[...].astype(jnp.float32)
    update = (forward_ref[...].astype(jnp.float32) - returned).astype(jnp.bfloat16)
    out_ref[0] = lax.dot_general(
        inv_ref[0], update, (((0,), (0,)), ((), ())), preferred_element_type=jnp.float32
    )


def last_solve(forward, inv, terms):
    return pl.pallas_call(
        last_kernel,
        out_shape=jax.ShapeDtypeStruct((1,) + forward.shape, jnp.float32),
        in_specs=[VMEM] * (2 + len(terms)),
        out_specs=VMEM,
    )(forward, inv, *terms)


def hop(x, source, target):
    if source // 2 == target // 2:
        return lax.ppermute(x, "col", [(source, target)])
    sent = lax.ppermute(x.astype(jnp.bfloat16), "col", [(source, target)])
    return sent.astype(jnp.float32)


def pair_index(t, u):
    return t * (t - 1) // 2 + u


def tile_table(levels):
    table = np.zeros((levels, levels - 1), np.int32)
    for c in range(levels):
        for j in range(levels - 1):
            table[c, j] = pair_index(c, j) if j < c else pair_index(j + 1, c)
    return table


def summed_chunks(x, peers, rows_n, me):
    chunks = x.reshape(peers, -1, x.shape[-1]).astype(jnp.bfloat16)
    bit = 1
    while bit < peers:
        pairs = chunks.reshape(-1, 2, *chunks.shape[1:])
        mine = (me // bit) % 2
        keep = lax.dynamic_index_in_dim(pairs, mine, 1, keepdims=False)
        give = lax.dynamic_index_in_dim(pairs, 1 - mine, 1, keepdims=False)
        got = swapped(give, "col", peers, bit)
        chunks = (keep.astype(jnp.float32) + got.astype(jnp.float32)).astype(jnp.bfloat16)
        bit *= 2
    part = chunks[0]
    bit = 1
    while bit < rows_n:
        got = swapped(part, "row", rows_n, bit)
        part = (part.astype(jnp.float32) + got.astype(jnp.float32)).astype(jnp.bfloat16)
        bit *= 2
    return part


def gathered_chunks(part, peers, me):
    pieces = [part] + [shifted(part, "col", peers, s) for s in range(1, peers)]
    stacked = jnp.stack(pieces)
    source = (me - jnp.arange(peers)) % peers
    return jnp.zeros_like(stacked).at[source].set(stacked)


def local(low_rhs, low_inv, low_tiles, tile_rows, tile_cols, top_rhs, top_inv, top_tiles):
    peers = lax.axis_size("col")
    rows_n = lax.axis_size("row")
    levels = top_rhs.shape[0]
    share = top_rhs.shape[1]
    width = top_rhs.shape[2]
    position = lax.axis_index("row")
    me = lax.axis_index("col")
    owned = jnp.minimum(me, levels - 1)

    pieces = [lax.dynamic_slice_in_dim(top_inv, owned, 1, 0)]
    for j in range(levels - 1):
        index = jnp.where(j < owned, owned * (owned - 1) // 2 + j, (j + 1) * j // 2 + owned)
        pieces.append(lax.dynamic_slice_in_dim(top_tiles, index, 1, 0))
    mine = jnp.concatenate(pieces, axis=0)
    mats = lax.all_gather(mine, "row", axis=1, tiled=True)
    inv = mats[0]

    slot_rows = tile_rows[0]
    slot_cols = tile_cols[0] % peers
    own_tiles = low_tiles[0]
    low_forward = jnp.dot(low_inv[0], low_rhs[0], preferred_element_type=jnp.float32).astype(
        jnp.bfloat16
    )
    received = [low_forward] + [shifted(low_forward, "col", peers, s) for s in range(1, peers)]
    source_of = (me - jnp.arange(peers)) % peers
    by_source = jnp.stack(received)
    slot_pick = jnp.argmax(source_of[None, :] == slot_cols[:, None], axis=1).astype(jnp.int32)
    fold = jnp.stack([position * share, me]).astype(jnp.int32)
    coupling = coupling_terms(slot_rows, slot_pick, fold, own_tiles, by_source, top_rhs, levels)
    part = summed_chunks(coupling, peers, rows_n, me)
    if peers == levels:
        level_sum = part
    else:
        level_sum = gathered_chunks(part, peers, me).reshape(levels, -1, width)[owned]
    rhs_level = -level_sum.astype(jnp.float32)

    top_forward = [None] * levels
    pushed = None
    for level in range(levels):
        residue = rhs_level
        if level > 0:
            pushed = hop(pushed, level - 1, level)
            residue = residue - pushed[0]
        solved = jnp.dot(inv, residue.astype(jnp.bfloat16), preferred_element_type=jnp.float32)
        top_forward[level] = solved.astype(jnp.bfloat16)
        if level < levels - 1:
            later = jnp.einsum(
                "kab,bc->kac", mats[level + 1 : levels], top_forward[level], preferred_element_type=jnp.float32
            )
            pushed = later if level == 0 else pushed[1:] + later
    own_solution = None
    for level in reversed(range(levels)):
        update = top_forward[level].astype(jnp.float32)
        if level < levels - 1:
            pushed = hop(pushed, level + 1, level)
            update = update - pushed[level]
        solved = lax.dot_general(
            inv, update.astype(jnp.bfloat16), (((0,), (0,)), ((), ())), preferred_element_type=jnp.float32
        )
        own_solution = solved if own_solution is None else jnp.where(me == level, solved, own_solution)
        if level > 0:
            earlier = jnp.einsum(
                "uab,ac->ubc", mats[1 : level + 1], solved.astype(jnp.bfloat16), preferred_element_type=jnp.float32
            )
            pushed = earlier if level == levels - 1 else pushed[:level] + earlier
    high = own_solution.astype(jnp.bfloat16)
    rows_here = lax.dynamic_slice_in_dim(own_solution - high.astype(jnp.float32), position * share, share, 0)
    packed = jnp.concatenate([high, rows_here.astype(jnp.bfloat16)], axis=0)
    pieces = [packed] + [shifted(packed, "col", peers, s) for s in range(1, peers)]
    table = ((me - jnp.arange(levels)) % peers).astype(jnp.int32)
    dests = ((me - slot_cols) % peers).astype(jnp.int32)
    start = (position * share)[None].astype(jnp.int32)
    terms, top_rows = tail_terms(slot_rows, dests, table, start, own_tiles, pieces, levels, share)
    returned = [terms[0]] + [shifted(terms[s], "col", peers, peers - s) for s in range(1, peers)]
    low_solution = last_solve(low_forward, low_inv, returned)
    return (low_solution, top_rows)


def solution(mesh):
    in_specs = (
        P(("row", "col"), None, None),
        P(("row", "col"), None, None),
        P(("row", "col"), None, None, None),
        P(("row", "col"), None),
        P(("row", "col"), None),
        P(None, "row", None),
        P(None, "row", None),
        P(None, "row", None),
    )
    out_specs = (P(("row", "col"), None, None), P(None, "row", None))
    return jax.shard_map(local, mesh=mesh, in_specs=in_specs, out_specs=out_specs, check_vma=False)
```

```python
import functools

import jax
import jax.numpy as jnp
import numpy as np
from jax import lax
from jax.experimental import pallas as pl
from jax.experimental.pallas import tpu as pltpu
from jax.sharding import PartitionSpec as P

SMEM = pl.BlockSpec(memory_space=pltpu.SMEM)
VMEM = pl.BlockSpec(memory_space=pltpu.VMEM)


def coupling_kernel(rows_ref, picks_ref, fold_ref, tiles_ref, panels_ref, rhs_ref, out_ref, acc_ref):
    acc_ref[...] = jnp.zeros_like(acc_ref)
    share = rhs_ref.shape[1]

    @pl.when(fold_ref[1] == 0)
    def _():
        start = pl.multiple_of(fold_ref[0], 8)
        acc_ref[:, pl.ds(start, share), :] = -rhs_ref[...].astype(jnp.float32)

    for s in range(tiles_ref.shape[0]):
        level = rows_ref[s]

        @pl.when(level >= 0)
        def _():
            prod = jnp.dot(tiles_ref[s], panels_ref[picks_ref[s]], preferred_element_type=jnp.float32)
            acc_ref[level] += prod

    out_ref[...] = acc_ref[...].astype(out_ref.dtype)


def coupling_terms(slot_rows, picks, fold, tiles, panels, rhs, levels):
    shape = (levels, panels.shape[1], panels.shape[2])
    return pl.pallas_call(
        coupling_kernel,
        out_shape=jax.ShapeDtypeStruct(shape, jnp.bfloat16),
        in_specs=[SMEM, SMEM, SMEM, VMEM, VMEM, VMEM],
        out_specs=VMEM,
        scratch_shapes=[pltpu.VMEM(shape, jnp.float32)],
    )(slot_rows, picks, fold, tiles, panels, rhs)


def back_kernel(rows_ref, dests_ref, tiles_ref, back_ref, out_ref, acc_ref):
    acc_ref[...] = jnp.zeros_like(acc_ref)
    for s in range(tiles_ref.shape[0]):
        level = rows_ref[s]

        @pl.when(level >= 0)
        def _():
            prod = lax.dot_general(
                tiles_ref[s], back_ref[level], (((0,), (0,)), ((), ())), preferred_element_type=jnp.float32
            )
            acc_ref[dests_ref[s]] += prod

    out_ref[...] = acc_ref[...].astype(out_ref.dtype)


def back_terms(slot_rows, dests, tiles, back, peers):
    shape = (peers, tiles.shape[2], back.shape[2])
    return pl.pallas_call(
        back_kernel,
        out_shape=jax.ShapeDtypeStruct(shape, jnp.bfloat16),
        in_specs=[SMEM, SMEM, VMEM, VMEM],
        out_specs=VMEM,
        scratch_shapes=[pltpu.VMEM(shape, jnp.float32)],
    )(slot_rows, dests, tiles, back)


def shifted(x, axis, size, shift):
    return lax.ppermute(x, axis, [(i, (i + shift) % size) for i in range(size)])


def swapped(x, axis, size, bit):
    return lax.ppermute(x, axis, [(i, i ^ bit) for i in range(size)])


def broadcast_from(x, owner, me, axis, size):
    got = None
    for s in range(1, size):
        part = lax.ppermute(x, axis, [(owner, (owner + s) % size)])
        got = part if got is None else got + part
    return jnp.where(me == owner, x, got)


def tail_kernel(levels, peers, rows_ref, dests_ref, table_ref, start_ref, tiles_ref, *refs):
    x_refs = refs[:peers]
    term_refs = refs[peers : 2 * peers]
    slices_ref = refs[2 * peers]
    acc_ref = refs[2 * peers + 1]
    share = slices_ref.shape[1]
    start = pl.multiple_of(start_ref[0], 8)
    for t in range(levels):
        for p in range(peers):

            @pl.when(table_ref[t] == p)
            def _():
                bulk = x_refs[p].shape[0] - share
                high = x_refs[p][pl.ds(start, share), :].astype(jnp.float32)
                slices_ref[t] = high + x_refs[p][pl.ds(bulk, share), :].astype(jnp.float32)

    acc_ref[...] = jnp.zeros_like(acc_ref)
    for s in range(tiles_ref.shape[0]):
        level = rows_ref[s]
        piece = table_ref[jnp.maximum(level, 0)]
        for p in range(peers):

            @pl.when((level >= 0) & (piece == p))
            def _():
                prod = lax.dot_general(
                    tiles_ref[s],
                    x_refs[p][pl.ds(0, tiles_ref.shape[2]), :],
                    (((0,), (0,)), ((), ())),
                    preferred_element_type=jnp.float32,
                )
                acc_ref[dests_ref[s]] += prod

    for p in range(peers):
        term_refs[p][...] = acc_ref[p].astype(jnp.bfloat16)


def tail_terms(slot_rows, dests, table, start, tiles, pieces, levels, share):
    peers = len(pieces)
    shape = (tiles.shape[2], pieces[0].shape[1])
    outs = [jax.ShapeDtypeStruct(shape, jnp.bfloat16) for _ in range(peers)]
    outs.append(jax.ShapeDtypeStruct((levels, share, shape[1]), jnp.float32))
    result = pl.pallas_call(
        functools.partial(tail_kernel, levels, peers),
        out_shape=outs,
        in_specs=[SMEM] * 4 + [VMEM] * (1 + peers),
        out_specs=[VMEM] * (peers + 1),
        scratch_shapes=[pltpu.VMEM((peers,) + shape, jnp.float32)],
    )(slot_rows, dests, table, start, tiles, *pieces)
    return result[:peers], result[peers]


def last_kernel(forward_ref, inv_ref, *refs):
    term_refs = refs[:-1]
    out_ref = refs[-1]
    returned = term_refs[0][...].astype(jnp.float32)
    for ref in term_refs[1:]:
        returned = returned + ref[...].astype(jnp.float32)
    update = (forward_ref[...].astype(jnp.float32) - returned).astype(jnp.bfloat16)
    out_ref[0] = lax.dot_general(
        inv_ref[0], update, (((0,), (0,)), ((), ())), preferred_element_type=jnp.float32
    )


def last_solve(forward, inv, terms):
    return pl.pallas_call(
        last_kernel,
        out_shape=jax.ShapeDtypeStruct((1,) + forward.shape, jnp.float32),
        in_specs=[VMEM] * (2 + len(terms)),
        out_specs=VMEM,
    )(forward, inv, *terms)


def hop(x, source, target):
    sent = lax.ppermute(x.astype(jnp.bfloat16), "col", [(source, target)])
    return sent.astype(jnp.float32)


def pair_index(t, u):
    return t * (t - 1) // 2 + u


def tile_table(levels):
    table = np.zeros((levels, levels - 1), np.int32)
    for c in range(levels):
        for j in range(levels - 1):
            table[c, j] = pair_index(c, j) if j < c else pair_index(j + 1, c)
    return table


def summed_chunks(x, peers, rows_n, me):
    chunks = x.reshape(peers, -1, x.shape[-1]).astype(jnp.bfloat16)
    bit = 1
    while bit < peers:
        pairs = chunks.reshape(-1, 2, *chunks.shape[1:])
        mine = (me // bit) % 2
        keep = lax.dynamic_index_in_dim(pairs, mine, 1, keepdims=False)
        give = lax.dynamic_index_in_dim(pairs, 1 - mine, 1, keepdims=False)
        got = swapped(give, "col", peers, bit)
        chunks = (keep.astype(jnp.float32) + got.astype(jnp.float32)).astype(jnp.bfloat16)
        bit *= 2
    part = chunks[0]
    bit = 1
    while bit < rows_n:
        got = swapped(part, "row", rows_n, bit)
        part = (part.astype(jnp.float32) + got.astype(jnp.float32)).astype(jnp.bfloat16)
        bit *= 2
    return part


def gathered_chunks(part, peers, me):
    pieces = [part] + [shifted(part, "col", peers, s) for s in range(1, peers)]
    stacked = jnp.stack(pieces)
    source = (me - jnp.arange(peers)) % peers
    return jnp.zeros_like(stacked).at[source].set(stacked)


def local(low_rhs, low_inv, low_tiles, tile_rows, tile_cols, top_rhs, top_inv, top_tiles):
    peers = lax.axis_size("col")
    rows_n = lax.axis_size("row")
    levels = top_rhs.shape[0]
    share = top_rhs.shape[1]
    width = top_rhs.shape[2]
    position = lax.axis_index("row")
    me = lax.axis_index("col")
    owned = jnp.minimum(me, levels - 1)

    pieces = [lax.dynamic_slice_in_dim(top_inv, owned, 1, 0)]
    for j in range(levels - 1):
        index = jnp.where(j < owned, owned * (owned - 1) // 2 + j, (j + 1) * j // 2 + owned)
        pieces.append(lax.dynamic_slice_in_dim(top_tiles, index, 1, 0))
    mine = jnp.concatenate(pieces, axis=0)
    mats = lax.all_gather(mine, "row", axis=1, tiled=True)
    inv = mats[0]

    slot_rows = tile_rows[0]
    slot_cols = tile_cols[0] % peers
    own_tiles = low_tiles[0]
    low_forward = jnp.dot(low_inv[0], low_rhs[0], preferred_element_type=jnp.float32).astype(
        jnp.bfloat16
    )
    received = [low_forward] + [shifted(low_forward, "col", peers, s) for s in range(1, peers)]
    source_of = (me - jnp.arange(peers)) % peers
    by_source = jnp.stack(received)
    slot_pick = jnp.argmax(source_of[None, :] == slot_cols[:, None], axis=1).astype(jnp.int32)
    fold = jnp.stack([position * share, me]).astype(jnp.int32)
    coupling = coupling_terms(slot_rows, slot_pick, fold, own_tiles, by_source, top_rhs, levels)
    part = summed_chunks(coupling, peers, rows_n, me)
    if peers == levels:
        level_sum = part
    else:
        level_sum = gathered_chunks(part, peers, me).reshape(levels, -1, width)[owned]
    rhs_level = -level_sum.astype(jnp.float32)

    top_forward = [None] * levels
    pushed = None
    for level in range(levels):
        residue = rhs_level
        if level > 0:
            pushed = hop(pushed, level - 1, level)
            residue = residue - pushed[0]
        solved = jnp.dot(inv, residue.astype(jnp.bfloat16), preferred_element_type=jnp.float32)
        top_forward[level] = solved.astype(jnp.bfloat16)
        if level < levels - 1:
            later = jnp.einsum(
                "kab,bc->kac", mats[level + 1 : levels], top_forward[level], preferred_element_type=jnp.float32
            )
            pushed = later if level == 0 else pushed[1:] + later
    own_solution = None
    for level in reversed(range(levels)):
        update = top_forward[level].astype(jnp.float32)
        if level < levels - 1:
            pushed = hop(pushed, level + 1, level)
            update = update - pushed[level]
        solved = lax.dot_general(
            inv, update.astype(jnp.bfloat16), (((0,), (0,)), ((), ())), preferred_element_type=jnp.float32
        )
        own_solution = solved if own_solution is None else jnp.where(me == level, solved, own_solution)
        if level > 0:
            earlier = jnp.einsum(
                "uab,ac->ubc", mats[1 : level + 1], solved.astype(jnp.bfloat16), preferred_element_type=jnp.float32
            )
            pushed = earlier if level == levels - 1 else pushed[:level] + earlier
    high = own_solution.astype(jnp.bfloat16)
    rows_here = lax.dynamic_slice_in_dim(own_solution - high.astype(jnp.float32), position * share, share, 0)
    packed = jnp.concatenate([high, rows_here.astype(jnp.bfloat16)], axis=0)
    pieces = [packed] + [shifted(packed, "col", peers, s) for s in range(1, peers)]
    table = ((me - jnp.arange(levels)) % peers).astype(jnp.int32)
    dests = ((me - slot_cols) % peers).astype(jnp.int32)
    start = (position * share)[None].astype(jnp.int32)
    terms, top_rows = tail_terms(slot_rows, dests, table, start, own_tiles, pieces, levels, share)
    returned = [terms[0]] + [shifted(terms[s], "col", peers, peers - s) for s in range(1, peers)]
    low_solution = last_solve(low_forward, low_inv, returned)
    return (low_solution, top_rows)


def solution(mesh):
    in_specs = (
        P(("row", "col"), None, None),
        P(("row", "col"), None, None),
        P(("row", "col"), None, None, None),
        P(("row", "col"), None),
        P(("row", "col"), None),
        P(None, "row", None),
        P(None, "row", None),
        P(None, "row", None),
    )
    out_specs = (P(("row", "col"), None, None), P(None, "row", None))
    return jax.shard_map(local, mesh=mesh, in_specs=in_specs, out_specs=out_specs, check_vma=False)
```

```python
import functools

import jax
import jax.numpy as jnp
import numpy as np
from jax import lax
from jax.experimental import pallas as pl
from jax.experimental.pallas import tpu as pltpu
from jax.sharding import PartitionSpec as P

SMEM = pl.BlockSpec(memory_space=pltpu.SMEM)
VMEM = pl.BlockSpec(memory_space=pltpu.VMEM)


def coupling_kernel(rows_ref, picks_ref, fold_ref, tiles_ref, panels_ref, rhs_ref, out_ref, acc_ref):
    acc_ref[...] = jnp.zeros_like(acc_ref)
    share = rhs_ref.shape[1]

    @pl.when(fold_ref[1] == 0)
    def _():
        start = pl.multiple_of(fold_ref[0], 8)
        acc_ref[:, pl.ds(start, share), :] = -rhs_ref[...].astype(jnp.float32)

    for s in range(tiles_ref.shape[0]):
        level = rows_ref[s]

        @pl.when(level >= 0)
        def _():
            prod = jnp.dot(tiles_ref[s], panels_ref[picks_ref[s]], preferred_element_type=jnp.float32)
            acc_ref[level] += prod

    out_ref[...] = acc_ref[...].astype(out_ref.dtype)


def coupling_terms(slot_rows, picks, fold, tiles, panels, rhs, levels):
    shape = (levels, panels.shape[1], panels.shape[2])
    return pl.pallas_call(
        coupling_kernel,
        out_shape=jax.ShapeDtypeStruct(shape, jnp.bfloat16),
        in_specs=[SMEM, SMEM, SMEM, VMEM, VMEM, VMEM],
        out_specs=VMEM,
        scratch_shapes=[pltpu.VMEM(shape, jnp.float32)],
    )(slot_rows, picks, fold, tiles, panels, rhs)


def back_kernel(rows_ref, dests_ref, tiles_ref, back_ref, out_ref, acc_ref):
    acc_ref[...] = jnp.zeros_like(acc_ref)
    for s in range(tiles_ref.shape[0]):
        level = rows_ref[s]

        @pl.when(level >= 0)
        def _():
            prod = lax.dot_general(
                tiles_ref[s], back_ref[level], (((0,), (0,)), ((), ())), preferred_element_type=jnp.float32
            )
            acc_ref[dests_ref[s]] += prod

    out_ref[...] = acc_ref[...].astype(out_ref.dtype)


def back_terms(slot_rows, dests, tiles, back, peers):
    shape = (peers, tiles.shape[2], back.shape[2])
    return pl.pallas_call(
        back_kernel,
        out_shape=jax.ShapeDtypeStruct(shape, jnp.bfloat16),
        in_specs=[SMEM, SMEM, VMEM, VMEM],
        out_specs=VMEM,
        scratch_shapes=[pltpu.VMEM(shape, jnp.float32)],
    )(slot_rows, dests, tiles, back)


def shifted(x, axis, size, shift):
    return lax.ppermute(x, axis, [(i, (i + shift) % size) for i in range(size)])


def swapped(x, axis, size, bit):
    return lax.ppermute(x, axis, [(i, i ^ bit) for i in range(size)])


def broadcast_from(x, owner, me, axis, size):
    got = None
    for s in range(1, size):
        part = lax.ppermute(x, axis, [(owner, (owner + s) % size)])
        got = part if got is None else got + part
    return jnp.where(me == owner, x, got)


def tail_kernel(levels, peers, rows_ref, dests_ref, table_ref, start_ref, tiles_ref, *refs):
    x_refs = refs[:peers]
    term_refs = refs[peers : 2 * peers]
    slices_ref = refs[2 * peers]
    acc_ref = refs[2 * peers + 1]
    share = slices_ref.shape[1]
    start = pl.multiple_of(start_ref[0], 8)
    for t in range(levels):
        for p in range(peers):

            @pl.when(table_ref[t] == p)
            def _():
                bulk = x_refs[p].shape[0] - share
                high = x_refs[p][pl.ds(start, share), :].astype(jnp.float32)
                slices_ref[t] = high + x_refs[p][pl.ds(bulk, share), :].astype(jnp.float32)

    acc_ref[...] = jnp.zeros_like(acc_ref)
    for s in range(tiles_ref.shape[0]):
        level = rows_ref[s]
        piece = table_ref[jnp.maximum(level, 0)]
        for p in range(peers):

            @pl.when((level >= 0) & (piece == p))
            def _():
                prod = lax.dot_general(
                    tiles_ref[s],
                    x_refs[p][pl.ds(0, tiles_ref.shape[2]), :],
                    (((0,), (0,)), ((), ())),
                    preferred_element_type=jnp.float32,
                )
                acc_ref[dests_ref[s]] += prod

    for p in range(peers):
        term_refs[p][...] = acc_ref[p].astype(jnp.bfloat16)


def tail_terms(slot_rows, dests, table, start, tiles, pieces, levels, share):
    peers = len(pieces)
    shape = (tiles.shape[2], pieces[0].shape[1])
    outs = [jax.ShapeDtypeStruct(shape, jnp.bfloat16) for _ in range(peers)]
    outs.append(jax.ShapeDtypeStruct((levels, share, shape[1]), jnp.float32))
    result = pl.pallas_call(
        functools.partial(tail_kernel, levels, peers),
        out_shape=outs,
        in_specs=[SMEM] * 4 + [VMEM] * (1 + peers),
        out_specs=[VMEM] * (peers + 1),
        scratch_shapes=[pltpu.VMEM((peers,) + shape, jnp.float32)],
    )(slot_rows, dests, table, start, tiles, *pieces)
    return result[:peers], result[peers]


def last_kernel(forward_ref, inv_ref, *refs):
    term_refs = refs[:-1]
    out_ref = refs[-1]
    returned = term_refs[0][...].astype(jnp.float32)
    for ref in term_refs[1:]:
        returned = returned + ref[...].astype(jnp.float32)
    update = (forward_ref[...].astype(jnp.float32) - returned).astype(jnp.bfloat16)
    out_ref[0] = lax.dot_general(
        inv_ref[0], update, (((0,), (0,)), ((), ())), preferred_element_type=jnp.float32
    )


def last_solve(forward, inv, terms):
    return pl.pallas_call(
        last_kernel,
        out_shape=jax.ShapeDtypeStruct((1,) + forward.shape, jnp.float32),
        in_specs=[VMEM] * (2 + len(terms)),
        out_specs=VMEM,
    )(forward, inv, *terms)


def hop(x, source, target):
    sent = lax.ppermute(x.astype(jnp.bfloat16), "col", [(source, target)])
    return sent.astype(jnp.float32)


def pair_index(t, u):
    return t * (t - 1) // 2 + u


def tile_table(levels):
    table = np.zeros((levels, levels - 1), np.int32)
    for c in range(levels):
        for j in range(levels - 1):
            table[c, j] = pair_index(c, j) if j < c else pair_index(j + 1, c)
    return table


def summed_chunks(x, peers, rows_n, me):
    chunks = x.reshape(peers, -1, x.shape[-1]).astype(jnp.bfloat16)
    bit = 1
    while bit < peers:
        pairs = chunks.reshape(-1, 2, *chunks.shape[1:])
        mine = (me // bit) % 2
        keep = lax.dynamic_index_in_dim(pairs, mine, 1, keepdims=False)
        give = lax.dynamic_index_in_dim(pairs, 1 - mine, 1, keepdims=False)
        got = swapped(give, "col", peers, bit)
        chunks = (keep.astype(jnp.float32) + got.astype(jnp.float32)).astype(jnp.bfloat16)
        bit *= 2
    part = chunks[0]
    bit = 1
    last = rows_n // 2 if rows_n == 8 else rows_n
    while bit < last:
        got = swapped(part, "row", rows_n, bit)
        part = (part.astype(jnp.float32) + got.astype(jnp.float32)).astype(jnp.bfloat16)
        bit *= 2
    if rows_n == 8:
        row = lax.axis_index("row")
        got = lax.ppermute(part, "row", [(2, 4), (4, 2), (3, 5), (5, 3)])
        part = (part.astype(jnp.float32) + got.astype(jnp.float32)).astype(jnp.bfloat16)
        handed = lax.ppermute(part, "row", [(2, 0), (3, 1), (4, 6), (5, 7)])
        part = jnp.where((row >= 2) & (row <= 5), part, handed)
    return part


def gathered_chunks(part, peers, me):
    pieces = [part] + [shifted(part, "col", peers, s) for s in range(1, peers)]
    stacked = jnp.stack(pieces)
    source = (me - jnp.arange(peers)) % peers
    return jnp.zeros_like(stacked).at[source].set(stacked)


def local(low_rhs, low_inv, low_tiles, tile_rows, tile_cols, top_rhs, top_inv, top_tiles):
    peers = lax.axis_size("col")
    rows_n = lax.axis_size("row")
    levels = top_rhs.shape[0]
    share = top_rhs.shape[1]
    width = top_rhs.shape[2]
    position = lax.axis_index("row")
    me = lax.axis_index("col")
    owned = jnp.minimum(me, levels - 1)

    pieces = [lax.dynamic_slice_in_dim(top_inv, owned, 1, 0)]
    for j in range(levels - 1):
        index = jnp.where(j < owned, owned * (owned - 1) // 2 + j, (j + 1) * j // 2 + owned)
        pieces.append(lax.dynamic_slice_in_dim(top_tiles, index, 1, 0))
    mine = jnp.concatenate(pieces, axis=0)
    mats = lax.all_gather(mine, "row", axis=1, tiled=True)
    inv = mats[0]

    slot_rows = tile_rows[0]
    slot_cols = tile_cols[0] % peers
    own_tiles = low_tiles[0]
    low_forward = jnp.dot(low_inv[0], low_rhs[0], preferred_element_type=jnp.float32).astype(
        jnp.bfloat16
    )
    received = [low_forward] + [shifted(low_forward, "col", peers, s) for s in range(1, peers)]
    source_of = (me - jnp.arange(peers)) % peers
    by_source = jnp.stack(received)
    slot_pick = jnp.argmax(source_of[None, :] == slot_cols[:, None], axis=1).astype(jnp.int32)
    fold = jnp.stack([position * share, me]).astype(jnp.int32)
    coupling = coupling_terms(slot_rows, slot_pick, fold, own_tiles, by_source, top_rhs, levels)
    part = summed_chunks(coupling, peers, rows_n, me)
    if peers == levels:
        level_sum = part
    else:
        level_sum = gathered_chunks(part, peers, me).reshape(levels, -1, width)[owned]
    rhs_level = -level_sum.astype(jnp.float32)

    top_forward = [None] * levels
    pushed = None
    for level in range(levels):
        residue = rhs_level
        if level > 0:
            pushed = hop(pushed, level - 1, level)
            residue = residue - pushed[0]
        solved = jnp.dot(inv, residue.astype(jnp.bfloat16), preferred_element_type=jnp.float32)
        top_forward[level] = solved.astype(jnp.bfloat16)
        if level < levels - 1:
            later = jnp.einsum(
                "kab,bc->kac", mats[level + 1 : levels], top_forward[level], preferred_element_type=jnp.float32
            )
            pushed = later if level == 0 else pushed[1:] + later
    own_solution = None
    for level in reversed(range(levels)):
        update = top_forward[level].astype(jnp.float32)
        if level < levels - 1:
            pushed = hop(pushed, level + 1, level)
            update = update - pushed[level]
        solved = lax.dot_general(
            inv, update.astype(jnp.bfloat16), (((0,), (0,)), ((), ())), preferred_element_type=jnp.float32
        )
        own_solution = solved if own_solution is None else jnp.where(me == level, solved, own_solution)
        if level > 0:
            earlier = jnp.einsum(
                "uab,ac->ubc", mats[1 : level + 1], solved.astype(jnp.bfloat16), preferred_element_type=jnp.float32
            )
            pushed = earlier if level == levels - 1 else pushed[:level] + earlier
    high = own_solution.astype(jnp.bfloat16)
    rows_here = lax.dynamic_slice_in_dim(own_solution - high.astype(jnp.float32), position * share, share, 0)
    packed = jnp.concatenate([high, rows_here.astype(jnp.bfloat16)], axis=0)
    pieces = [packed] + [shifted(packed, "col", peers, s) for s in range(1, peers)]
    table = ((me - jnp.arange(levels)) % peers).astype(jnp.int32)
    dests = ((me - slot_cols) % peers).astype(jnp.int32)
    start = (position * share)[None].astype(jnp.int32)
    terms, top_rows = tail_terms(slot_rows, dests, table, start, own_tiles, pieces, levels, share)
    returned = [terms[0]] + [shifted(terms[s], "col", peers, peers - s) for s in range(1, peers)]
    low_solution = last_solve(low_forward, low_inv, returned)
    return (low_solution, top_rows)


def solution(mesh):
    in_specs = (
        P(("row", "col"), None, None),
        P(("row", "col"), None, None),
        P(("row", "col"), None, None, None),
        P(("row", "col"), None),
        P(("row", "col"), None),
        P(None, "row", None),
        P(None, "row", None),
        P(None, "row", None),
    )
    out_specs = (P(("row", "col"), None, None), P(None, "row", None))
    return jax.shard_map(local, mesh=mesh, in_specs=in_specs, out_specs=out_specs, check_vma=False)
```

```python
import functools

import jax
import jax.numpy as jnp
import numpy as np
from jax import lax
from jax.experimental import pallas as pl
from jax.experimental.pallas import tpu as pltpu
from jax.sharding import PartitionSpec as P

SMEM = pl.BlockSpec(memory_space=pltpu.SMEM)
VMEM = pl.BlockSpec(memory_space=pltpu.VMEM)


def coupling_kernel(rows_ref, picks_ref, fold_ref, tiles_ref, panels_ref, rhs_ref, out_ref, acc_ref):
    acc_ref[...] = jnp.zeros_like(acc_ref)
    share = rhs_ref.shape[1]

    @pl.when(fold_ref[1] == 0)
    def _():
        start = pl.multiple_of(fold_ref[0], 8)
        acc_ref[:, pl.ds(start, share), :] = -rhs_ref[...].astype(jnp.float32)

    for s in range(tiles_ref.shape[0]):
        level = rows_ref[s]

        @pl.when(level >= 0)
        def _():
            prod = jnp.dot(tiles_ref[s], panels_ref[picks_ref[s]], preferred_element_type=jnp.float32)
            acc_ref[level] += prod

    out_ref[...] = acc_ref[...].astype(out_ref.dtype)


def coupling_terms(slot_rows, picks, fold, tiles, panels, rhs, levels):
    shape = (levels, panels.shape[1], panels.shape[2])
    return pl.pallas_call(
        coupling_kernel,
        out_shape=jax.ShapeDtypeStruct(shape, jnp.bfloat16),
        in_specs=[SMEM, SMEM, SMEM, VMEM, VMEM, VMEM],
        out_specs=VMEM,
        scratch_shapes=[pltpu.VMEM(shape, jnp.float32)],
    )(slot_rows, picks, fold, tiles, panels, rhs)


def back_kernel(rows_ref, dests_ref, tiles_ref, back_ref, out_ref, acc_ref):
    acc_ref[...] = jnp.zeros_like(acc_ref)
    for s in range(tiles_ref.shape[0]):
        level = rows_ref[s]

        @pl.when(level >= 0)
        def _():
            prod = lax.dot_general(
                tiles_ref[s], back_ref[level], (((0,), (0,)), ((), ())), preferred_element_type=jnp.float32
            )
            acc_ref[dests_ref[s]] += prod

    out_ref[...] = acc_ref[...].astype(out_ref.dtype)


def back_terms(slot_rows, dests, tiles, back, peers):
    shape = (peers, tiles.shape[2], back.shape[2])
    return pl.pallas_call(
        back_kernel,
        out_shape=jax.ShapeDtypeStruct(shape, jnp.bfloat16),
        in_specs=[SMEM, SMEM, VMEM, VMEM],
        out_specs=VMEM,
        scratch_shapes=[pltpu.VMEM(shape, jnp.float32)],
    )(slot_rows, dests, tiles, back)


def shifted(x, axis, size, shift):
    return lax.ppermute(x, axis, [(i, (i + shift) % size) for i in range(size)])


def swapped(x, axis, size, bit):
    return lax.ppermute(x, axis, [(i, i ^ bit) for i in range(size)])


def broadcast_from(x, owner, me, axis, size):
    got = None
    for s in range(1, size):
        part = lax.ppermute(x, axis, [(owner, (owner + s) % size)])
        got = part if got is None else got + part
    return jnp.where(me == owner, x, got)


def tail_kernel(levels, peers, rows_ref, dests_ref, table_ref, start_ref, tiles_ref, *refs):
    x_refs = refs[:peers]
    term_refs = refs[peers : 2 * peers]
    slices_ref = refs[2 * peers]
    acc_ref = refs[2 * peers + 1]
    share = slices_ref.shape[1]
    start = pl.multiple_of(start_ref[0], 8)
    for t in range(levels):
        for p in range(peers):

            @pl.when(table_ref[t] == p)
            def _():
                bulk = x_refs[p].shape[0] - share
                high = x_refs[p][pl.ds(start, share), :].astype(jnp.float32)
                slices_ref[t] = high + x_refs[p][pl.ds(bulk, share), :].astype(jnp.float32)

    acc_ref[...] = jnp.zeros_like(acc_ref)
    for s in range(tiles_ref.shape[0]):
        level = rows_ref[s]
        piece = table_ref[jnp.maximum(level, 0)]
        for p in range(peers):

            @pl.when((level >= 0) & (piece == p))
            def _():
                prod = lax.dot_general(
                    tiles_ref[s],
                    x_refs[p][pl.ds(0, tiles_ref.shape[2]), :],
                    (((0,), (0,)), ((), ())),
                    preferred_element_type=jnp.float32,
                )
                acc_ref[dests_ref[s]] += prod

    for p in range(peers):
        term_refs[p][...] = acc_ref[p].astype(jnp.bfloat16)


def tail_terms(slot_rows, dests, table, start, tiles, pieces, levels, share):
    peers = len(pieces)
    shape = (tiles.shape[2], pieces[0].shape[1])
    outs = [jax.ShapeDtypeStruct(shape, jnp.bfloat16) for _ in range(peers)]
    outs.append(jax.ShapeDtypeStruct((levels, share, shape[1]), jnp.float32))
    result = pl.pallas_call(
        functools.partial(tail_kernel, levels, peers),
        out_shape=outs,
        in_specs=[SMEM] * 4 + [VMEM] * (1 + peers),
        out_specs=[VMEM] * (peers + 1),
        scratch_shapes=[pltpu.VMEM((peers,) + shape, jnp.float32)],
    )(slot_rows, dests, table, start, tiles, *pieces)
    return result[:peers], result[peers]


def last_kernel(forward_ref, inv_ref, *refs):
    term_refs = refs[:-1]
    out_ref = refs[-1]
    returned = term_refs[0][...].astype(jnp.float32)
    for ref in term_refs[1:]:
        returned = returned + ref[...].astype(jnp.float32)
    update = (forward_ref[...].astype(jnp.float32) - returned).astype(jnp.bfloat16)
    out_ref[0] = lax.dot_general(
        inv_ref[0], update, (((0,), (0,)), ((), ())), preferred_element_type=jnp.float32
    )


def last_solve(forward, inv, terms):
    return pl.pallas_call(
        last_kernel,
        out_shape=jax.ShapeDtypeStruct((1,) + forward.shape, jnp.float32),
        in_specs=[VMEM] * (2 + len(terms)),
        out_specs=VMEM,
    )(forward, inv, *terms)


def hop(x, source, target):
    sent = lax.ppermute(x.astype(jnp.bfloat16), "col", [(source, target)])
    return sent.astype(jnp.float32)


def pair_index(t, u):
    return t * (t - 1) // 2 + u


def tile_table(levels):
    table = np.zeros((levels, levels - 1), np.int32)
    for c in range(levels):
        for j in range(levels - 1):
            table[c, j] = pair_index(c, j) if j < c else pair_index(j + 1, c)
    return table


def summed_chunks(x, peers, rows_n, me):
    chunks = x.reshape(peers, -1, x.shape[-1]).astype(jnp.bfloat16)
    bit = 1
    while bit < peers:
        pairs = chunks.reshape(-1, 2, *chunks.shape[1:])
        mine = (me // bit) % 2
        keep = lax.dynamic_index_in_dim(pairs, mine, 1, keepdims=False)
        give = lax.dynamic_index_in_dim(pairs, 1 - mine, 1, keepdims=False)
        got = swapped(give, "col", peers, bit)
        chunks = (keep.astype(jnp.float32) + got.astype(jnp.float32)).astype(jnp.bfloat16)
        bit *= 2
    part = chunks[0]
    bit = 1
    while bit < rows_n:
        got = swapped(part, "row", rows_n, bit)
        part = (part.astype(jnp.float32) + got.astype(jnp.float32)).astype(jnp.bfloat16)
        bit *= 2
    return part


def gathered_chunks(part, peers, me):
    pieces = [part] + [shifted(part, "col", peers, s) for s in range(1, peers)]
    stacked = jnp.stack(pieces)
    source = (me - jnp.arange(peers)) % peers
    return jnp.zeros_like(stacked).at[source].set(stacked)


def local(low_rhs, low_inv, low_tiles, tile_rows, tile_cols, top_rhs, top_inv, top_tiles):
    peers = lax.axis_size("col")
    rows_n = lax.axis_size("row")
    levels = top_rhs.shape[0]
    share = top_rhs.shape[1]
    width = top_rhs.shape[2]
    position = lax.axis_index("row")
    me = lax.axis_index("col")
    owned = jnp.minimum(me, levels - 1)

    pieces = [lax.dynamic_slice_in_dim(top_inv, owned, 1, 0)]
    for j in range(levels - 1):
        index = jnp.where(j < owned, owned * (owned - 1) // 2 + j, (j + 1) * j // 2 + owned)
        pieces.append(lax.dynamic_slice_in_dim(top_tiles, index, 1, 0))
    inv = lax.all_gather(pieces[0], "row", axis=1, tiled=True)[0]
    tiles_held = lax.all_gather(jnp.concatenate(pieces[1:], axis=0), "row", axis=1, tiled=True)

    slot_rows = tile_rows[0]
    slot_cols = tile_cols[0] % peers
    own_tiles = low_tiles[0]
    low_forward = jnp.dot(low_inv[0], low_rhs[0], preferred_element_type=jnp.float32).astype(
        jnp.bfloat16
    )
    received = [low_forward] + [shifted(low_forward, "col", peers, s) for s in range(1, peers)]
    source_of = (me - jnp.arange(peers)) % peers
    by_source = jnp.stack(received)
    slot_pick = jnp.argmax(source_of[None, :] == slot_cols[:, None], axis=1).astype(jnp.int32)
    fold = jnp.stack([position * share, me]).astype(jnp.int32)
    coupling = coupling_terms(slot_rows, slot_pick, fold, own_tiles, by_source, top_rhs, levels)
    part = summed_chunks(coupling, peers, rows_n, me)
    if peers == levels:
        level_sum = part
    else:
        level_sum = gathered_chunks(part, peers, me).reshape(levels, -1, width)[owned]
    rhs_level = -level_sum.astype(jnp.float32)

    top_forward = [None] * levels
    pushed = None
    for level in range(levels):
        residue = rhs_level
        if level > 0:
            pushed = hop(pushed, level - 1, level)
            residue = residue - pushed[0]
        solved = jnp.dot(inv, residue.astype(jnp.bfloat16), preferred_element_type=jnp.float32)
        top_forward[level] = solved.astype(jnp.bfloat16)
        if level < levels - 1:
            later = jnp.einsum(
                "kab,bc->kac", tiles_held[level : levels - 1], top_forward[level], preferred_element_type=jnp.float32
            )
            pushed = later if level == 0 else pushed[1:] + later
    own_solution = None
    for level in reversed(range(levels)):
        update = top_forward[level].astype(jnp.float32)
        if level < levels - 1:
            pushed = hop(pushed, level + 1, level)
            update = update - pushed[level]
        solved = lax.dot_general(
            inv, update.astype(jnp.bfloat16), (((0,), (0,)), ((), ())), preferred_element_type=jnp.float32
        )
        own_solution = solved if own_solution is None else jnp.where(me == level, solved, own_solution)
        if level > 0:
            earlier = jnp.einsum(
                "uab,ac->ubc", tiles_held[0:level], solved.astype(jnp.bfloat16), preferred_element_type=jnp.float32
            )
            pushed = earlier if level == levels - 1 else pushed[:level] + earlier
    high = own_solution.astype(jnp.bfloat16)
    rows_here = lax.dynamic_slice_in_dim(own_solution - high.astype(jnp.float32), position * share, share, 0)
    packed = jnp.concatenate([high, rows_here.astype(jnp.bfloat16)], axis=0)
    pieces = [packed] + [shifted(packed, "col", peers, s) for s in range(1, peers)]
    table = ((me - jnp.arange(levels)) % peers).astype(jnp.int32)
    dests = ((me - slot_cols) % peers).astype(jnp.int32)
    start = (position * share)[None].astype(jnp.int32)
    terms, top_rows = tail_terms(slot_rows, dests, table, start, own_tiles, pieces, levels, share)
    returned = [terms[0]] + [shifted(terms[s], "col", peers, peers - s) for s in range(1, peers)]
    low_solution = last_solve(low_forward, low_inv, returned)
    return (low_solution, top_rows)


def solution(mesh):
    in_specs = (
        P(("row", "col"), None, None),
        P(("row", "col"), None, None),
        P(("row", "col"), None, None, None),
        P(("row", "col"), None),
        P(("row", "col"), None),
        P(None, "row", None),
        P(None, "row", None),
        P(None, "row", None),
    )
    out_specs = (P(("row", "col"), None, None), P(None, "row", None))
    return jax.shard_map(local, mesh=mesh, in_specs=in_specs, out_specs=out_specs, check_vma=False)
```
